128 devices in a mesh: space: 32 (over x_hi, z, y), chan: 4 (over x_lo, core).
Axes of the slice: x: 4 (x_hi: 2, x_lo: 2; x = x_hi * 2 + x_lo), y: 4, z: 4, core: 2. Of those that a mesh axis runs over, the one named last changes fastest.
Arguments:
- latents: bfloat16 [256, 2, 640, 128], P('space', None, 'chan'), as said below
- targets: bfloat16 [256, 2, 640, 128], P('space', None, 'chan'), may hold values from -6 to 6
- norm_gain: float32 [640], P('chan'), may hold values from 0.5 to 2
- norm_bias: float32 [640], P('chan'), may hold values from -2.5 to 2.5
- conv_weight: bfloat16 [3, 3, 640, 640], P(None, None, 'chan'), may hold values from -0.078125 to 0.078125
- tile_image: int32 [32, 8], replicated, may hold values from -1 to 63, as said below
- tile_owner: int32 [32, 8], replicated, may hold values from -1 to 31, as said below
- tile_slot: int32 [32, 8], replicated, may hold values from -1 to 3, as said below
- timesteps: int32 [64], replicated, may hold values from 0 to 999
Outputs:
- x_grad: bfloat16 [128, 2, 640, 128], P('space', None, 'chan')
- weight_grad: float32 [3, 3, 640, 640], P(None, None, 'chan')
The draws below stay inside these ranges and needn't reach their ends.
Inputs may be any that keep to these rules, and one draw needn't show every extreme that they name: `tile_image`: every index s of space holds the tiles of exactly two images, each in consecutive slots in row order from the image's first row; unused slots come last and hold -1. Every image has one tile or more, all indices together hold 128 tiles, and some index has all 8 slots used. `tile_owner`: for a used slot, the index along space that computes the tile; -1 for unused slots. Every index receives exactly 4 tiles, and no index sends more than 1 tile to one index, a bound that some pair reaches. `tile_slot`: for a used slot, the tile's position among the 4 tiles of its assigned index, each position taken once; -1 for unused slots. `latents`: latent features of the images.
All inputs are finite; a program needn't handle non-finite values.
Results may differ from the reference program's by a relative error of at most 0.018.
Values may be sent and summed in bfloat16 or wider, within the bound.
No kernel may reach another device: no remote copies, remote signals or barrier semaphores. Data moves between devices by JAX's collectives and lax.ppermute only.
A program may use at most 128 MiB of HBM per device.

```python
import math
import jax
import jax.numpy as jnp
from jax import lax

C = 640
GROUPS = 32
W = 128
TILE_ROWS = 2
TILES_DEV = 4
STORE_DEV = 8
IMAGES = 64
TILES = 128
SLOTS = 256
N_SPACE = 32


def tile_layout(key):
    base_key = jax.random.fold_in(key, 31)
    key_order, key_moved, key_split, key_dest, key_names = jax.random.split(base_key, 5)
    device_order = jax.random.permutation(key_order, N_SPACE)
    pair_count = (N_SPACE - 3) // 2
    load_shift = jnp.zeros((N_SPACE,), jnp.int32)
    load_shift = load_shift.at[0].set(TILES_DEV).at[1].set(-(TILES_DEV // 2)).at[2].set(-(TILES_DEV - TILES_DEV // 2))
    if pair_count > 0:
        moved_tiles = jax.random.randint(key_moved, (pair_count,), 0, TILES_DEV - 1).astype(jnp.int32)
        lead_index = 3 + 2 * jnp.arange(pair_count)
        load_shift = load_shift.at[lead_index].set(moved_tiles).at[lead_index + 1].set(-moved_tiles)
    load_tiles = jnp.zeros((N_SPACE,), jnp.int32).at[device_order].set(TILES_DEV + load_shift)
    first_len = jax.random.randint(key_split, (N_SPACE,), 1, load_tiles).astype(jnp.int32)
    slot_index = jnp.arange(STORE_DEV, dtype=jnp.int32)[None, :]
    occupied = slot_index < load_tiles[:, None]
    image_names = jax.random.permutation(key_names, IMAGES).astype(jnp.int32)
    local_image = 2 * jnp.arange(N_SPACE, dtype=jnp.int32)[:, None] + (slot_index >= first_len[:, None]).astype(jnp.int32)
    image_of = jnp.where(occupied, image_names[local_image], -1)
    start_tile = jnp.cumsum(load_tiles) - load_tiles
    global_tile = start_tile[:, None] + slot_index
    dest_order = jax.random.permutation(key_dest, N_SPACE).astype(jnp.int32)
    owner_of = jnp.where(occupied, dest_order[global_tile % N_SPACE], -1)
    slot_of = jnp.where(occupied, global_tile // N_SPACE, -1)
    return (image_of.astype(jnp.int32), owner_of.astype(jnp.int32), slot_of.astype(jnp.int32))


def draw_tile_image(key, part):
    return tile_layout(key)[0]


def draw_tile_owner(key, part):
    return tile_layout(key)[1]


def draw_tile_slot(key, part):
    return tile_layout(key)[2]


def draw_latents(key, part):
    sub_keys = jax.random.split(jax.random.fold_in(key, 5), 4)
    full_shape = (N_SPACE * STORE_DEV, TILE_ROWS, C, W)
    base_noise = jnp.clip(jax.random.normal(sub_keys[0], full_shape, jnp.float32), -5.0, 5.0)
    row_scale = jnp.exp(jax.random.uniform(sub_keys[1], (full_shape[0], TILE_ROWS, 1, 1), jnp.float32, 0.0, math.log(10.0)))
    chan_scale = jnp.exp(jax.random.uniform(sub_keys[2], (1, 1, C, 1), jnp.float32, 0.0, math.log(10.0)))
    offset = 0.5 * jnp.clip(jax.random.normal(sub_keys[3], (full_shape[0], 1, C, 1), jnp.float32), -4.0, 4.0)
    rise_factor = 1.0 + 2.0 * jnp.arange(full_shape[0], dtype=jnp.float32)[:, None, None, None] / (full_shape[0] - 1)
    return ((base_noise * row_scale + offset) * chan_scale * rise_factor).astype(jnp.bfloat16)


def plant(array, stream_key, least, top_value):
    extent = array.shape
    place = [jax.random.randint(jax.random.fold_in(stream_key, axis), (), 0, extent[axis]) for axis in range(len(extent))]
    array = array.at[tuple(place)].set(least)
    longest = extent.index(max(extent))
    place[longest] = (place[longest] + 1) % extent[longest]
    return array.at[tuple(place)].set(top_value)


def block_scale(key, extent, shards, least, high):
    level, own = 1.0, jax.random.fold_in(key, 6)
    for axis_at, parts in shards:
        heights = jnp.exp(jax.random.uniform(jax.random.fold_in(own, axis_at), (parts,), jnp.float32, least / len(shards), high / len(shards)))
        level = level * jnp.repeat(heights, extent[axis_at] // parts).reshape([-1 if axis == axis_at else 1 for axis in range(len(extent))])
    return level


def normal_values(own_key, dims, width, bound, pieces=(), kind=jnp.bfloat16):
    values = jax.random.normal(own_key, dims, jnp.float32) * width
    if len(pieces) > 0:
        values = block_scale(own_key, dims, pieces, -0.22, 0.18) * values
    return jnp.clip(values, min=-bound, max=bound).astype(kind)


def setup_inputs(seed: int = 0) -> dict:
    key_list = jax.random.split(jax.random.key(seed), 10)
    return {
        "latents": draw_latents(jax.random.fold_in(key_list[9], 71), 0),
        "targets": normal_values(key_list[1], (SLOTS, TILE_ROWS, C, W), 1.0, 6.0, ((0, 32), (2, 4))),
        "norm_gain": jnp.clip(0.5 + 1.5 * jax.random.uniform(key_list[2], (C,), jnp.float32) ** block_scale(key_list[2], (C,), ((0, 4),), -0.2, 0.2), 0.5, 2.0),
        "norm_bias": normal_values(key_list[3], (C,), 0.5, 2.5, ((0, 4),), jnp.float32),
        "conv_weight": normal_values(key_list[4], (3, 3, C, C), (9 * C) ** -0.5, 0.078125, ((2, 4),)),
        "tile_image": draw_tile_image(jax.random.fold_in(key_list[9], 71), 0),
        "tile_owner": draw_tile_owner(jax.random.fold_in(key_list[9], 71), 0),
        "tile_slot": draw_tile_slot(jax.random.fold_in(key_list[9], 71), 0),
        "timesteps": plant(jax.random.randint(key_list[8], (IMAGES,), 0, 1000), jax.random.fold_in(key_list[8], 1), 0, 999).astype(jnp.int32),
    }


EPS = 1e-05
HIGH = lax.Precision.HIGHEST

def loss_weights(timesteps):
    phase = (timesteps.astype(jnp.float32) / 1000.0 + 0.008) / 1.008 * (math.pi / 2.0)
    alpha_bar = jnp.cos(phase) ** 2
    return jnp.minimum(1.0, 5.0 * (1.0 - alpha_bar) / alpha_bar)

def silu_slope(pre_act):
    sigma_val = jax.nn.sigmoid(pre_act)
    return sigma_val * (1.0 + pre_act * (1.0 - sigma_val))

def group_sums(values, groups):
    grouped = values.reshape(values.shape[:-2] + (groups, values.shape[-2] // groups, values.shape[-1]))
    return lax.optimization_barrier(jnp.sum(grouped, axis=(-2, -1)))

def norm_stats(sum_first, sum_second, counts):
    mean_img = sum_first / counts[:, None]
    var_img = sum_second / counts[:, None] - mean_img * mean_img
    return (mean_img, lax.rsqrt(var_img + EPS))

def conv_views(row_views, weight):
    running = None
    for row_tap in range(3):
        source = row_views[row_tap]
        col_count = source.shape[-1]
        padded = jnp.pad(source, ((0, 0), (0, 0), (0, 0), (1, 1)))
        for col_tap in range(3):
            window = padded[:, :, :, col_tap:col_tap + col_count].astype(jnp.float32)
            tap_term = jnp.einsum('nrcw,oc->nrow', window, weight[row_tap, col_tap].astype(jnp.float32), precision=HIGH)
            running = tap_term if running is None else running + tap_term
    return running

def weight_terms(row_views, grad_field):
    grads_float = grad_field.astype(jnp.float32)
    tap_rows = []
    for row_tap in range(3):
        source = row_views[row_tap]
        col_count = source.shape[-1]
        padded = jnp.pad(source, ((0, 0), (0, 0), (0, 0), (1, 1)))
        tap_cols = []
        for col_tap in range(3):
            window = padded[:, :, :, col_tap:col_tap + col_count].astype(jnp.float32)
            tap_cols.append(jnp.einsum('nrow,nrcw->oc', grads_float, window, precision=HIGH))
        tap_rows.append(jnp.stack(tap_cols))
    return jnp.stack(tap_rows)

def shifted_views(source_field, up_ok, down_ok):
    zero_rows = jnp.zeros_like(source_field[:, :1])
    up_mask = up_ok.astype(source_field.dtype)[None, :, None, None]
    down_mask = down_ok.astype(source_field.dtype)[None, :, None, None]
    rows_above = jnp.concatenate([zero_rows, source_field[:, :-1]], axis=1) * up_mask
    rows_below = jnp.concatenate([source_field[:, 1:], zero_rows], axis=1) * down_mask
    return [rows_above, source_field, rows_below]

def device_pass(lat_dev, tar_dev, image_dev, norm_gain, norm_bias, conv_weight, flipped, counts, weights_img):
    row_total = STORE_DEV * TILE_ROWS
    group_size = C // GROUPS
    row_image = jnp.repeat(image_dev, TILE_ROWS)
    row_valid = row_image >= 0
    prev_image = jnp.concatenate([jnp.full((1,), -2, jnp.int32), row_image[:-1]])
    next_image = jnp.concatenate([row_image[1:], jnp.full((1,), -2, jnp.int32)])
    up_ok = row_valid & (prev_image == row_image)
    down_ok = row_valid & (next_image == row_image)
    image_ids = jnp.arange(IMAGES, dtype=jnp.int32)
    onehot = (row_image[:, None] == image_ids[None, :]).astype(jnp.float32)
    lat_float = lat_dev.reshape(1, row_total, C, W).astype(jnp.float32)
    part_first = jnp.dot(onehot.T, group_sums(lat_float, GROUPS)[0], precision=HIGH)
    part_second = jnp.dot(onehot.T, group_sums(lat_float * lat_float, GROUPS)[0], precision=HIGH)
    mean_img, rstd_img = norm_stats(part_first, part_second, counts)
    mean_rows = jnp.repeat(jnp.dot(onehot, mean_img, precision=HIGH), group_size, axis=1)[None, :, :, None]
    rstd_rows = jnp.repeat(jnp.dot(onehot, rstd_img, precision=HIGH), group_size, axis=1)[None, :, :, None]
    valid_rows = row_valid.astype(jnp.float32)[None, :, None, None]
    normed = (lat_float - mean_rows) * rstd_rows
    pre_act = normed * norm_gain[:, None] + norm_bias[:, None]
    act = (jax.nn.silu(pre_act) * valid_rows).astype(jnp.bfloat16)
    prediction = conv_views(shifted_views(act, up_ok, down_ok), conv_weight)
    loss_rows = jnp.dot(onehot, weights_img, precision=HIGH)[None, :, None, None]
    target_float = tar_dev.reshape(1, row_total, C, W).astype(jnp.float32)
    out_grad = (loss_rows * (prediction - target_float) * valid_rows).astype(jnp.bfloat16)
    act_grad = conv_views(shifted_views(out_grad, up_ok, down_ok), flipped)
    norm_grad = act_grad * silu_slope(pre_act) * norm_gain[:, None]
    grad_first = jnp.dot(onehot.T, group_sums(norm_grad, GROUPS)[0], precision=HIGH)
    grad_second = jnp.dot(onehot.T, group_sums(norm_grad * normed, GROUPS)[0], precision=HIGH)
    mean_g = jnp.repeat(jnp.dot(onehot, grad_first / counts[:, None], precision=HIGH), group_size, axis=1)[None, :, :, None]
    mean_gn = jnp.repeat(jnp.dot(onehot, grad_second / counts[:, None], precision=HIGH), group_size, axis=1)[None, :, :, None]
    x_grad = (rstd_rows * (norm_grad - mean_g - normed * mean_gn) * valid_rows).astype(jnp.bfloat16)
    weight_sum = weight_terms(shifted_views(act, up_ok, down_ok), out_grad)
    return (x_grad.reshape(STORE_DEV, TILE_ROWS, C, W), weight_sum)

def reference(latents, targets, norm_gain, norm_bias, conv_weight, tile_image, tile_owner, tile_slot, timesteps):
    group_size = C // GROUPS
    image_ids = jnp.arange(IMAGES, dtype=jnp.int32)
    counts = lax.optimization_barrier(jnp.sum((tile_image.reshape(-1)[None, :] == image_ids[:, None]).astype(jnp.float32), axis=1)) * float(TILE_ROWS * W * group_size)
    weights_img = loss_weights(timesteps)
    flipped = jnp.transpose(conv_weight[::-1, ::-1], (0, 1, 3, 2))
    lat_split = latents.reshape(N_SPACE, STORE_DEV, TILE_ROWS, C, W)
    tar_split = targets.reshape(N_SPACE, STORE_DEV, TILE_ROWS, C, W)

    def one_device(carry, device_inputs):
        grad_tiles, weight_sum = device_pass(device_inputs[0], device_inputs[1], device_inputs[2], norm_gain, norm_bias, conv_weight, flipped, counts, weights_img)
        return (carry + weight_sum, grad_tiles)
    weight_total, grad_tiles = lax.scan(one_device, jnp.zeros((3, 3, C, C), jnp.float32), (lat_split, tar_split, tile_image))
    dest_index = jnp.where(tile_owner >= 0, tile_owner * TILES_DEV + tile_slot, TILES).reshape(-1).astype(jnp.int32)
    x_grad = jnp.zeros((TILES, TILE_ROWS, C, W), jnp.bfloat16).at[dest_index].set(grad_tiles.reshape(SLOTS, TILE_ROWS, C, W), mode='drop')
    weight_grad = weight_total / math.sqrt(TILES * TILE_ROWS * W)
    return (x_grad, weight_grad)
```

```python
import math

import jax
import jax.numpy as jnp
from jax import lax
from jax.sharding import PartitionSpec as P

GROUPS = 32


EPS = 1e-05
HIGH = lax.Precision.HIGHEST


def loss_weights(timesteps):
    phase = (timesteps.astype(jnp.float32) / 1000.0 + 0.008) / 1.008 * (math.pi / 2.0)
    alpha_bar = jnp.cos(phase) ** 2
    return jnp.minimum(1.0, 5.0 * (1.0 - alpha_bar) / alpha_bar)


def silu_slope(pre_act):
    sigma_val = jax.nn.sigmoid(pre_act)
    return sigma_val * (1.0 + pre_act * (1.0 - sigma_val))


def group_sums(values, groups):
    grouped = values.reshape(
        values.shape[:-2] + (groups, values.shape[-2] // groups, values.shape[-1])
    )
    return jnp.sum(grouped, axis=(-2, -1))


def norm_stats(sum_first, sum_second, counts):
    mean_img = sum_first / counts[:, None]
    var_img = sum_second / counts[:, None] - mean_img * mean_img
    return (mean_img, lax.rsqrt(var_img + EPS))


def shifted_views(source_field, up_ok, down_ok):
    zero_rows = jnp.zeros_like(source_field[:1])
    up_mask = up_ok.astype(source_field.dtype)[:, None, None]
    down_mask = down_ok.astype(source_field.dtype)[:, None, None]
    rows_above = jnp.concatenate([zero_rows, source_field[:-1]], axis=0) * up_mask
    rows_below = jnp.concatenate([source_field[1:], zero_rows], axis=0) * down_mask
    return [rows_above, source_field, rows_below]


def conv_views(row_views, weight):
    running = None
    for row_tap in range(3):
        source = row_views[row_tap]
        col_count = source.shape[-1]
        padded = jnp.pad(source, ((0, 0), (0, 0), (1, 1)))
        for col_tap in range(3):
            window = padded[:, :, col_tap : col_tap + col_count]
            tap_term = jnp.einsum(
                "rcw,oc->row",
                window,
                weight[row_tap, col_tap],
                preferred_element_type=jnp.float32,
            )
            running = tap_term if running is None else running + tap_term
    return running


def weight_terms(row_views, grad_field):
    tap_rows = []
    for row_tap in range(3):
        source = row_views[row_tap]
        col_count = source.shape[-1]
        padded = jnp.pad(source, ((0, 0), (0, 0), (1, 1)))
        tap_cols = []
        for col_tap in range(3):
            window = padded[:, :, col_tap : col_tap + col_count]
            tap_cols.append(
                jnp.einsum("row,rcw->oc", grad_field, window, preferred_element_type=jnp.float32)
            )
        tap_rows.append(jnp.stack(tap_cols))
    return jnp.stack(tap_rows)


def local(
    latents,
    targets,
    norm_gain,
    norm_bias,
    conv_weight,
    tile_image,
    tile_owner,
    tile_slot,
    timesteps,
):
    my_index = lax.axis_index("space")
    devices = lax.axis_size("space")
    slots_dev, tile_rows, local_ch, col_count = latents.shape
    channels = conv_weight.shape[3]
    group_size = channels // GROUPS
    groups_here = local_ch // group_size
    image_total = timesteps.shape[0]
    tiles_dev = slots_dev // 2
    row_total = slots_dev * tile_rows
    image_ids = jnp.arange(image_total, dtype=jnp.int32)
    counts = jnp.sum(
        (tile_image.reshape(-1)[None, :] == image_ids[:, None]).astype(jnp.float32), axis=1
    ) * float(tile_rows * col_count * group_size)
    weights_img = loss_weights(timesteps)
    flipped = jnp.transpose(conv_weight[::-1, ::-1], (0, 1, 3, 2))
    gain_col = norm_gain[:, None]
    bias_col = norm_bias[:, None]
    grad_scale = 1.0 / math.sqrt(devices * tiles_dev * tile_rows * col_count)

    my_image = lax.dynamic_index_in_dim(tile_image, my_index, 0, keepdims=False)
    my_owner = lax.dynamic_index_in_dim(tile_owner, my_index, 0, keepdims=False)
    row_image = jnp.repeat(my_image, tile_rows)
    row_valid = row_image >= 0
    prev_image = jnp.concatenate([jnp.full((1,), -2, jnp.int32), row_image[:-1]])
    next_image = jnp.concatenate([row_image[1:], jnp.full((1,), -2, jnp.int32)])
    up_ok = row_valid & (prev_image == row_image)
    down_ok = row_valid & (next_image == row_image)
    onehot = (row_image[:, None] == image_ids[None, :]).astype(jnp.float32)
    valid_rows = row_valid.astype(jnp.float32)[:, None, None]

    lat_float = latents.reshape(row_total, local_ch, col_count).astype(jnp.float32)
    part_first = jnp.dot(onehot.T, group_sums(lat_float, groups_here), precision=HIGH)
    part_second = jnp.dot(onehot.T, group_sums(lat_float * lat_float, groups_here), precision=HIGH)
    mean_img, rstd_img = norm_stats(part_first, part_second, counts)
    mean_rows = jnp.repeat(jnp.dot(onehot, mean_img, precision=HIGH), group_size, axis=1)[
        :, :, None
    ]
    rstd_rows = jnp.repeat(jnp.dot(onehot, rstd_img, precision=HIGH), group_size, axis=1)[
        :, :, None
    ]
    normed = (lat_float - mean_rows) * rstd_rows
    pre_act = normed * gain_col + bias_col
    act = (jax.nn.silu(pre_act) * valid_rows).astype(jnp.bfloat16)
    act_full = lax.all_gather(act, "chan", axis=1, tiled=True)
    act_views = shifted_views(act_full, up_ok, down_ok)
    prediction = conv_views(act_views, conv_weight)
    loss_rows = jnp.dot(onehot, weights_img, precision=HIGH)[:, None, None]
    target_float = targets.reshape(row_total, local_ch, col_count).astype(jnp.float32)
    out_grad = (loss_rows * (prediction - target_float) * valid_rows).astype(jnp.bfloat16)
    act_partial = conv_views(shifted_views(out_grad, up_ok, down_ok), flipped)
    act_grad = lax.psum_scatter(
        act_partial.astype(jnp.bfloat16), "chan", scatter_dimension=1, tiled=True
    ).astype(jnp.float32)
    norm_grad = act_grad * silu_slope(pre_act) * gain_col
    grad_first = jnp.dot(onehot.T, group_sums(norm_grad, groups_here), precision=HIGH)
    grad_second = jnp.dot(onehot.T, group_sums(norm_grad * normed, groups_here), precision=HIGH)
    mean_g = jnp.repeat(
        jnp.dot(onehot, grad_first / counts[:, None], precision=HIGH), group_size, axis=1
    )[:, :, None]
    mean_gn = jnp.repeat(
        jnp.dot(onehot, grad_second / counts[:, None], precision=HIGH), group_size, axis=1
    )[:, :, None]
    x_rows = (rstd_rows * (norm_grad - mean_g - normed * mean_gn) * valid_rows).astype(
        jnp.bfloat16
    )

    dest_ids = jnp.arange(devices, dtype=jnp.int32)
    send_table = ((my_owner[None, :] == dest_ids[:, None]) & (my_owner[None, :] >= 0)).astype(
        jnp.bfloat16
    )
    outgoing = jnp.dot(
        send_table, x_rows.reshape(slots_dev, -1), preferred_element_type=jnp.float32
    ).astype(jnp.bfloat16)
    incoming = lax.all_to_all(
        outgoing.reshape(devices, 1, -1), "space", split_axis=0, concat_axis=0, tiled=True
    ).reshape(devices, -1)
    slot_ids = jnp.arange(tiles_dev, dtype=jnp.int32)
    hit_mask = (tile_owner[None] == my_index) & (tile_slot[None] == slot_ids[:, None, None])
    recv_table = jnp.any(hit_mask, axis=2).astype(jnp.bfloat16)
    x_grad = jnp.dot(recv_table, incoming, preferred_element_type=jnp.float32).astype(
        jnp.bfloat16
    )
    x_grad = x_grad.reshape(tiles_dev, tile_rows, local_ch, col_count)

    weight_sum = weight_terms(act_views, out_grad)
    weight_grad = lax.psum((weight_sum * grad_scale).astype(jnp.bfloat16), "space").astype(
        jnp.float32
    )
    return (x_grad, weight_grad)


def solution(mesh):
    in_specs = (
        P("space", None, "chan", None),
        P("space", None, "chan", None),
        P("chan"),
        P("chan"),
        P(None, None, "chan", None),
        P(),
        P(),
        P(),
        P(),
    )
    out_specs = (P("space", None, "chan", None), P(None, None, "chan", None))
    return jax.shard_map(local, mesh=mesh, in_specs=in_specs, out_specs=out_specs, check_vma=False)
```

```python
import math

import jax
import jax.numpy as jnp
from jax import lax
from jax.sharding import Mesh, NamedSharding
from jax.sharding import PartitionSpec as P

GROUPS = 32


EPS = 1e-05
HIGH = lax.Precision.HIGHEST


def loss_weights(timesteps):
    phase = (timesteps.astype(jnp.float32) / 1000.0 + 0.008) / 1.008 * (math.pi / 2.0)
    alpha_bar = jnp.cos(phase) ** 2
    return jnp.minimum(1.0, 5.0 * (1.0 - alpha_bar) / alpha_bar)


def silu_slope(pre_act):
    sigma_val = jax.nn.sigmoid(pre_act)
    return sigma_val * (1.0 + pre_act * (1.0 - sigma_val))


def group_sums(values, groups):
    grouped = values.reshape(
        values.shape[:-2] + (groups, values.shape[-2] // groups, values.shape[-1])
    )
    return jnp.sum(grouped, axis=(-2, -1))


def norm_stats(sum_first, sum_second, counts):
    mean_img = sum_first / counts[:, None]
    var_img = sum_second / counts[:, None] - mean_img * mean_img
    return (mean_img, lax.rsqrt(var_img + EPS))


def shifted_views(source_field, up_ok, down_ok):
    zero_rows = jnp.zeros_like(source_field[:1])
    up_mask = up_ok.astype(source_field.dtype)[:, None, None]
    down_mask = down_ok.astype(source_field.dtype)[:, None, None]
    rows_above = jnp.concatenate([zero_rows, source_field[:-1]], axis=0) * up_mask
    rows_below = jnp.concatenate([source_field[1:], zero_rows], axis=0) * down_mask
    return [rows_above, source_field, rows_below]


def conv_views(row_views, weight):
    running = None
    for row_tap in range(3):
        source = row_views[row_tap]
        col_count = source.shape[-1]
        padded = jnp.pad(source, ((0, 0), (0, 0), (1, 1)))
        for col_tap in range(3):
            window = padded[:, :, col_tap : col_tap + col_count]
            tap_term = jnp.einsum(
                "rcw,oc->row",
                window,
                weight[row_tap, col_tap],
                preferred_element_type=jnp.float32,
            )
            running = tap_term if running is None else running + tap_term
    return running


def weight_terms(row_views, grad_field):
    tap_rows = []
    for row_tap in range(3):
        source = row_views[row_tap]
        col_count = source.shape[-1]
        padded = jnp.pad(source, ((0, 0), (0, 0), (1, 1)))
        tap_cols = []
        for col_tap in range(3):
            window = padded[:, :, col_tap : col_tap + col_count]
            tap_cols.append(
                jnp.einsum("row,rcw->oc", grad_field, window, preferred_element_type=jnp.float32)
            )
        tap_rows.append(jnp.stack(tap_cols))
    return jnp.stack(tap_rows)


def local(
    latents,
    targets,
    norm_gain,
    norm_bias,
    conv_weight,
    tile_image,
    tile_owner,
    tile_slot,
    timesteps,
):
    my_index = lax.axis_index(("xh", "z", "y"))
    devices = lax.axis_size(("xh", "z", "y"))
    slots_dev, tile_rows, local_ch, col_count = latents.shape
    channels = conv_weight.shape[3]
    group_size = channels // GROUPS
    groups_here = local_ch // group_size
    image_total = timesteps.shape[0]
    tiles_dev = slots_dev // 2
    row_total = slots_dev * tile_rows
    image_ids = jnp.arange(image_total, dtype=jnp.int32)
    counts = jnp.sum(
        (tile_image.reshape(-1)[None, :] == image_ids[:, None]).astype(jnp.float32), axis=1
    ) * float(tile_rows * col_count * group_size)
    weights_img = loss_weights(timesteps)
    flipped = jnp.transpose(conv_weight[::-1, ::-1], (0, 1, 3, 2))
    gain_col = norm_gain[:, None]
    bias_col = norm_bias[:, None]
    grad_scale = 1.0 / math.sqrt(devices * tiles_dev * tile_rows * col_count)

    my_image = lax.dynamic_index_in_dim(tile_image, my_index, 0, keepdims=False)
    my_owner = lax.dynamic_index_in_dim(tile_owner, my_index, 0, keepdims=False)
    row_image = jnp.repeat(my_image, tile_rows)
    row_valid = row_image >= 0
    prev_image = jnp.concatenate([jnp.full((1,), -2, jnp.int32), row_image[:-1]])
    next_image = jnp.concatenate([row_image[1:], jnp.full((1,), -2, jnp.int32)])
    up_ok = row_valid & (prev_image == row_image)
    down_ok = row_valid & (next_image == row_image)
    onehot = (row_image[:, None] == image_ids[None, :]).astype(jnp.float32)
    valid_rows = row_valid.astype(jnp.float32)[:, None, None]

    lat_float = latents.reshape(row_total, local_ch, col_count).astype(jnp.float32)
    part_first = jnp.dot(onehot.T, group_sums(lat_float, groups_here), precision=HIGH)
    part_second = jnp.dot(onehot.T, group_sums(lat_float * lat_float, groups_here), precision=HIGH)
    mean_img, rstd_img = norm_stats(part_first, part_second, counts)
    mean_rows = jnp.repeat(jnp.dot(onehot, mean_img, precision=HIGH), group_size, axis=1)[
        :, :, None
    ]
    rstd_rows = jnp.repeat(jnp.dot(onehot, rstd_img, precision=HIGH), group_size, axis=1)[
        :, :, None
    ]
    normed = (lat_float - mean_rows) * rstd_rows
    pre_act = normed * gain_col + bias_col
    act = (jax.nn.silu(pre_act) * valid_rows).astype(jnp.bfloat16)
    act_full = lax.all_gather(act, ("xl", "core"), axis=1, tiled=True)
    act_views = shifted_views(act_full, up_ok, down_ok)
    prediction = conv_views(act_views, conv_weight)
    loss_rows = jnp.dot(onehot, weights_img, precision=HIGH)[:, None, None]
    target_float = targets.reshape(row_total, local_ch, col_count).astype(jnp.float32)
    out_grad = (loss_rows * (prediction - target_float) * valid_rows).astype(jnp.bfloat16)
    act_partial = conv_views(shifted_views(out_grad, up_ok, down_ok), flipped)
    act_grad = lax.psum_scatter(
        act_partial.astype(jnp.bfloat16), ("xl", "core"), scatter_dimension=1, tiled=True
    ).astype(jnp.float32)
    norm_grad = act_grad * silu_slope(pre_act) * gain_col
    grad_first = jnp.dot(onehot.T, group_sums(norm_grad, groups_here), precision=HIGH)
    grad_second = jnp.dot(onehot.T, group_sums(norm_grad * normed, groups_here), precision=HIGH)
    mean_g = jnp.repeat(
        jnp.dot(onehot, grad_first / counts[:, None], precision=HIGH), group_size, axis=1
    )[:, :, None]
    mean_gn = jnp.repeat(
        jnp.dot(onehot, grad_second / counts[:, None], precision=HIGH), group_size, axis=1
    )[:, :, None]
    x_rows = (rstd_rows * (norm_grad - mean_g - normed * mean_gn) * valid_rows).astype(
        jnp.bfloat16
    )

    dest_ids = jnp.arange(devices, dtype=jnp.int32)
    send_table = ((my_owner[None, :] == dest_ids[:, None]) & (my_owner[None, :] >= 0)).astype(
        jnp.bfloat16
    )
    outgoing = jnp.dot(
        send_table, x_rows.reshape(slots_dev, -1), preferred_element_type=jnp.float32
    ).astype(jnp.bfloat16)
    incoming = lax.all_to_all(
        outgoing.reshape(devices, 1, -1), ("xh", "z", "y"), split_axis=0, concat_axis=0, tiled=True
    ).reshape(devices, -1)
    slot_ids = jnp.arange(tiles_dev, dtype=jnp.int32)
    hit_mask = (tile_owner[None] == my_index) & (tile_slot[None] == slot_ids[:, None, None])
    recv_table = jnp.any(hit_mask, axis=2).astype(jnp.bfloat16)
    x_grad = jnp.dot(recv_table, incoming, preferred_element_type=jnp.float32).astype(
        jnp.bfloat16
    )
    x_grad = x_grad.reshape(tiles_dev, tile_rows, local_ch, col_count)

    weight_sum = weight_terms(act_views, out_grad)
    weight_grad = sum_space((weight_sum * grad_scale).astype(jnp.bfloat16)).astype(jnp.float32)
    return (x_grad, weight_grad)


WEIGHT_PLAN = "joint"


def sum_space(partial):
    shape = partial.shape
    flat = partial.reshape(-1, shape[-1])
    rows = flat.shape[0]
    padded_rows = -(-rows // 256) * 256
    flat = jnp.pad(flat, ((0, padded_rows - rows), (0, 0)))
    if WEIGHT_PLAN == "yz":
        part = lax.psum_scatter(flat, "y", scatter_dimension=0, tiled=True)
        part = lax.psum_scatter(part, "z", scatter_dimension=0, tiled=True)
        part = lax.psum(part, "xh")
        part = lax.all_gather(part, "z", axis=0, tiled=True)
        flat = lax.all_gather(part, "y", axis=0, tiled=True)
    else:
        part = lax.psum_scatter(flat, ("z", "y"), scatter_dimension=0, tiled=True)
        part = lax.psum(part, "xh")
        flat = lax.all_gather(part, ("z", "y"), axis=0, tiled=True)
    return flat[:rows].reshape(shape)


def solution(mesh):
    space_axes = ("xh", "z", "y")
    chan_axes = ("xl", "core")
    fine = Mesh(mesh.devices.reshape(2, 4, 4, 2, 2), space_axes + chan_axes)
    tiles = P(space_axes, None, chan_axes, None)
    in_specs = (
        tiles,
        tiles,
        P(chan_axes),
        P(chan_axes),
        P(None, None, chan_axes, None),
        P(),
        P(),
        P(),
        P(),
    )
    out_specs = (tiles, P(None, None, chan_axes, None))
    inner = jax.shard_map(
        fine_local, mesh=fine, in_specs=in_specs, out_specs=out_specs, check_vma=False
    )
    out_shardings = (
        NamedSharding(mesh, P("space", None, "chan", None)),
        NamedSharding(mesh, P(None, None, "chan", None)),
    )

    def run(*args):
        outs = inner(*args)
        return tuple(lax.with_sharding_constraint(o, sh) for o, sh in zip(outs, out_shardings))

    return run


def fine_local(*args):
    return local(*args)
```

```python
import math

import jax
import jax.numpy as jnp
from jax import lax
from jax.sharding import Mesh, NamedSharding
from jax.sharding import PartitionSpec as P

GROUPS = 32


EPS = 1e-05
HIGH = lax.Precision.HIGHEST


def loss_weights(timesteps):
    phase = (timesteps.astype(jnp.float32) / 1000.0 + 0.008) / 1.008 * (math.pi / 2.0)
    alpha_bar = jnp.cos(phase) ** 2
    return jnp.minimum(1.0, 5.0 * (1.0 - alpha_bar) / alpha_bar)


def silu_slope(pre_act):
    sigma_val = jax.nn.sigmoid(pre_act)
    return sigma_val * (1.0 + pre_act * (1.0 - sigma_val))


def group_sums(values, groups):
    grouped = values.reshape(
        values.shape[:-2] + (groups, values.shape[-2] // groups, values.shape[-1])
    )
    return jnp.sum(grouped, axis=(-2, -1))


def norm_stats(sum_first, sum_second, counts):
    mean_img = sum_first / counts[:, None]
    var_img = sum_second / counts[:, None] - mean_img * mean_img
    return (mean_img, lax.rsqrt(var_img + EPS))


def shifted_views(source_field, up_ok, down_ok):
    zero_rows = jnp.zeros_like(source_field[:1])
    up_mask = up_ok.astype(source_field.dtype)[:, None, None]
    down_mask = down_ok.astype(source_field.dtype)[:, None, None]
    rows_above = jnp.concatenate([zero_rows, source_field[:-1]], axis=0) * up_mask
    rows_below = jnp.concatenate([source_field[1:], zero_rows], axis=0) * down_mask
    return [rows_above, source_field, rows_below]


def conv_views(row_views, weight):
    running = None
    for row_tap in range(3):
        source = row_views[row_tap]
        col_count = source.shape[-1]
        padded = jnp.pad(source, ((0, 0), (0, 0), (1, 1)))
        for col_tap in range(3):
            window = padded[:, :, col_tap : col_tap + col_count]
            tap_term = jnp.einsum(
                "rcw,oc->row",
                window,
                weight[row_tap, col_tap],
                preferred_element_type=jnp.float32,
            )
            running = tap_term if running is None else running + tap_term
    return running


def weight_terms(row_views, grad_field):
    tap_rows = []
    for row_tap in range(3):
        source = row_views[row_tap]
        col_count = source.shape[-1]
        padded = jnp.pad(source, ((0, 0), (0, 0), (1, 1)))
        tap_cols = []
        for col_tap in range(3):
            window = padded[:, :, col_tap : col_tap + col_count]
            tap_cols.append(
                jnp.einsum("row,rcw->oc", grad_field, window, preferred_element_type=jnp.float32)
            )
        tap_rows.append(jnp.stack(tap_cols))
    return jnp.stack(tap_rows)


def local(
    latents,
    targets,
    norm_gain,
    norm_bias,
    conv_weight,
    tile_image,
    tile_owner,
    tile_slot,
    timesteps,
):
    my_index = lax.axis_index(("xh", "z", "y"))
    devices = lax.axis_size(("xh", "z", "y"))
    slots_dev, tile_rows, local_ch, col_count = latents.shape
    channels = conv_weight.shape[3]
    group_size = channels // GROUPS
    groups_here = local_ch // group_size
    image_total = timesteps.shape[0]
    tiles_dev = slots_dev // 2
    row_total = slots_dev * tile_rows
    image_ids = jnp.arange(image_total, dtype=jnp.int32)
    counts = jnp.sum(
        (tile_image.reshape(-1)[None, :] == image_ids[:, None]).astype(jnp.float32), axis=1
    ) * float(tile_rows * col_count * group_size)
    weights_img = loss_weights(timesteps)
    flipped = jnp.transpose(conv_weight[::-1, ::-1], (0, 1, 3, 2))
    gain_col = norm_gain[:, None]
    bias_col = norm_bias[:, None]
    grad_scale = 1.0 / math.sqrt(devices * tiles_dev * tile_rows * col_count)

    my_image = lax.dynamic_index_in_dim(tile_image, my_index, 0, keepdims=False)
    my_owner = lax.dynamic_index_in_dim(tile_owner, my_index, 0, keepdims=False)
    row_image = jnp.repeat(my_image, tile_rows)
    row_valid = row_image >= 0
    prev_image = jnp.concatenate([jnp.full((1,), -2, jnp.int32), row_image[:-1]])
    next_image = jnp.concatenate([row_image[1:], jnp.full((1,), -2, jnp.int32)])
    up_ok = row_valid & (prev_image == row_image)
    down_ok = row_valid & (next_image == row_image)
    onehot = (row_image[:, None] == image_ids[None, :]).astype(jnp.float32)
    valid_rows = row_valid.astype(jnp.float32)[:, None, None]

    lat_float = latents.reshape(row_total, local_ch, col_count).astype(jnp.float32)
    part_first = jnp.dot(onehot.T, group_sums(lat_float, groups_here), precision=HIGH)
    part_second = jnp.dot(onehot.T, group_sums(lat_float * lat_float, groups_here), precision=HIGH)
    mean_img, rstd_img = norm_stats(part_first, part_second, counts)
    mean_rows = jnp.repeat(jnp.dot(onehot, mean_img, precision=HIGH), group_size, axis=1)[
        :, :, None
    ]
    rstd_rows = jnp.repeat(jnp.dot(onehot, rstd_img, precision=HIGH), group_size, axis=1)[
        :, :, None
    ]
    normed = (lat_float - mean_rows) * rstd_rows
    pre_act = normed * gain_col + bias_col
    act = (jax.nn.silu(pre_act) * valid_rows).astype(jnp.bfloat16)
    act_full = lax.all_gather(act, ("xl", "core"), axis=1, tiled=True)
    act_views = shifted_views(act_full, up_ok, down_ok)
    prediction = conv_views(act_views, conv_weight)
    loss_rows = jnp.dot(onehot, weights_img, precision=HIGH)[:, None, None]
    target_float = targets.reshape(row_total, local_ch, col_count).astype(jnp.float32)
    out_grad = (loss_rows * (prediction - target_float) * valid_rows).astype(jnp.bfloat16)
    act_partial = conv_views(shifted_views(out_grad, up_ok, down_ok), flipped)
    act_grad = sum_chan(act_partial.astype(jnp.bfloat16))
    norm_grad = act_grad * silu_slope(pre_act) * gain_col
    grad_first = jnp.dot(onehot.T, group_sums(norm_grad, groups_here), precision=HIGH)
    grad_second = jnp.dot(onehot.T, group_sums(norm_grad * normed, groups_here), precision=HIGH)
    mean_g = jnp.repeat(
        jnp.dot(onehot, grad_first / counts[:, None], precision=HIGH), group_size, axis=1
    )[:, :, None]
    mean_gn = jnp.repeat(
        jnp.dot(onehot, grad_second / counts[:, None], precision=HIGH), group_size, axis=1
    )[:, :, None]
    x_rows = (rstd_rows * (norm_grad - mean_g - normed * mean_gn) * valid_rows).astype(
        jnp.bfloat16
    )

    dest_ids = jnp.arange(devices, dtype=jnp.int32)
    send_table = ((my_owner[None, :] == dest_ids[:, None]) & (my_owner[None, :] >= 0)).astype(
        jnp.bfloat16
    )
    outgoing = jnp.dot(
        send_table, x_rows.reshape(slots_dev, -1), preferred_element_type=jnp.float32
    ).astype(jnp.bfloat16)
    incoming = lax.all_to_all(
        outgoing.reshape(devices, 1, -1), ("xh", "z", "y"), split_axis=0, concat_axis=0, tiled=True
    ).reshape(devices, -1)
    slot_ids = jnp.arange(tiles_dev, dtype=jnp.int32)
    hit_mask = (tile_owner[None] == my_index) & (tile_slot[None] == slot_ids[:, None, None])
    recv_table = jnp.any(hit_mask, axis=2).astype(jnp.bfloat16)
    x_grad = jnp.dot(recv_table, incoming, preferred_element_type=jnp.float32).astype(
        jnp.bfloat16
    )
    x_grad = x_grad.reshape(tiles_dev, tile_rows, local_ch, col_count)

    weight_sum = weight_terms(act_views, out_grad)
    weight_grad = sum_space((weight_sum * grad_scale).astype(jnp.bfloat16)).astype(jnp.float32)
    return (x_grad, weight_grad)


WEIGHT_PLAN = "joint"


def sum_chan(partial):
    parts = lax.axis_size(("xl", "core"))
    rows, channels, cols = partial.shape
    split = partial.reshape(rows, parts, channels // parts, cols).transpose(1, 0, 2, 3)
    gathered = lax.all_to_all(split, ("xl", "core"), split_axis=0, concat_axis=0, tiled=True)
    return jnp.sum(gathered.astype(jnp.float32), axis=0)


def sum_space(partial):
    shape = partial.shape
    flat = partial.reshape(-1, shape[-1])
    rows = flat.shape[0]
    padded_rows = -(-rows // 256) * 256
    flat = jnp.pad(flat, ((0, padded_rows - rows), (0, 0)))
    if WEIGHT_PLAN == "yz":
        part = lax.psum_scatter(flat, "y", scatter_dimension=0, tiled=True)
        part = lax.psum_scatter(part, "z", scatter_dimension=0, tiled=True)
        part = lax.psum(part, "xh")
        part = lax.all_gather(part, "z", axis=0, tiled=True)
        flat = lax.all_gather(part, "y", axis=0, tiled=True)
    else:
        part = lax.psum_scatter(flat, ("z", "y"), scatter_dimension=0, tiled=True)
        part = lax.psum(part, "xh")
        flat = lax.all_gather(part, ("z", "y"), axis=0, tiled=True)
    return flat[:rows].reshape(shape)


def solution(mesh):
    space_axes = ("xh", "z", "y")
    chan_axes = ("xl", "core")
    fine = Mesh(mesh.devices.reshape(2, 4, 4, 2, 2), space_axes + chan_axes)
    tiles = P(space_axes, None, chan_axes, None)
    in_specs = (
        tiles,
        tiles,
        P(chan_axes),
        P(chan_axes),
        P(None, None, chan_axes, None),
        P(),
        P(),
        P(),
        P(),
    )
    out_specs = (tiles, P(None, None, chan_axes, None))
    inner = jax.shard_map(
        fine_local, mesh=fine, in_specs=in_specs, out_specs=out_specs, check_vma=False
    )
    out_shardings = (
        NamedSharding(mesh, P("space", None, "chan", None)),
        NamedSharding(mesh, P(None, None, "chan", None)),
    )

    def run(*args):
        outs = inner(*args)
        return tuple(lax.with_sharding_constraint(o, sh) for o, sh in zip(outs, out_shardings))

    return run


def fine_local(*args):
    return local(*args)
```

```python
import math

import jax
import jax.numpy as jnp
from jax import lax
from jax.sharding import Mesh, NamedSharding
from jax.sharding import PartitionSpec as P

GROUPS = 32


EPS = 1e-05
HIGH = lax.Precision.HIGHEST


def loss_weights(timesteps):
    phase = (timesteps.astype(jnp.float32) / 1000.0 + 0.008) / 1.008 * (math.pi / 2.0)
    alpha_bar = jnp.cos(phase) ** 2
    return jnp.minimum(1.0, 5.0 * (1.0 - alpha_bar) / alpha_bar)


def silu_slope(pre_act):
    sigma_val = jax.nn.sigmoid(pre_act)
    return sigma_val * (1.0 + pre_act * (1.0 - sigma_val))


def group_sums(values, groups):
    grouped = values.reshape(
        values.shape[:-2] + (groups, values.shape[-2] // groups, values.shape[-1])
    )
    return jnp.sum(grouped, axis=(-2, -1))


def norm_stats(sum_first, sum_second, counts):
    mean_img = sum_first / counts[:, None]
    var_img = sum_second / counts[:, None] - mean_img * mean_img
    return (mean_img, lax.rsqrt(var_img + EPS))


def shifted_views(source_field, up_ok, down_ok):
    zero_rows = jnp.zeros_like(source_field[:1])
    up_mask = up_ok.astype(source_field.dtype)[:, None, None]
    down_mask = down_ok.astype(source_field.dtype)[:, None, None]
    rows_above = jnp.concatenate([zero_rows, source_field[:-1]], axis=0) * up_mask
    rows_below = jnp.concatenate([source_field[1:], zero_rows], axis=0) * down_mask
    return [rows_above, source_field, rows_below]


def conv_views(row_views, weight):
    running = None
    for row_tap in range(3):
        source = row_views[row_tap]
        col_count = source.shape[-1]
        padded = jnp.pad(source, ((0, 0), (0, 0), (1, 1)))
        for col_tap in range(3):
            window = padded[:, :, col_tap : col_tap + col_count]
            tap_term = jnp.einsum(
                "rcw,oc->row",
                window,
                weight[row_tap, col_tap],
                preferred_element_type=jnp.float32,
            )
            running = tap_term if running is None else running + tap_term
    return running


def weight_terms(row_views, grad_field):
    tap_rows = []
    for row_tap in range(3):
        source = row_views[row_tap]
        col_count = source.shape[-1]
        padded = jnp.pad(source, ((0, 0), (0, 0), (1, 1)))
        tap_cols = []
        for col_tap in range(3):
            window = padded[:, :, col_tap : col_tap + col_count]
            tap_cols.append(
                jnp.einsum("row,rcw->oc", grad_field, window, preferred_element_type=jnp.float32)
            )
        tap_rows.append(jnp.stack(tap_cols))
    return jnp.stack(tap_rows)


def local(
    latents,
    targets,
    norm_gain,
    norm_bias,
    conv_weight,
    tile_image,
    tile_owner,
    tile_slot,
    timesteps,
):
    my_index = lax.axis_index(("xh", "z", "y"))
    devices = lax.axis_size(("xh", "z", "y"))
    slots_dev, tile_rows, local_ch, col_count = latents.shape
    channels = conv_weight.shape[3]
    group_size = channels // GROUPS
    groups_here = local_ch // group_size
    image_total = timesteps.shape[0]
    tiles_dev = slots_dev // 2
    row_total = slots_dev * tile_rows
    image_ids = jnp.arange(image_total, dtype=jnp.int32)
    counts = jnp.sum(
        (tile_image.reshape(-1)[None, :] == image_ids[:, None]).astype(jnp.float32), axis=1
    ) * float(tile_rows * col_count * group_size)
    weights_img = loss_weights(timesteps)
    flipped = jnp.transpose(conv_weight[::-1, ::-1], (0, 1, 3, 2))
    gain_col = norm_gain[:, None]
    bias_col = norm_bias[:, None]
    grad_scale = 1.0 / math.sqrt(devices * tiles_dev * tile_rows * col_count)

    my_image = lax.dynamic_index_in_dim(tile_image, my_index, 0, keepdims=False)
    my_owner = lax.dynamic_index_in_dim(tile_owner, my_index, 0, keepdims=False)
    row_image = jnp.repeat(my_image, tile_rows)
    row_valid = row_image >= 0
    prev_image = jnp.concatenate([jnp.full((1,), -2, jnp.int32), row_image[:-1]])
    next_image = jnp.concatenate([row_image[1:], jnp.full((1,), -2, jnp.int32)])
    up_ok = row_valid & (prev_image == row_image)
    down_ok = row_valid & (next_image == row_image)
    onehot = (row_image[:, None] == image_ids[None, :]).astype(jnp.float32)
    valid_rows = row_valid.astype(jnp.float32)[:, None, None]

    lat_float = latents.reshape(row_total, local_ch, col_count).astype(jnp.float32)
    part_first = jnp.dot(onehot.T, group_sums(lat_float, groups_here), precision=HIGH)
    part_second = jnp.dot(onehot.T, group_sums(lat_float * lat_float, groups_here), precision=HIGH)
    mean_img, rstd_img = norm_stats(part_first, part_second, counts)
    mean_rows = jnp.repeat(jnp.dot(onehot, mean_img, precision=HIGH), group_size, axis=1)[
        :, :, None
    ]
    rstd_rows = jnp.repeat(jnp.dot(onehot, rstd_img, precision=HIGH), group_size, axis=1)[
        :, :, None
    ]
    normed = (lat_float - mean_rows) * rstd_rows
    pre_act = normed * gain_col + bias_col
    act = (jax.nn.silu(pre_act) * valid_rows).astype(jnp.bfloat16)
    act_full = lax.all_gather(act, ("xl", "core"), axis=1, tiled=True)
    act_views = shifted_views(act_full, up_ok, down_ok)
    prediction = conv_views(act_views, conv_weight)
    loss_rows = jnp.dot(onehot, weights_img, precision=HIGH)[:, None, None]
    target_float = targets.reshape(row_total, local_ch, col_count).astype(jnp.float32)
    out_grad = (loss_rows * (prediction - target_float) * valid_rows).astype(jnp.bfloat16)
    act_partial = conv_views(shifted_views(out_grad, up_ok, down_ok), flipped)
    act_grad = sum_chan(act_partial.astype(jnp.bfloat16))
    norm_grad = act_grad * silu_slope(pre_act) * gain_col
    grad_first = jnp.dot(onehot.T, group_sums(norm_grad, groups_here), precision=HIGH)
    grad_second = jnp.dot(onehot.T, group_sums(norm_grad * normed, groups_here), precision=HIGH)
    mean_g = jnp.repeat(
        jnp.dot(onehot, grad_first / counts[:, None], precision=HIGH), group_size, axis=1
    )[:, :, None]
    mean_gn = jnp.repeat(
        jnp.dot(onehot, grad_second / counts[:, None], precision=HIGH), group_size, axis=1
    )[:, :, None]
    x_rows = (rstd_rows * (norm_grad - mean_g - normed * mean_gn) * valid_rows).astype(
        jnp.bfloat16
    )

    dest_ids = jnp.arange(devices, dtype=jnp.int32)
    send_table = ((my_owner[None, :] == dest_ids[:, None]) & (my_owner[None, :] >= 0)).astype(
        jnp.bfloat16
    )
    outgoing = jnp.dot(
        send_table, x_rows.reshape(slots_dev, -1), preferred_element_type=jnp.float32
    ).astype(jnp.bfloat16)
    incoming = lax.all_to_all(
        outgoing.reshape(devices, 1, -1), ("xh", "z", "y"), split_axis=0, concat_axis=0, tiled=True
    ).reshape(devices, -1)
    slot_ids = jnp.arange(tiles_dev, dtype=jnp.int32)
    hit_mask = (tile_owner[None] == my_index) & (tile_slot[None] == slot_ids[:, None, None])
    recv_table = jnp.any(hit_mask, axis=2).astype(jnp.bfloat16)
    x_grad = jnp.dot(recv_table, incoming, preferred_element_type=jnp.float32).astype(
        jnp.bfloat16
    )
    x_grad = x_grad.reshape(tiles_dev, tile_rows, local_ch, col_count)

    weight_sum = weight_terms(act_views, out_grad)
    weight_grad = sum_space((weight_sum * grad_scale).astype(jnp.bfloat16)).astype(jnp.float32)
    return (x_grad, weight_grad)


WEIGHT_PLAN = "all"


def sum_chan(partial):
    parts = lax.axis_size(("xl", "core"))
    rows, channels, cols = partial.shape
    split = partial.reshape(rows, parts, channels // parts, cols).transpose(1, 0, 2, 3)
    gathered = lax.all_to_all(split, ("xl", "core"), split_axis=0, concat_axis=0, tiled=True)
    return jnp.sum(gathered.astype(jnp.float32), axis=0)


def sum_space(partial):
    shape = partial.shape
    flat = partial.reshape(-1, shape[-1])
    rows = flat.shape[0]
    padded_rows = -(-rows // 512) * 512
    flat = jnp.pad(flat, ((0, padded_rows - rows), (0, 0)))
    if WEIGHT_PLAN == "yz":
        part = lax.psum_scatter(flat, "y", scatter_dimension=0, tiled=True)
        part = lax.psum_scatter(part, "z", scatter_dimension=0, tiled=True)
        part = lax.psum(part, "xh")
        part = lax.all_gather(part, "z", axis=0, tiled=True)
        flat = lax.all_gather(part, "y", axis=0, tiled=True)
    elif WEIGHT_PLAN == "all":
        part = lax.psum_scatter(flat, ("xh", "z", "y"), scatter_dimension=0, tiled=True)
        flat = lax.all_gather(part, ("xh", "z", "y"), axis=0, tiled=True)
    else:
        part = lax.psum_scatter(flat, ("z", "y"), scatter_dimension=0, tiled=True)
        part = lax.psum(part, "xh")
        flat = lax.all_gather(part, ("z", "y"), axis=0, tiled=True)
    return flat[:rows].reshape(shape)


def solution(mesh):
    space_axes = ("xh", "z", "y")
    chan_axes = ("xl", "core")
    fine = Mesh(mesh.devices.reshape(2, 4, 4, 2, 2), space_axes + chan_axes)
    tiles = P(space_axes, None, chan_axes, None)
    in_specs = (
        tiles,
        tiles,
        P(chan_axes),
        P(chan_axes),
        P(None, None, chan_axes, None),
        P(),
        P(),
        P(),
        P(),
    )
    out_specs = (tiles, P(None, None, chan_axes, None))
    inner = jax.shard_map(
        fine_local, mesh=fine, in_specs=in_specs, out_specs=out_specs, check_vma=False
    )
    out_shardings = (
        NamedSharding(mesh, P("space", None, "chan", None)),
        NamedSharding(mesh, P(None, None, "chan", None)),
    )

    def run(*args):
        outs = inner(*args)
        return tuple(lax.with_sharding_constraint(o, sh) for o, sh in zip(outs, out_shardings))

    return run


def fine_local(*args):
    return local(*args)
```

```python
import math

import jax
import jax.numpy as jnp
from jax import lax
from jax.sharding import Mesh, NamedSharding
from jax.sharding import PartitionSpec as P

GROUPS = 32


EPS = 1e-05
HIGH = lax.Precision.HIGHEST


def loss_weights(timesteps):
    phase = (timesteps.astype(jnp.float32) / 1000.0 + 0.008) / 1.008 * (math.pi / 2.0)
    alpha_bar = jnp.cos(phase) ** 2
    return jnp.minimum(1.0, 5.0 * (1.0 - alpha_bar) / alpha_bar)


def silu_slope(pre_act):
    sigma_val = jax.nn.sigmoid(pre_act)
    return sigma_val * (1.0 + pre_act * (1.0 - sigma_val))


def group_sums(values, groups):
    grouped = values.reshape(
        values.shape[:-2] + (groups, values.shape[-2] // groups, values.shape[-1])
    )
    return jnp.sum(grouped, axis=(-2, -1))


def norm_stats(sum_first, sum_second, counts):
    mean_img = sum_first / counts[:, None]
    var_img = sum_second / counts[:, None] - mean_img * mean_img
    return (mean_img, lax.rsqrt(var_img + EPS))


def shifted_views(source_field, up_ok, down_ok):
    zero_rows = jnp.zeros_like(source_field[:1])
    up_mask = up_ok.astype(source_field.dtype)[:, None, None]
    down_mask = down_ok.astype(source_field.dtype)[:, None, None]
    rows_above = jnp.concatenate([zero_rows, source_field[:-1]], axis=0) * up_mask
    rows_below = jnp.concatenate([source_field[1:], zero_rows], axis=0) * down_mask
    return [rows_above, source_field, rows_below]


def conv_views(row_views, weight):
    running = None
    for row_tap in range(3):
        source = row_views[row_tap]
        col_count = source.shape[-1]
        padded = jnp.pad(source, ((0, 0), (0, 0), (1, 1)))
        for col_tap in range(3):
            window = padded[:, :, col_tap : col_tap + col_count]
            tap_term = jnp.einsum(
                "rcw,oc->row",
                window,
                weight[row_tap, col_tap],
                preferred_element_type=jnp.float32,
            )
            running = tap_term if running is None else running + tap_term
    return running


def weight_terms(row_views, grad_field):
    tap_rows = []
    for row_tap in range(3):
        source = row_views[row_tap]
        col_count = source.shape[-1]
        padded = jnp.pad(source, ((0, 0), (0, 0), (1, 1)))
        tap_cols = []
        for col_tap in range(3):
            window = padded[:, :, col_tap : col_tap + col_count]
            tap_cols.append(
                jnp.einsum("row,rcw->oc", grad_field, window, preferred_element_type=jnp.float32)
            )
        tap_rows.append(jnp.stack(tap_cols))
    return jnp.stack(tap_rows)


def local(
    latents,
    targets,
    norm_gain,
    norm_bias,
    conv_weight,
    tile_image,
    tile_owner,
    tile_slot,
    timesteps,
):
    my_index = lax.axis_index(("xh", "z", "y"))
    devices = lax.axis_size(("xh", "z", "y"))
    slots_dev, tile_rows, local_ch, col_count = latents.shape
    channels = conv_weight.shape[3]
    group_size = channels // GROUPS
    groups_here = local_ch // group_size
    image_total = timesteps.shape[0]
    tiles_dev = slots_dev // 2
    row_total = slots_dev * tile_rows
    image_ids = jnp.arange(image_total, dtype=jnp.int32)
    counts = jnp.sum(
        (tile_image.reshape(-1)[None, :] == image_ids[:, None]).astype(jnp.float32), axis=1
    ) * float(tile_rows * col_count * group_size)
    weights_img = loss_weights(timesteps)
    flipped = jnp.transpose(conv_weight[::-1, ::-1], (0, 1, 3, 2))
    gain_col = norm_gain[:, None]
    bias_col = norm_bias[:, None]
    grad_scale = 1.0 / math.sqrt(devices * tiles_dev * tile_rows * col_count)

    my_image = lax.dynamic_index_in_dim(tile_image, my_index, 0, keepdims=False)
    my_owner = lax.dynamic_index_in_dim(tile_owner, my_index, 0, keepdims=False)
    row_image = jnp.repeat(my_image, tile_rows)
    row_valid = row_image >= 0
    prev_image = jnp.concatenate([jnp.full((1,), -2, jnp.int32), row_image[:-1]])
    next_image = jnp.concatenate([row_image[1:], jnp.full((1,), -2, jnp.int32)])
    up_ok = row_valid & (prev_image == row_image)
    down_ok = row_valid & (next_image == row_image)
    onehot = (row_image[:, None] == image_ids[None, :]).astype(jnp.float32)
    valid_rows = row_valid.astype(jnp.float32)[:, None, None]

    lat_float = latents.reshape(row_total, local_ch, col_count).astype(jnp.float32)
    part_first = jnp.dot(onehot.T, group_sums(lat_float, groups_here), precision=HIGH)
    part_second = jnp.dot(onehot.T, group_sums(lat_float * lat_float, groups_here), precision=HIGH)
    mean_img, rstd_img = norm_stats(part_first, part_second, counts)
    mean_rows = jnp.repeat(jnp.dot(onehot, mean_img, precision=HIGH), group_size, axis=1)[
        :, :, None
    ]
    rstd_rows = jnp.repeat(jnp.dot(onehot, rstd_img, precision=HIGH), group_size, axis=1)[
        :, :, None
    ]
    normed = (lat_float - mean_rows) * rstd_rows
    pre_act = normed * gain_col + bias_col
    act = (jax.nn.silu(pre_act) * valid_rows).astype(jnp.bfloat16)
    act_full = lax.all_gather(act, ("xl", "core"), axis=1, tiled=True)
    act_views = shifted_views(act_full, up_ok, down_ok)
    prediction = conv_views(act_views, conv_weight)
    loss_rows = jnp.dot(onehot, weights_img, precision=HIGH)[:, None, None]
    target_float = targets.reshape(row_total, local_ch, col_count).astype(jnp.float32)
    out_grad = (loss_rows * (prediction - target_float) * valid_rows).astype(jnp.bfloat16)
    act_partial = conv_views(shifted_views(out_grad, up_ok, down_ok), flipped)
    act_grad = sum_chan(act_partial.astype(jnp.bfloat16))
    norm_grad = act_grad * silu_slope(pre_act) * gain_col
    grad_first = jnp.dot(onehot.T, group_sums(norm_grad, groups_here), precision=HIGH)
    grad_second = jnp.dot(onehot.T, group_sums(norm_grad * normed, groups_here), precision=HIGH)
    mean_g = jnp.repeat(
        jnp.dot(onehot, grad_first / counts[:, None], precision=HIGH), group_size, axis=1
    )[:, :, None]
    mean_gn = jnp.repeat(
        jnp.dot(onehot, grad_second / counts[:, None], precision=HIGH), group_size, axis=1
    )[:, :, None]
    x_rows = (rstd_rows * (norm_grad - mean_g - normed * mean_gn) * valid_rows).astype(
        jnp.bfloat16
    )

    dest_ids = jnp.arange(devices, dtype=jnp.int32)
    send_table = ((my_owner[None, :] == dest_ids[:, None]) & (my_owner[None, :] >= 0)).astype(
        jnp.bfloat16
    )
    outgoing = jnp.dot(
        send_table, x_rows.reshape(slots_dev, -1), preferred_element_type=jnp.float32
    ).astype(jnp.bfloat16)
    incoming = lax.all_to_all(
        outgoing.reshape(devices, 1, -1), ("xh", "z", "y"), split_axis=0, concat_axis=0, tiled=True
    ).reshape(devices, -1)
    slot_ids = jnp.arange(tiles_dev, dtype=jnp.int32)
    hit_mask = (tile_owner[None] == my_index) & (tile_slot[None] == slot_ids[:, None, None])
    recv_table = jnp.any(hit_mask, axis=2).astype(jnp.bfloat16)
    x_grad = jnp.dot(recv_table, incoming, preferred_element_type=jnp.float32).astype(
        jnp.bfloat16
    )
    x_grad = x_grad.reshape(tiles_dev, tile_rows, local_ch, col_count)

    weight_sum = weight_terms(act_views, out_grad)
    weight_grad = sum_space((weight_sum * grad_scale).astype(jnp.bfloat16)).astype(jnp.float32)
    return (x_grad, weight_grad)


WEIGHT_PLAN = "joint"


def add_partner(part, axis):
    swapped = lax.ppermute(part, axis, perm=[(0, 1), (1, 0)])
    return (part.astype(jnp.float32) + swapped.astype(jnp.float32)).astype(part.dtype)


def sum_chan(partial):
    parts = lax.axis_size(("xl", "core"))
    rows, channels, cols = partial.shape
    split = partial.reshape(rows, parts, channels // parts, cols).transpose(1, 0, 2, 3)
    gathered = lax.all_to_all(split, ("xl", "core"), split_axis=0, concat_axis=0, tiled=True)
    return jnp.sum(gathered.astype(jnp.float32), axis=0)


def sum_space(partial):
    shape = partial.shape
    flat = partial.reshape(-1, shape[-1])
    rows = flat.shape[0]
    padded_rows = -(-rows // 256) * 256
    flat = jnp.pad(flat, ((0, padded_rows - rows), (0, 0)))
    if WEIGHT_PLAN == "yz":
        part = lax.psum_scatter(flat, "y", scatter_dimension=0, tiled=True)
        part = lax.psum_scatter(part, "z", scatter_dimension=0, tiled=True)
        part = lax.psum(part, "xh")
        part = lax.all_gather(part, "z", axis=0, tiled=True)
        flat = lax.all_gather(part, "y", axis=0, tiled=True)
    else:
        part = lax.psum_scatter(flat, ("z", "y"), scatter_dimension=0, tiled=True)
        part = add_partner(part, "xh")
        flat = lax.all_gather(part, ("z", "y"), axis=0, tiled=True)
    return flat[:rows].reshape(shape)


def solution(mesh):
    space_axes = ("xh", "z", "y")
    chan_axes = ("xl", "core")
    fine = Mesh(mesh.devices.reshape(2, 4, 4, 2, 2), space_axes + chan_axes)
    tiles = P(space_axes, None, chan_axes, None)
    in_specs = (
        tiles,
        tiles,
        P(chan_axes),
        P(chan_axes),
        P(None, None, chan_axes, None),
        P(),
        P(),
        P(),
        P(),
    )
    out_specs = (tiles, P(None, None, chan_axes, None))
    inner = jax.shard_map(
        fine_local, mesh=fine, in_specs=in_specs, out_specs=out_specs, check_vma=False
    )
    out_shardings = (
        NamedSharding(mesh, P("space", None, "chan", None)),
        NamedSharding(mesh, P(None, None, "chan", None)),
    )

    def run(*args):
        outs = inner(*args)
        return tuple(lax.with_sharding_constraint(o, sh) for o, sh in zip(outs, out_shardings))

    return run


def fine_local(*args):
    return local(*args)
```

```python
import math

import jax
import jax.numpy as jnp
from jax import lax
from jax.sharding import Mesh, NamedSharding
from jax.sharding import PartitionSpec as P

GROUPS = 32


EPS = 1e-05
HIGH = lax.Precision.HIGHEST


def loss_weights(timesteps):
    phase = (timesteps.astype(jnp.float32) / 1000.0 + 0.008) / 1.008 * (math.pi / 2.0)
    alpha_bar = jnp.cos(phase) ** 2
    return jnp.minimum(1.0, 5.0 * (1.0 - alpha_bar) / alpha_bar)


def silu_slope(pre_act):
    sigma_val = jax.nn.sigmoid(pre_act)
    return sigma_val * (1.0 + pre_act * (1.0 - sigma_val))


def group_sums(values, groups):
    grouped = values.reshape(
        values.shape[:-2] + (groups, values.shape[-2] // groups, values.shape[-1])
    )
    return jnp.sum(grouped, axis=(-2, -1))


def norm_stats(sum_first, sum_second, counts):
    mean_img = sum_first / counts[:, None]
    var_img = sum_second / counts[:, None] - mean_img * mean_img
    return (mean_img, lax.rsqrt(var_img + EPS))


def shifted_views(source_field, up_ok, down_ok):
    zero_rows = jnp.zeros_like(source_field[:1])
    up_mask = up_ok.astype(source_field.dtype)[:, None, None]
    down_mask = down_ok.astype(source_field.dtype)[:, None, None]
    rows_above = jnp.concatenate([zero_rows, source_field[:-1]], axis=0) * up_mask
    rows_below = jnp.concatenate([source_field[1:], zero_rows], axis=0) * down_mask
    return [rows_above, source_field, rows_below]


def conv_views(row_views, weight):
    running = None
    for row_tap in range(3):
        source = row_views[row_tap]
        col_count = source.shape[-1]
        padded = jnp.pad(source, ((0, 0), (0, 0), (1, 1)))
        for col_tap in range(3):
            window = padded[:, :, col_tap : col_tap + col_count]
            tap_term = jnp.einsum(
                "rcw,oc->row",
                window,
                weight[row_tap, col_tap],
                preferred_element_type=jnp.float32,
            )
            running = tap_term if running is None else running + tap_term
    return running


def weight_terms(row_views, grad_field):
    tap_rows = []
    for row_tap in range(3):
        source = row_views[row_tap]
        col_count = source.shape[-1]
        padded = jnp.pad(source, ((0, 0), (0, 0), (1, 1)))
        tap_cols = []
        for col_tap in range(3):
            window = padded[:, :, col_tap : col_tap + col_count]
            tap_cols.append(
                jnp.einsum("row,rcw->oc", grad_field, window, preferred_element_type=jnp.float32)
            )
        tap_rows.append(jnp.stack(tap_cols))
    return jnp.stack(tap_rows)


def local(
    latents,
    targets,
    norm_gain,
    norm_bias,
    conv_weight,
    tile_image,
    tile_owner,
    tile_slot,
    timesteps,
):
    my_index = lax.axis_index(("xh", "z", "y"))
    devices = lax.axis_size(("xh", "z", "y"))
    slots_dev, tile_rows, local_ch, col_count = latents.shape
    channels = conv_weight.shape[3]
    group_size = channels // GROUPS
    groups_here = local_ch // group_size
    image_total = timesteps.shape[0]
    tiles_dev = slots_dev // 2
    row_total = slots_dev * tile_rows
    image_ids = jnp.arange(image_total, dtype=jnp.int32)
    counts = jnp.sum(
        (tile_image.reshape(-1)[None, :] == image_ids[:, None]).astype(jnp.float32), axis=1
    ) * float(tile_rows * col_count * group_size)
    weights_img = loss_weights(timesteps)
    flipped = jnp.transpose(conv_weight[::-1, ::-1], (0, 1, 3, 2))
    gain_col = norm_gain[:, None]
    bias_col = norm_bias[:, None]
    grad_scale = 1.0 / math.sqrt(devices * tiles_dev * tile_rows * col_count)

    my_image = lax.dynamic_index_in_dim(tile_image, my_index, 0, keepdims=False)
    my_owner = lax.dynamic_index_in_dim(tile_owner, my_index, 0, keepdims=False)
    row_image = jnp.repeat(my_image, tile_rows)
    row_valid = row_image >= 0
    prev_image = jnp.concatenate([jnp.full((1,), -2, jnp.int32), row_image[:-1]])
    next_image = jnp.concatenate([row_image[1:], jnp.full((1,), -2, jnp.int32)])
    up_ok = row_valid & (prev_image == row_image)
    down_ok = row_valid & (next_image == row_image)
    onehot = (row_image[:, None] == image_ids[None, :]).astype(jnp.float32)
    valid_rows = row_valid.astype(jnp.float32)[:, None, None]

    lat_float = latents.reshape(row_total, local_ch, col_count).astype(jnp.float32)
    part_first = jnp.dot(onehot.T, group_sums(lat_float, groups_here), precision=HIGH)
    part_second = jnp.dot(onehot.T, group_sums(lat_float * lat_float, groups_here), precision=HIGH)
    mean_img, rstd_img = norm_stats(part_first, part_second, counts)
    mean_rows = jnp.repeat(jnp.dot(onehot, mean_img, precision=HIGH), group_size, axis=1)[
        :, :, None
    ]
    rstd_rows = jnp.repeat(jnp.dot(onehot, rstd_img, precision=HIGH), group_size, axis=1)[
        :, :, None
    ]
    normed = (lat_float - mean_rows) * rstd_rows
    pre_act = normed * gain_col + bias_col
    act = (jax.nn.silu(pre_act) * valid_rows).astype(jnp.bfloat16)
    act_full = lax.all_gather(act, ("xl", "core"), axis=1, tiled=True)
    act_views = shifted_views(act_full, up_ok, down_ok)
    prediction = conv_views(act_views, conv_weight)
    loss_rows = jnp.dot(onehot, weights_img, precision=HIGH)[:, None, None]
    target_float = targets.reshape(row_total, local_ch, col_count).astype(jnp.float32)
    out_grad = (loss_rows * (prediction - target_float) * valid_rows).astype(jnp.bfloat16)
    act_partial = conv_views(shifted_views(out_grad, up_ok, down_ok), flipped)
    act_grad = sum_chan(act_partial.astype(jnp.bfloat16))
    norm_grad = act_grad * silu_slope(pre_act) * gain_col
    grad_first = jnp.dot(onehot.T, group_sums(norm_grad, groups_here), precision=HIGH)
    grad_second = jnp.dot(onehot.T, group_sums(norm_grad * normed, groups_here), precision=HIGH)
    mean_g = jnp.repeat(
        jnp.dot(onehot, grad_first / counts[:, None], precision=HIGH), group_size, axis=1
    )[:, :, None]
    mean_gn = jnp.repeat(
        jnp.dot(onehot, grad_second / counts[:, None], precision=HIGH), group_size, axis=1
    )[:, :, None]
    x_rows = (rstd_rows * (norm_grad - mean_g - normed * mean_gn) * valid_rows).astype(
        jnp.bfloat16
    )

    dest_ids = jnp.arange(devices, dtype=jnp.int32)
    send_table = ((my_owner[None, :] == dest_ids[:, None]) & (my_owner[None, :] >= 0)).astype(
        jnp.bfloat16
    )
    outgoing = jnp.dot(
        send_table, x_rows.reshape(slots_dev, -1), preferred_element_type=jnp.float32
    ).astype(jnp.bfloat16)
    incoming = lax.all_to_all(
        outgoing.reshape(devices, 1, -1), ("xh", "z", "y"), split_axis=0, concat_axis=0, tiled=True
    ).reshape(devices, -1)
    slot_ids = jnp.arange(tiles_dev, dtype=jnp.int32)
    hit_mask = (tile_owner[None] == my_index) & (tile_slot[None] == slot_ids[:, None, None])
    recv_table = jnp.any(hit_mask, axis=2).astype(jnp.bfloat16)
    x_grad = jnp.dot(recv_table, incoming, preferred_element_type=jnp.float32).astype(
        jnp.bfloat16
    )
    x_grad = x_grad.reshape(tiles_dev, tile_rows, local_ch, col_count)

    weight_sum = weight_terms(act_views, out_grad)
    weight_grad = sum_space((weight_sum * grad_scale).astype(jnp.bfloat16)).astype(jnp.float32)
    return (x_grad, weight_grad)


WEIGHT_PLAN = "joint"


def scatter_sum(flat, axes):
    parts = lax.axis_size(axes)
    split = flat.reshape((parts, flat.shape[0] // parts) + flat.shape[1:])
    gathered = lax.all_to_all(split, axes, split_axis=0, concat_axis=0, tiled=True)
    return jnp.sum(gathered.astype(jnp.float32), axis=0).astype(flat.dtype)


def add_partner(part, axis):
    swapped = lax.ppermute(part, axis, perm=[(0, 1), (1, 0)])
    return (part.astype(jnp.float32) + swapped.astype(jnp.float32)).astype(part.dtype)


def sum_chan(partial):
    parts = lax.axis_size(("xl", "core"))
    rows, channels, cols = partial.shape
    split = partial.reshape(rows, parts, channels // parts, cols).transpose(1, 0, 2, 3)
    gathered = lax.all_to_all(split, ("xl", "core"), split_axis=0, concat_axis=0, tiled=True)
    return jnp.sum(gathered.astype(jnp.float32), axis=0)


def sum_space(partial):
    shape = partial.shape
    flat = partial.reshape(-1, shape[-1])
    rows = flat.shape[0]
    padded_rows = -(-rows // 256) * 256
    flat = jnp.pad(flat, ((0, padded_rows - rows), (0, 0)))
    if WEIGHT_PLAN == "yz":
        part = lax.psum_scatter(flat, "y", scatter_dimension=0, tiled=True)
        part = lax.psum_scatter(part, "z", scatter_dimension=0, tiled=True)
        part = lax.psum(part, "xh")
        part = lax.all_gather(part, "z", axis=0, tiled=True)
        flat = lax.all_gather(part, "y", axis=0, tiled=True)
    else:
        part = scatter_sum(flat, ("z", "y"))
        part = add_partner(part, "xh")
        flat = lax.all_gather(part, ("z", "y"), axis=0, tiled=True)
    return flat[:rows].reshape(shape)


def solution(mesh):
    space_axes = ("xh", "z", "y")
    chan_axes = ("xl", "core")
    fine = Mesh(mesh.devices.reshape(2, 4, 4, 2, 2), space_axes + chan_axes)
    tiles = P(space_axes, None, chan_axes, None)
    in_specs = (
        tiles,
        tiles,
        P(chan_axes),
        P(chan_axes),
        P(None, None, chan_axes, None),
        P(),
        P(),
        P(),
        P(),
    )
    out_specs = (tiles, P(None, None, chan_axes, None))
    inner = jax.shard_map(
        fine_local, mesh=fine, in_specs=in_specs, out_specs=out_specs, check_vma=False
    )
    out_shardings = (
        NamedSharding(mesh, P("space", None, "chan", None)),
        NamedSharding(mesh, P(None, None, "chan", None)),
    )

    def run(*args):
        outs = inner(*args)
        return tuple(lax.with_sharding_constraint(o, sh) for o, sh in zip(outs, out_shardings))

    return run


def fine_local(*args):
    return local(*args)
```

```python
import math

import jax
import jax.numpy as jnp
from jax import lax
from jax.sharding import Mesh, NamedSharding
from jax.sharding import PartitionSpec as P

GROUPS = 32


EPS = 1e-05
HIGH = lax.Precision.HIGHEST


def loss_weights(timesteps):
    phase = (timesteps.astype(jnp.float32) / 1000.0 + 0.008) / 1.008 * (math.pi / 2.0)
    alpha_bar = jnp.cos(phase) ** 2
    return jnp.minimum(1.0, 5.0 * (1.0 - alpha_bar) / alpha_bar)


def silu_slope(pre_act):
    sigma_val = jax.nn.sigmoid(pre_act)
    return sigma_val * (1.0 + pre_act * (1.0 - sigma_val))


def group_sums(values, groups):
    grouped = values.reshape(
        values.shape[:-2] + (groups, values.shape[-2] // groups, values.shape[-1])
    )
    return jnp.sum(grouped, axis=(-2, -1))


def norm_stats(sum_first, sum_second, counts):
    mean_img = sum_first / counts[:, None]
    var_img = sum_second / counts[:, None] - mean_img * mean_img
    return (mean_img, lax.rsqrt(var_img + EPS))


def shifted_views(source_field, up_ok, down_ok):
    zero_rows = jnp.zeros_like(source_field[:1])
    up_mask = up_ok.astype(source_field.dtype)[:, None, None]
    down_mask = down_ok.astype(source_field.dtype)[:, None, None]
    rows_above = jnp.concatenate([zero_rows, source_field[:-1]], axis=0) * up_mask
    rows_below = jnp.concatenate([source_field[1:], zero_rows], axis=0) * down_mask
    return [rows_above, source_field, rows_below]


def conv_views(row_views, weight):
    running = None
    for row_tap in range(3):
        source = row_views[row_tap]
        col_count = source.shape[-1]
        padded = jnp.pad(source, ((0, 0), (0, 0), (1, 1)))
        for col_tap in range(3):
            window = padded[:, :, col_tap : col_tap + col_count]
            tap_term = jnp.einsum(
                "rcw,oc->row",
                window,
                weight[row_tap, col_tap],
                preferred_element_type=jnp.float32,
            )
            running = tap_term if running is None else running + tap_term
    return running


def weight_terms(row_views, grad_field):
    tap_rows = []
    for row_tap in range(3):
        source = row_views[row_tap]
        col_count = source.shape[-1]
        padded = jnp.pad(source, ((0, 0), (0, 0), (1, 1)))
        tap_cols = []
        for col_tap in range(3):
            window = padded[:, :, col_tap : col_tap + col_count]
            tap_cols.append(
                jnp.einsum("row,rcw->oc", grad_field, window, preferred_element_type=jnp.float32)
            )
        tap_rows.append(jnp.stack(tap_cols))
    return jnp.stack(tap_rows)


def local(
    latents,
    targets,
    norm_gain,
    norm_bias,
    conv_weight,
    tile_image,
    tile_owner,
    tile_slot,
    timesteps,
):
    my_index = lax.axis_index(("xh", "z", "y"))
    devices = lax.axis_size(("xh", "z", "y"))
    slots_dev, tile_rows, local_ch, col_count = latents.shape
    channels = conv_weight.shape[3]
    group_size = channels // GROUPS
    groups_here = local_ch // group_size
    image_total = timesteps.shape[0]
    tiles_dev = slots_dev // 2
    row_total = slots_dev * tile_rows
    image_ids = jnp.arange(image_total, dtype=jnp.int32)
    counts = jnp.sum(
        (tile_image.reshape(-1)[None, :] == image_ids[:, None]).astype(jnp.float32), axis=1
    ) * float(tile_rows * col_count * group_size)
    weights_img = loss_weights(timesteps)
    flipped = jnp.transpose(conv_weight[::-1, ::-1], (0, 1, 3, 2))
    gain_col = norm_gain[:, None]
    bias_col = norm_bias[:, None]
    grad_scale = 1.0 / math.sqrt(devices * tiles_dev * tile_rows * col_count)

    my_image = lax.dynamic_index_in_dim(tile_image, my_index, 0, keepdims=False)
    my_owner = lax.dynamic_index_in_dim(tile_owner, my_index, 0, keepdims=False)
    row_image = jnp.repeat(my_image, tile_rows)
    row_valid = row_image >= 0
    prev_image = jnp.concatenate([jnp.full((1,), -2, jnp.int32), row_image[:-1]])
    next_image = jnp.concatenate([row_image[1:], jnp.full((1,), -2, jnp.int32)])
    up_ok = row_valid & (prev_image == row_image)
    down_ok = row_valid & (next_image == row_image)
    onehot = (row_image[:, None] == image_ids[None, :]).astype(jnp.float32)
    valid_rows = row_valid.astype(jnp.float32)[:, None, None]

    lat_float = latents.reshape(row_total, local_ch, col_count).astype(jnp.float32)
    part_first = jnp.dot(onehot.T, group_sums(lat_float, groups_here), precision=HIGH)
    part_second = jnp.dot(onehot.T, group_sums(lat_float * lat_float, groups_here), precision=HIGH)
    mean_img, rstd_img = norm_stats(part_first, part_second, counts)
    mean_rows = jnp.repeat(jnp.dot(onehot, mean_img, precision=HIGH), group_size, axis=1)[
        :, :, None
    ]
    rstd_rows = jnp.repeat(jnp.dot(onehot, rstd_img, precision=HIGH), group_size, axis=1)[
        :, :, None
    ]
    normed = (lat_float - mean_rows) * rstd_rows
    pre_act = normed * gain_col + bias_col
    act = (jax.nn.silu(pre_act) * valid_rows).astype(jnp.bfloat16)
    act_full = lax.all_gather(act, ("xl", "core"), axis=1, tiled=True)
    act_views = shifted_views(act_full, up_ok, down_ok)
    prediction = conv_views(act_views, conv_weight)
    loss_rows = jnp.dot(onehot, weights_img, precision=HIGH)[:, None, None]
    target_float = targets.reshape(row_total, local_ch, col_count).astype(jnp.float32)
    out_grad = (loss_rows * (prediction - target_float) * valid_rows).astype(jnp.bfloat16)
    act_partial = conv_views(shifted_views(out_grad, up_ok, down_ok), flipped)
    act_grad = sum_chan(act_partial.astype(jnp.bfloat16))
    norm_grad = act_grad * silu_slope(pre_act) * gain_col
    grad_first = jnp.dot(onehot.T, group_sums(norm_grad, groups_here), precision=HIGH)
    grad_second = jnp.dot(onehot.T, group_sums(norm_grad * normed, groups_here), precision=HIGH)
    mean_g = jnp.repeat(
        jnp.dot(onehot, grad_first / counts[:, None], precision=HIGH), group_size, axis=1
    )[:, :, None]
    mean_gn = jnp.repeat(
        jnp.dot(onehot, grad_second / counts[:, None], precision=HIGH), group_size, axis=1
    )[:, :, None]
    x_rows = (rstd_rows * (norm_grad - mean_g - normed * mean_gn) * valid_rows).astype(
        jnp.bfloat16
    )

    tile_len = tile_rows * local_ch
    x_tiles = x_rows.reshape(slots_dev, tile_len, col_count)
    x_tiles = jnp.concatenate([x_tiles, jnp.zeros_like(x_tiles[:1])], axis=0)
    dest_ids = jnp.arange(devices, dtype=jnp.int32)
    send_match = my_owner[None, :] == dest_ids[:, None]
    send_slot = jnp.where(
        jnp.any(send_match, axis=1), jnp.argmax(send_match, axis=1), slots_dev
    ).astype(jnp.int32)
    outgoing = jnp.take(x_tiles, send_slot, axis=0)
    incoming = lax.all_to_all(outgoing, ("xh", "z", "y"), split_axis=0, concat_axis=0, tiled=True)
    slot_ids = jnp.arange(tiles_dev, dtype=jnp.int32)
    hit_mask = (tile_owner[None] == my_index) & (tile_slot[None] == slot_ids[:, None, None])
    recv_src = jnp.argmax(jnp.any(hit_mask, axis=2), axis=1).astype(jnp.int32)
    x_grad = jnp.take(incoming, recv_src, axis=0)
    x_grad = x_grad.reshape(tiles_dev, tile_rows, local_ch, col_count)

    weight_sum = weight_terms(act_views, out_grad)
    weight_grad = sum_space((weight_sum * grad_scale).astype(jnp.bfloat16)).astype(jnp.float32)
    return (x_grad, weight_grad)


WEIGHT_PLAN = "joint"


def add_partner(part, axis):
    swapped = lax.ppermute(part, axis, perm=[(0, 1), (1, 0)])
    return (part.astype(jnp.float32) + swapped.astype(jnp.float32)).astype(part.dtype)


def sum_chan(partial):
    parts = lax.axis_size(("xl", "core"))
    rows, channels, cols = partial.shape
    split = partial.reshape(rows, parts, channels // parts, cols).transpose(1, 0, 2, 3)
    gathered = lax.all_to_all(split, ("xl", "core"), split_axis=0, concat_axis=0, tiled=True)
    return jnp.sum(gathered.astype(jnp.float32), axis=0)


def sum_space(partial):
    shape = partial.shape
    flat = partial.reshape(-1, shape[-1])
    rows = flat.shape[0]
    padded_rows = -(-rows // 256) * 256
    flat = jnp.pad(flat, ((0, padded_rows - rows), (0, 0)))
    if WEIGHT_PLAN == "yz":
        part = lax.psum_scatter(flat, "y", scatter_dimension=0, tiled=True)
        part = lax.psum_scatter(part, "z", scatter_dimension=0, tiled=True)
        part = lax.psum(part, "xh")
        part = lax.all_gather(part, "z", axis=0, tiled=True)
        flat = lax.all_gather(part, "y", axis=0, tiled=True)
    else:
        part = lax.psum_scatter(flat, ("z", "y"), scatter_dimension=0, tiled=True)
        part = add_partner(part, "xh")
        flat = lax.all_gather(part, ("z", "y"), axis=0, tiled=True)
    return flat[:rows].reshape(shape)


def solution(mesh):
    space_axes = ("xh", "z", "y")
    chan_axes = ("xl", "core")
    fine = Mesh(mesh.devices.reshape(2, 4, 4, 2, 2), space_axes + chan_axes)
    tiles = P(space_axes, None, chan_axes, None)
    in_specs = (
        tiles,
        tiles,
        P(chan_axes),
        P(chan_axes),
        P(None, None, chan_axes, None),
        P(),
        P(),
        P(),
        P(),
    )
    out_specs = (tiles, P(None, None, chan_axes, None))
    inner = jax.shard_map(
        fine_local, mesh=fine, in_specs=in_specs, out_specs=out_specs, check_vma=False
    )
    out_shardings = (
        NamedSharding(mesh, P("space", None, "chan", None)),
        NamedSharding(mesh, P(None, None, "chan", None)),
    )

    def run(*args):
        outs = inner(*args)
        return tuple(lax.with_sharding_constraint(o, sh) for o, sh in zip(outs, out_shardings))

    return run


def fine_local(*args):
    return local(*args)
```

```python
import math

import jax
import jax.numpy as jnp
from jax import lax
from jax.sharding import Mesh, NamedSharding
from jax.sharding import PartitionSpec as P

GROUPS = 32


EPS = 1e-05
HIGH = lax.Precision.HIGHEST


def loss_weights(timesteps):
    phase = (timesteps.astype(jnp.float32) / 1000.0 + 0.008) / 1.008 * (math.pi / 2.0)
    alpha_bar = jnp.cos(phase) ** 2
    return jnp.minimum(1.0, 5.0 * (1.0 - alpha_bar) / alpha_bar)


def silu_slope(pre_act):
    sigma_val = jax.nn.sigmoid(pre_act)
    return sigma_val * (1.0 + pre_act * (1.0 - sigma_val))


def group_sums(values, groups):
    grouped = values.reshape(
        values.shape[:-2] + (groups, values.shape[-2] // groups, values.shape[-1])
    )
    return jnp.sum(grouped, axis=(-2, -1))


def norm_stats(sum_first, sum_second, counts):
    mean_img = sum_first / counts[:, None]
    var_img = sum_second / counts[:, None] - mean_img * mean_img
    return (mean_img, lax.rsqrt(var_img + EPS))


def shifted_views(source_field, up_ok, down_ok):
    zero_rows = jnp.zeros_like(source_field[:1])
    up_mask = up_ok.astype(source_field.dtype)[:, None, None]
    down_mask = down_ok.astype(source_field.dtype)[:, None, None]
    rows_above = jnp.concatenate([zero_rows, source_field[:-1]], axis=0) * up_mask
    rows_below = jnp.concatenate([source_field[1:], zero_rows], axis=0) * down_mask
    return [rows_above, source_field, rows_below]


def conv_views(row_views, weight):
    running = None
    for row_tap in range(3):
        source = row_views[row_tap]
        col_count = source.shape[-1]
        padded = jnp.pad(source, ((0, 0), (0, 0), (1, 1)))
        for col_tap in range(3):
            window = padded[:, :, col_tap : col_tap + col_count]
            tap_term = jnp.einsum(
                "rcw,oc->row",
                window,
                weight[row_tap, col_tap],
                preferred_element_type=jnp.float32,
            )
            running = tap_term if running is None else running + tap_term
    return running


def weight_terms(row_views, grad_field):
    col_count = grad_field.shape[-1]
    padded = jnp.pad(grad_field, ((0, 0), (0, 0), (1, 1)))
    shifted = jnp.stack(
        [padded[:, :, 2 - col_tap : 2 - col_tap + col_count] for col_tap in range(3)]
    )
    tap_rows = [
        jnp.einsum("drow,rcw->doc", shifted, source, preferred_element_type=jnp.float32)
        for source in row_views
    ]
    return jnp.stack(tap_rows)


def local(
    latents,
    targets,
    norm_gain,
    norm_bias,
    conv_weight,
    tile_image,
    tile_owner,
    tile_slot,
    timesteps,
):
    my_index = lax.axis_index(("xh", "z", "y"))
    devices = lax.axis_size(("xh", "z", "y"))
    slots_dev, tile_rows, local_ch, col_count = latents.shape
    channels = conv_weight.shape[3]
    group_size = channels // GROUPS
    groups_here = local_ch // group_size
    image_total = timesteps.shape[0]
    tiles_dev = slots_dev // 2
    row_total = slots_dev * tile_rows
    image_ids = jnp.arange(image_total, dtype=jnp.int32)
    counts = jnp.sum(
        (tile_image.reshape(-1)[None, :] == image_ids[:, None]).astype(jnp.float32), axis=1
    ) * float(tile_rows * col_count * group_size)
    weights_img = loss_weights(timesteps)
    flipped = jnp.transpose(conv_weight[::-1, ::-1], (0, 1, 3, 2))
    gain_col = norm_gain[:, None]
    bias_col = norm_bias[:, None]
    grad_scale = 1.0 / math.sqrt(devices * tiles_dev * tile_rows * col_count)

    my_image = lax.dynamic_index_in_dim(tile_image, my_index, 0, keepdims=False)
    my_owner = lax.dynamic_index_in_dim(tile_owner, my_index, 0, keepdims=False)
    row_image = jnp.repeat(my_image, tile_rows)
    row_valid = row_image >= 0
    prev_image = jnp.concatenate([jnp.full((1,), -2, jnp.int32), row_image[:-1]])
    next_image = jnp.concatenate([row_image[1:], jnp.full((1,), -2, jnp.int32)])
    up_ok = row_valid & (prev_image == row_image)
    down_ok = row_valid & (next_image == row_image)
    onehot = (row_image[:, None] == image_ids[None, :]).astype(jnp.float32)
    valid_rows = row_valid.astype(jnp.float32)[:, None, None]

    lat_float = latents.reshape(row_total, local_ch, col_count).astype(jnp.float32)
    part_first = jnp.dot(onehot.T, group_sums(lat_float, groups_here), precision=HIGH)
    part_second = jnp.dot(onehot.T, group_sums(lat_float * lat_float, groups_here), precision=HIGH)
    mean_img, rstd_img = norm_stats(part_first, part_second, counts)
    mean_rows = jnp.repeat(jnp.dot(onehot, mean_img, precision=HIGH), group_size, axis=1)[
        :, :, None
    ]
    rstd_rows = jnp.repeat(jnp.dot(onehot, rstd_img, precision=HIGH), group_size, axis=1)[
        :, :, None
    ]
    normed = (lat_float - mean_rows) * rstd_rows
    pre_act = normed * gain_col + bias_col
    act = (jax.nn.silu(pre_act) * valid_rows).astype(jnp.bfloat16)
    act_full = lax.all_gather(act, ("xl", "core"), axis=1, tiled=True)
    act_views = shifted_views(act_full, up_ok, down_ok)
    prediction = conv_views(act_views, conv_weight)
    loss_rows = jnp.dot(onehot, weights_img, precision=HIGH)[:, None, None]
    target_float = targets.reshape(row_total, local_ch, col_count).astype(jnp.float32)
    out_grad = (loss_rows * (prediction - target_float) * valid_rows).astype(jnp.bfloat16)
    act_partial = conv_views(shifted_views(out_grad, up_ok, down_ok), flipped)
    act_grad = sum_chan(act_partial.astype(jnp.bfloat16))
    norm_grad = act_grad * silu_slope(pre_act) * gain_col
    grad_first = jnp.dot(onehot.T, group_sums(norm_grad, groups_here), precision=HIGH)
    grad_second = jnp.dot(onehot.T, group_sums(norm_grad * normed, groups_here), precision=HIGH)
    mean_g = jnp.repeat(
        jnp.dot(onehot, grad_first / counts[:, None], precision=HIGH), group_size, axis=1
    )[:, :, None]
    mean_gn = jnp.repeat(
        jnp.dot(onehot, grad_second / counts[:, None], precision=HIGH), group_size, axis=1
    )[:, :, None]
    x_rows = (rstd_rows * (norm_grad - mean_g - normed * mean_gn) * valid_rows).astype(
        jnp.bfloat16
    )

    tile_len = tile_rows * local_ch
    x_tiles = x_rows.reshape(slots_dev, tile_len, col_count)
    x_tiles = jnp.concatenate([x_tiles, jnp.zeros_like(x_tiles[:1])], axis=0)
    dest_ids = jnp.arange(devices, dtype=jnp.int32)
    send_match = my_owner[None, :] == dest_ids[:, None]
    send_slot = jnp.where(
        jnp.any(send_match, axis=1), jnp.argmax(send_match, axis=1), slots_dev
    ).astype(jnp.int32)
    outgoing = jnp.take(x_tiles, send_slot, axis=0)
    incoming = lax.all_to_all(outgoing, ("xh", "z", "y"), split_axis=0, concat_axis=0, tiled=True)
    slot_ids = jnp.arange(tiles_dev, dtype=jnp.int32)
    hit_mask = (tile_owner[None] == my_index) & (tile_slot[None] == slot_ids[:, None, None])
    recv_src = jnp.argmax(jnp.any(hit_mask, axis=2), axis=1).astype(jnp.int32)
    x_grad = jnp.take(incoming, recv_src, axis=0)
    x_grad = x_grad.reshape(tiles_dev, tile_rows, local_ch, col_count)

    weight_sum = weight_terms(act_views, out_grad)
    weight_grad = sum_space((weight_sum * grad_scale).astype(jnp.bfloat16)).astype(jnp.float32)
    return (x_grad, weight_grad)


WEIGHT_PLAN = "joint"


def add_partner(part, axis):
    swapped = lax.ppermute(part, axis, perm=[(0, 1), (1, 0)])
    return (part.astype(jnp.float32) + swapped.astype(jnp.float32)).astype(part.dtype)


def sum_chan(partial):
    parts = lax.axis_size(("xl", "core"))
    rows, channels, cols = partial.shape
    split = partial.reshape(rows, parts, channels // parts, cols).transpose(1, 0, 2, 3)
    gathered = lax.all_to_all(split, ("xl", "core"), split_axis=0, concat_axis=0, tiled=True)
    return jnp.sum(gathered.astype(jnp.float32), axis=0)


def sum_space(partial):
    shape = partial.shape
    flat = partial.reshape(-1, shape[-1])
    rows = flat.shape[0]
    padded_rows = -(-rows // 256) * 256
    flat = jnp.pad(flat, ((0, padded_rows - rows), (0, 0)))
    if WEIGHT_PLAN == "yz":
        part = lax.psum_scatter(flat, "y", scatter_dimension=0, tiled=True)
        part = lax.psum_scatter(part, "z", scatter_dimension=0, tiled=True)
        part = lax.psum(part, "xh")
        part = lax.all_gather(part, "z", axis=0, tiled=True)
        flat = lax.all_gather(part, "y", axis=0, tiled=True)
    else:
        part = lax.psum_scatter(flat, ("z", "y"), scatter_dimension=0, tiled=True)
        part = add_partner(part, "xh")
        flat = lax.all_gather(part, ("z", "y"), axis=0, tiled=True)
    return flat[:rows].reshape(shape)


def solution(mesh):
    space_axes = ("xh", "z", "y")
    chan_axes = ("xl", "core")
    fine = Mesh(mesh.devices.reshape(2, 4, 4, 2, 2), space_axes + chan_axes)
    tiles = P(space_axes, None, chan_axes, None)
    in_specs = (
        tiles,
        tiles,
        P(chan_axes),
        P(chan_axes),
        P(None, None, chan_axes, None),
        P(),
        P(),
        P(),
        P(),
    )
    out_specs = (tiles, P(None, None, chan_axes, None))
    inner = jax.shard_map(
        fine_local, mesh=fine, in_specs=in_specs, out_specs=out_specs, check_vma=False
    )
    out_shardings = (
        NamedSharding(mesh, P("space", None, "chan", None)),
        NamedSharding(mesh, P(None, None, "chan", None)),
    )

    def run(*args):
        outs = inner(*args)
        return tuple(lax.with_sharding_constraint(o, sh) for o, sh in zip(outs, out_shardings))

    return run


def fine_local(*args):
    return local(*args)
```

```python
import math

import jax
import jax.numpy as jnp
from jax import lax
from jax.sharding import Mesh, NamedSharding
from jax.sharding import PartitionSpec as P

GROUPS = 32


EPS = 1e-05
HIGH = lax.Precision.HIGHEST


def loss_weights(timesteps):
    phase = (timesteps.astype(jnp.float32) / 1000.0 + 0.008) / 1.008 * (math.pi / 2.0)
    alpha_bar = jnp.cos(phase) ** 2
    return jnp.minimum(1.0, 5.0 * (1.0 - alpha_bar) / alpha_bar)


def silu_slope(pre_act):
    sigma_val = jax.nn.sigmoid(pre_act)
    return sigma_val * (1.0 + pre_act * (1.0 - sigma_val))


def group_sums(values, groups):
    grouped = values.reshape(
        values.shape[:-2] + (groups, values.shape[-2] // groups, values.shape[-1])
    )
    return jnp.sum(grouped, axis=(-2, -1))


def norm_stats(sum_first, sum_second, counts):
    mean_img = sum_first / counts[:, None]
    var_img = sum_second / counts[:, None] - mean_img * mean_img
    return (mean_img, lax.rsqrt(var_img + EPS))


def shifted_views(source_field, up_ok, down_ok):
    zero_rows = jnp.zeros_like(source_field[:1])
    up_mask = up_ok.astype(source_field.dtype)[:, None, None]
    down_mask = down_ok.astype(source_field.dtype)[:, None, None]
    rows_above = jnp.concatenate([zero_rows, source_field[:-1]], axis=0) * up_mask
    rows_below = jnp.concatenate([source_field[1:], zero_rows], axis=0) * down_mask
    return [rows_above, source_field, rows_below]


def conv_views(row_views, weight):
    running = None
    for row_tap in range(3):
        source = row_views[row_tap]
        col_count = source.shape[-1]
        padded = jnp.pad(source, ((0, 0), (0, 0), (1, 1)))
        for col_tap in range(3):
            window = padded[:, :, col_tap : col_tap + col_count]
            tap_term = jnp.einsum(
                "rcw,oc->row",
                window,
                weight[row_tap, col_tap],
                preferred_element_type=jnp.float32,
            )
            running = tap_term if running is None else running + tap_term
    return running


def weight_terms(row_views, grad_field):
    col_count = grad_field.shape[-1]
    padded = jnp.pad(grad_field, ((0, 0), (0, 0), (1, 1)))
    shifted = jnp.stack(
        [padded[:, :, 2 - col_tap : 2 - col_tap + col_count] for col_tap in range(3)]
    )
    tap_rows = [
        jnp.einsum("drow,rcw->doc", shifted, source, preferred_element_type=jnp.float32)
        for source in row_views
    ]
    return jnp.stack(tap_rows)


def grad_conv(row_views, weight, parts):
    col_count = row_views[0].shape[-1]
    cols = []
    for source in row_views:
        padded = jnp.pad(source, ((0, 0), (0, 0), (1, 1)))
        for col_tap in range(3):
            cols.append(padded[:, :, col_tap : col_tap + col_count])
    stacked = jnp.concatenate(cols, axis=1)
    c_total, o_total = weight.shape[2], weight.shape[3]
    matrix = jnp.transpose(weight, (2, 0, 1, 3)).reshape(parts, c_total // parts, 9 * o_total)
    return jnp.einsum("rkw,pck->prcw", stacked, matrix, preferred_element_type=jnp.float32)


def local(
    latents,
    targets,
    norm_gain,
    norm_bias,
    conv_weight,
    tile_image,
    tile_owner,
    tile_slot,
    timesteps,
):
    my_index = lax.axis_index(("xh", "z", "y"))
    devices = lax.axis_size(("xh", "z", "y"))
    slots_dev, tile_rows, local_ch, col_count = latents.shape
    channels = conv_weight.shape[3]
    group_size = channels // GROUPS
    groups_here = local_ch // group_size
    image_total = timesteps.shape[0]
    tiles_dev = slots_dev // 2
    row_total = slots_dev * tile_rows
    image_ids = jnp.arange(image_total, dtype=jnp.int32)
    counts = jnp.sum(
        (tile_image.reshape(-1)[None, :] == image_ids[:, None]).astype(jnp.float32), axis=1
    ) * float(tile_rows * col_count * group_size)
    weights_img = loss_weights(timesteps)
    flipped = jnp.transpose(conv_weight[::-1, ::-1], (0, 1, 3, 2))
    gain_col = norm_gain[:, None]
    bias_col = norm_bias[:, None]
    grad_scale = 1.0 / math.sqrt(devices * tiles_dev * tile_rows * col_count)

    my_image = lax.dynamic_index_in_dim(tile_image, my_index, 0, keepdims=False)
    my_owner = lax.dynamic_index_in_dim(tile_owner, my_index, 0, keepdims=False)
    row_image = jnp.repeat(my_image, tile_rows)
    row_valid = row_image >= 0
    prev_image = jnp.concatenate([jnp.full((1,), -2, jnp.int32), row_image[:-1]])
    next_image = jnp.concatenate([row_image[1:], jnp.full((1,), -2, jnp.int32)])
    up_ok = row_valid & (prev_image == row_image)
    down_ok = row_valid & (next_image == row_image)
    onehot = (row_image[:, None] == image_ids[None, :]).astype(jnp.float32)
    valid_rows = row_valid.astype(jnp.float32)[:, None, None]

    lat_float = latents.reshape(row_total, local_ch, col_count).astype(jnp.float32)
    part_first = jnp.dot(onehot.T, group_sums(lat_float, groups_here), precision=HIGH)
    part_second = jnp.dot(onehot.T, group_sums(lat_float * lat_float, groups_here), precision=HIGH)
    mean_img, rstd_img = norm_stats(part_first, part_second, counts)
    mean_rows = jnp.repeat(jnp.dot(onehot, mean_img, precision=HIGH), group_size, axis=1)[
        :, :, None
    ]
    rstd_rows = jnp.repeat(jnp.dot(onehot, rstd_img, precision=HIGH), group_size, axis=1)[
        :, :, None
    ]
    normed = (lat_float - mean_rows) * rstd_rows
    pre_act = normed * gain_col + bias_col
    act = (jax.nn.silu(pre_act) * valid_rows).astype(jnp.bfloat16)
    act_full = lax.all_gather(act, ("xl", "core"), axis=1, tiled=True)
    act_views = shifted_views(act_full, up_ok, down_ok)
    prediction = conv_views(act_views, conv_weight)
    loss_rows = jnp.dot(onehot, weights_img, precision=HIGH)[:, None, None]
    target_float = targets.reshape(row_total, local_ch, col_count).astype(jnp.float32)
    out_grad = (loss_rows * (prediction - target_float) * valid_rows).astype(jnp.bfloat16)
    parts = lax.axis_size(("xl", "core"))
    act_partial = grad_conv(shifted_views(out_grad, up_ok, down_ok), flipped, parts)
    act_grad = sum_chan(act_partial.astype(jnp.bfloat16))
    norm_grad = act_grad * silu_slope(pre_act) * gain_col
    grad_first = jnp.dot(onehot.T, group_sums(norm_grad, groups_here), precision=HIGH)
    grad_second = jnp.dot(onehot.T, group_sums(norm_grad * normed, groups_here), precision=HIGH)
    mean_g = jnp.repeat(
        jnp.dot(onehot, grad_first / counts[:, None], precision=HIGH), group_size, axis=1
    )[:, :, None]
    mean_gn = jnp.repeat(
        jnp.dot(onehot, grad_second / counts[:, None], precision=HIGH), group_size, axis=1
    )[:, :, None]
    x_rows = (rstd_rows * (norm_grad - mean_g - normed * mean_gn) * valid_rows).astype(
        jnp.bfloat16
    )

    tile_len = tile_rows * local_ch
    x_tiles = x_rows.reshape(slots_dev, tile_len, col_count)
    x_tiles = jnp.concatenate([x_tiles, jnp.zeros_like(x_tiles[:1])], axis=0)
    dest_ids = jnp.arange(devices, dtype=jnp.int32)
    send_match = my_owner[None, :] == dest_ids[:, None]
    send_slot = jnp.where(
        jnp.any(send_match, axis=1), jnp.argmax(send_match, axis=1), slots_dev
    ).astype(jnp.int32)
    outgoing = jnp.take(x_tiles, send_slot, axis=0)
    incoming = lax.all_to_all(outgoing, ("xh", "z", "y"), split_axis=0, concat_axis=0, tiled=True)
    slot_ids = jnp.arange(tiles_dev, dtype=jnp.int32)
    hit_mask = (tile_owner[None] == my_index) & (tile_slot[None] == slot_ids[:, None, None])
    recv_src = jnp.argmax(jnp.any(hit_mask, axis=2), axis=1).astype(jnp.int32)
    x_grad = jnp.take(incoming, recv_src, axis=0)
    x_grad = x_grad.reshape(tiles_dev, tile_rows, local_ch, col_count)

    weight_sum = weight_terms(act_views, out_grad)
    weight_grad = sum_space((weight_sum * grad_scale).astype(jnp.bfloat16)).astype(jnp.float32)
    return (x_grad, weight_grad)


WEIGHT_PLAN = "joint"


def add_partner(part, axis):
    swapped = lax.ppermute(part, axis, perm=[(0, 1), (1, 0)])
    return (part.astype(jnp.float32) + swapped.astype(jnp.float32)).astype(part.dtype)


def sum_chan(partial):
    gathered = lax.all_to_all(partial, ("xl", "core"), split_axis=0, concat_axis=0, tiled=True)
    return jnp.sum(gathered.astype(jnp.float32), axis=0)


def sum_space(partial):
    shape = partial.shape
    flat = partial.reshape(-1, shape[-1])
    rows = flat.shape[0]
    padded_rows = -(-rows // 256) * 256
    flat = jnp.pad(flat, ((0, padded_rows - rows), (0, 0)))
    if WEIGHT_PLAN == "yz":
        part = lax.psum_scatter(flat, "y", scatter_dimension=0, tiled=True)
        part = lax.psum_scatter(part, "z", scatter_dimension=0, tiled=True)
        part = lax.psum(part, "xh")
        part = lax.all_gather(part, "z", axis=0, tiled=True)
        flat = lax.all_gather(part, "y", axis=0, tiled=True)
    else:
        part = lax.psum_scatter(flat, ("z", "y"), scatter_dimension=0, tiled=True)
        part = add_partner(part, "xh")
        flat = lax.all_gather(part, ("z", "y"), axis=0, tiled=True)
    return flat[:rows].reshape(shape)


def solution(mesh):
    space_axes = ("xh", "z", "y")
    chan_axes = ("xl", "core")
    fine = Mesh(mesh.devices.reshape(2, 4, 4, 2, 2), space_axes + chan_axes)
    tiles = P(space_axes, None, chan_axes, None)
    in_specs = (
        tiles,
        tiles,
        P(chan_axes),
        P(chan_axes),
        P(None, None, chan_axes, None),
        P(),
        P(),
        P(),
        P(),
    )
    out_specs = (tiles, P(None, None, chan_axes, None))
    inner = jax.shard_map(
        fine_local, mesh=fine, in_specs=in_specs, out_specs=out_specs, check_vma=False
    )
    out_shardings = (
        NamedSharding(mesh, P("space", None, "chan", None)),
        NamedSharding(mesh, P(None, None, "chan", None)),
    )

    def run(*args):
        outs = inner(*args)
        return tuple(lax.with_sharding_constraint(o, sh) for o, sh in zip(outs, out_shardings))

    return run


def fine_local(*args):
    return local(*args)
```

```python
import math

import jax
import jax.numpy as jnp
from jax import lax
from jax.sharding import Mesh, NamedSharding
from jax.sharding import PartitionSpec as P

GROUPS = 32


EPS = 1e-05
HIGH = lax.Precision.HIGHEST


def loss_weights(timesteps):
    phase = (timesteps.astype(jnp.float32) / 1000.0 + 0.008) / 1.008 * (math.pi / 2.0)
    alpha_bar = jnp.cos(phase) ** 2
    return jnp.minimum(1.0, 5.0 * (1.0 - alpha_bar) / alpha_bar)


def silu_slope(pre_act):
    sigma_val = jax.nn.sigmoid(pre_act)
    return sigma_val * (1.0 + pre_act * (1.0 - sigma_val))


def group_sums(values, groups):
    grouped = values.reshape(
        values.shape[:-2] + (groups, values.shape[-2] // groups, values.shape[-1])
    )
    return jnp.sum(grouped, axis=(-2, -1))


def norm_stats(sum_first, sum_second, counts):
    mean_img = sum_first / counts[:, None]
    var_img = sum_second / counts[:, None] - mean_img * mean_img
    return (mean_img, lax.rsqrt(var_img + EPS))


def shifted_views(source_field, up_ok, down_ok):
    zero_rows = jnp.zeros_like(source_field[:1])
    up_mask = up_ok.astype(source_field.dtype)[:, None, None]
    down_mask = down_ok.astype(source_field.dtype)[:, None, None]
    rows_above = jnp.concatenate([zero_rows, source_field[:-1]], axis=0) * up_mask
    rows_below = jnp.concatenate([source_field[1:], zero_rows], axis=0) * down_mask
    return [rows_above, source_field, rows_below]


def conv_views(row_views, weight):
    running = None
    for row_tap in range(3):
        source = row_views[row_tap]
        col_count = source.shape[-1]
        padded = jnp.pad(source, ((0, 0), (0, 0), (1, 1)))
        for col_tap in range(3):
            window = padded[:, :, col_tap : col_tap + col_count]
            tap_term = jnp.einsum(
                "rcw,oc->row",
                window,
                weight[row_tap, col_tap],
                preferred_element_type=jnp.float32,
            )
            running = tap_term if running is None else running + tap_term
    return running


def weight_terms(row_views, grad_field):
    col_count = grad_field.shape[-1]
    padded = jnp.pad(grad_field, ((0, 0), (0, 0), (1, 1)))
    shifted = jnp.stack(
        [padded[:, :, 2 - col_tap : 2 - col_tap + col_count] for col_tap in range(3)]
    )
    tap_rows = [
        jnp.einsum("drow,rcw->doc", shifted, source, preferred_element_type=jnp.float32)
        for source in row_views
    ]
    return jnp.stack(tap_rows)


def grad_conv(row_views, weight, parts):
    col_count = row_views[0].shape[-1]
    cols = []
    for source in row_views:
        padded = jnp.pad(source, ((0, 0), (0, 0), (1, 1)))
        for col_tap in range(3):
            cols.append(padded[:, :, col_tap : col_tap + col_count])
    stacked = jnp.concatenate(cols, axis=1)
    c_total, o_total = weight.shape[2], weight.shape[3]
    matrix = jnp.transpose(weight, (2, 0, 1, 3)).reshape(parts, c_total // parts, 9 * o_total)
    return jnp.einsum("rkw,pck->prcw", stacked, matrix, preferred_element_type=jnp.float32)


def local(
    latents,
    targets,
    norm_gain,
    norm_bias,
    conv_weight,
    tile_image,
    tile_owner,
    tile_slot,
    timesteps,
):
    my_index = lax.axis_index(("xh", "z", "y"))
    devices = lax.axis_size(("xh", "z", "y"))
    slots_dev, tile_rows, local_ch, col_count = latents.shape
    channels = conv_weight.shape[3]
    group_size = channels // GROUPS
    groups_here = local_ch // group_size
    image_total = timesteps.shape[0]
    tiles_dev = slots_dev // 2
    row_total = slots_dev * tile_rows
    image_ids = jnp.arange(image_total, dtype=jnp.int32)
    counts = jnp.sum(
        (tile_image.reshape(-1)[None, :] == image_ids[:, None]).astype(jnp.float32), axis=1
    ) * float(tile_rows * col_count * group_size)
    weights_img = loss_weights(timesteps)
    flipped = jnp.transpose(conv_weight[::-1, ::-1], (0, 1, 3, 2))
    gain_col = norm_gain[:, None]
    bias_col = norm_bias[:, None]
    grad_scale = 1.0 / math.sqrt(devices * tiles_dev * tile_rows * col_count)

    my_image = lax.dynamic_index_in_dim(tile_image, my_index, 0, keepdims=False)
    my_owner = lax.dynamic_index_in_dim(tile_owner, my_index, 0, keepdims=False)
    row_image = jnp.repeat(my_image, tile_rows)
    row_valid = row_image >= 0
    prev_image = jnp.concatenate([jnp.full((1,), -2, jnp.int32), row_image[:-1]])
    next_image = jnp.concatenate([row_image[1:], jnp.full((1,), -2, jnp.int32)])
    up_ok = row_valid & (prev_image == row_image)
    down_ok = row_valid & (next_image == row_image)
    onehot = (row_image[:, None] == image_ids[None, :]).astype(jnp.float32)
    valid_rows = row_valid.astype(jnp.float32)[:, None, None]

    lat_float = latents.reshape(row_total, local_ch, col_count).astype(jnp.float32)
    part_first = jnp.dot(onehot.T, group_sums(lat_float, groups_here), precision=HIGH)
    part_second = jnp.dot(onehot.T, group_sums(lat_float * lat_float, groups_here), precision=HIGH)
    mean_img, rstd_img = norm_stats(part_first, part_second, counts)
    mean_rows = jnp.repeat(jnp.dot(onehot, mean_img, precision=HIGH), group_size, axis=1)[
        :, :, None
    ]
    rstd_rows = jnp.repeat(jnp.dot(onehot, rstd_img, precision=HIGH), group_size, axis=1)[
        :, :, None
    ]
    normed = (lat_float - mean_rows) * rstd_rows
    pre_act = normed * gain_col + bias_col
    act = (jax.nn.silu(pre_act) * valid_rows).astype(jnp.bfloat16)
    act_full = lax.all_gather(act, ("xl", "core"), axis=1, tiled=True)
    act_views = shifted_views(act_full, up_ok, down_ok)
    prediction = conv_views(act_views, conv_weight)
    loss_rows = jnp.dot(onehot, weights_img, precision=HIGH)[:, None, None]
    target_float = targets.reshape(row_total, local_ch, col_count).astype(jnp.float32)
    out_grad = (loss_rows * (prediction - target_float) * valid_rows).astype(jnp.bfloat16)
    parts = lax.axis_size(("xl", "core"))
    act_partial = grad_conv(shifted_views(out_grad, up_ok, down_ok), flipped, parts)
    act_grad = sum_chan(act_partial.astype(jnp.bfloat16))
    norm_grad = act_grad * silu_slope(pre_act) * gain_col
    grad_first = jnp.dot(onehot.T, group_sums(norm_grad, groups_here), precision=HIGH)
    grad_second = jnp.dot(onehot.T, group_sums(norm_grad * normed, groups_here), precision=HIGH)
    mean_g = jnp.repeat(
        jnp.dot(onehot, grad_first / counts[:, None], precision=HIGH), group_size, axis=1
    )[:, :, None]
    mean_gn = jnp.repeat(
        jnp.dot(onehot, grad_second / counts[:, None], precision=HIGH), group_size, axis=1
    )[:, :, None]
    x_rows = (rstd_rows * (norm_grad - mean_g - normed * mean_gn) * valid_rows).astype(
        jnp.bfloat16
    )

    tile_len = tile_rows * local_ch
    x_tiles = x_rows.reshape(slots_dev, tile_len, col_count)
    x_tiles = jnp.concatenate([x_tiles, jnp.zeros_like(x_tiles[:1])], axis=0)
    dest_ids = jnp.arange(devices, dtype=jnp.int32)
    send_match = my_owner[None, :] == dest_ids[:, None]
    send_slot = jnp.where(
        jnp.any(send_match, axis=1), jnp.argmax(send_match, axis=1), slots_dev
    ).astype(jnp.int32)
    outgoing = jnp.take(x_tiles, send_slot, axis=0)
    incoming = lax.all_to_all(outgoing, ("xh", "z", "y"), split_axis=0, concat_axis=0, tiled=True)
    slot_ids = jnp.arange(tiles_dev, dtype=jnp.int32)
    hit_mask = (tile_owner[None] == my_index) & (tile_slot[None] == slot_ids[:, None, None])
    recv_src = jnp.argmax(jnp.any(hit_mask, axis=2), axis=1).astype(jnp.int32)
    x_grad = jnp.take(incoming, recv_src, axis=0)
    x_grad = x_grad.reshape(tiles_dev, tile_rows, local_ch, col_count)

    weight_sum = weight_terms(act_views, out_grad)
    weight_grad = sum_space((weight_sum * grad_scale).astype(jnp.bfloat16)).astype(jnp.float32)
    return (x_grad, weight_grad)


WEIGHT_PLAN = "joint"


def gather_all(part, axes):
    parts = lax.axis_size(axes)
    copies = jnp.broadcast_to(part[None], (parts,) + part.shape)
    gathered = lax.all_to_all(copies, axes, split_axis=0, concat_axis=0, tiled=True)
    return gathered.reshape((-1,) + part.shape[1:])


def add_partner(part, axis):
    swapped = lax.ppermute(part, axis, perm=[(0, 1), (1, 0)])
    return (part.astype(jnp.float32) + swapped.astype(jnp.float32)).astype(part.dtype)


def sum_chan(partial):
    gathered = lax.all_to_all(partial, ("xl", "core"), split_axis=0, concat_axis=0, tiled=True)
    return jnp.sum(gathered.astype(jnp.float32), axis=0)


def sum_space(partial):
    shape = partial.shape
    flat = partial.reshape(-1, shape[-1])
    rows = flat.shape[0]
    padded_rows = -(-rows // 256) * 256
    flat = jnp.pad(flat, ((0, padded_rows - rows), (0, 0)))
    if WEIGHT_PLAN == "yz":
        part = lax.psum_scatter(flat, "y", scatter_dimension=0, tiled=True)
        part = lax.psum_scatter(part, "z", scatter_dimension=0, tiled=True)
        part = lax.psum(part, "xh")
        part = lax.all_gather(part, "z", axis=0, tiled=True)
        flat = lax.all_gather(part, "y", axis=0, tiled=True)
    else:
        part = lax.psum_scatter(flat, ("z", "y"), scatter_dimension=0, tiled=True)
        part = add_partner(part, "xh")
        flat = gather_all(part, ("z", "y"))
    return flat[:rows].reshape(shape)


def solution(mesh):
    space_axes = ("xh", "z", "y")
    chan_axes = ("xl", "core")
    fine = Mesh(mesh.devices.reshape(2, 4, 4, 2, 2), space_axes + chan_axes)
    tiles = P(space_axes, None, chan_axes, None)
    in_specs = (
        tiles,
        tiles,
        P(chan_axes),
        P(chan_axes),
        P(None, None, chan_axes, None),
        P(),
        P(),
        P(),
        P(),
    )
    out_specs = (tiles, P(None, None, chan_axes, None))
    inner = jax.shard_map(
        fine_local, mesh=fine, in_specs=in_specs, out_specs=out_specs, check_vma=False
    )
    out_shardings = (
        NamedSharding(mesh, P("space", None, "chan", None)),
        NamedSharding(mesh, P(None, None, "chan", None)),
    )

    def run(*args):
        outs = inner(*args)
        return tuple(lax.with_sharding_constraint(o, sh) for o, sh in zip(outs, out_shardings))

    return run


def fine_local(*args):
    return local(*args)
```

```python
import math

import jax
import jax.numpy as jnp
from jax import lax
from jax.sharding import Mesh, NamedSharding
from jax.sharding import PartitionSpec as P

GROUPS = 32


EPS = 1e-05
HIGH = lax.Precision.HIGHEST


def loss_weights(timesteps):
    phase = (timesteps.astype(jnp.float32) / 1000.0 + 0.008) / 1.008 * (math.pi / 2.0)
    alpha_bar = jnp.cos(phase) ** 2
    return jnp.minimum(1.0, 5.0 * (1.0 - alpha_bar) / alpha_bar)


def silu_slope(pre_act):
    sigma_val = jax.nn.sigmoid(pre_act)
    return sigma_val * (1.0 + pre_act * (1.0 - sigma_val))


def group_sums(values, groups):
    grouped = values.reshape(
        values.shape[:-2] + (groups, values.shape[-2] // groups, values.shape[-1])
    )
    return jnp.sum(grouped, axis=(-2, -1))


def norm_stats(sum_first, sum_second, counts):
    mean_img = sum_first / counts[:, None]
    var_img = sum_second / counts[:, None] - mean_img * mean_img
    return (mean_img, lax.rsqrt(var_img + EPS))


def shifted_views(source_field, up_ok, down_ok):
    zero_rows = jnp.zeros_like(source_field[:1])
    up_mask = up_ok.astype(source_field.dtype)[:, None, None]
    down_mask = down_ok.astype(source_field.dtype)[:, None, None]
    rows_above = jnp.concatenate([zero_rows, source_field[:-1]], axis=0) * up_mask
    rows_below = jnp.concatenate([source_field[1:], zero_rows], axis=0) * down_mask
    return [rows_above, source_field, rows_below]


def conv_views(row_views, weight):
    running = None
    for row_tap in range(3):
        source = row_views[row_tap]
        col_count = source.shape[-1]
        padded = jnp.pad(source, ((0, 0), (0, 0), (1, 1)))
        for col_tap in range(3):
            window = padded[:, :, col_tap : col_tap + col_count]
            tap_term = jnp.einsum(
                "rcw,oc->row",
                window,
                weight[row_tap, col_tap],
                preferred_element_type=jnp.float32,
            )
            running = tap_term if running is None else running + tap_term
    return running


def weight_terms(row_views, grad_field):
    col_count = grad_field.shape[-1]
    padded = jnp.pad(grad_field, ((0, 0), (0, 0), (1, 1)))
    shifted = jnp.stack(
        [padded[:, :, 2 - col_tap : 2 - col_tap + col_count] for col_tap in range(3)]
    )
    tap_rows = [
        jnp.einsum("drow,rcw->doc", shifted, source, preferred_element_type=jnp.float32)
        for source in row_views
    ]
    return jnp.stack(tap_rows)


def grad_conv(row_views, weight, parts):
    col_count = row_views[0].shape[-1]
    cols = []
    for source in row_views:
        padded = jnp.pad(source, ((0, 0), (0, 0), (1, 1)))
        for col_tap in range(3):
            cols.append(padded[:, :, col_tap : col_tap + col_count])
    stacked = jnp.concatenate(cols, axis=1)
    c_total, o_total = weight.shape[2], weight.shape[3]
    matrix = jnp.transpose(weight, (2, 0, 1, 3)).reshape(parts, c_total // parts, 9 * o_total)
    return jnp.einsum("rkw,pck->prcw", stacked, matrix, preferred_element_type=jnp.float32)


def local(
    latents,
    targets,
    norm_gain,
    norm_bias,
    conv_weight,
    tile_image,
    tile_owner,
    tile_slot,
    timesteps,
):
    my_index = lax.axis_index(("xh", "z", "y"))
    devices = lax.axis_size(("xh", "z", "y"))
    slots_dev, tile_rows, local_ch, col_count = latents.shape
    channels = conv_weight.shape[3]
    group_size = channels // GROUPS
    groups_here = local_ch // group_size
    image_total = timesteps.shape[0]
    tiles_dev = slots_dev // 2
    row_total = slots_dev * tile_rows
    image_ids = jnp.arange(image_total, dtype=jnp.int32)
    counts = jnp.sum(
        (tile_image.reshape(-1)[None, :] == image_ids[:, None]).astype(jnp.float32), axis=1
    ) * float(tile_rows * col_count * group_size)
    weights_img = loss_weights(timesteps)
    flipped = jnp.transpose(conv_weight[::-1, ::-1], (0, 1, 3, 2))
    gain_col = norm_gain[:, None]
    bias_col = norm_bias[:, None]
    grad_scale = 1.0 / math.sqrt(devices * tiles_dev * tile_rows * col_count)

    my_image = lax.dynamic_index_in_dim(tile_image, my_index, 0, keepdims=False)
    my_owner = lax.dynamic_index_in_dim(tile_owner, my_index, 0, keepdims=False)
    row_image = jnp.repeat(my_image, tile_rows)
    row_valid = row_image >= 0
    prev_image = jnp.concatenate([jnp.full((1,), -2, jnp.int32), row_image[:-1]])
    next_image = jnp.concatenate([row_image[1:], jnp.full((1,), -2, jnp.int32)])
    up_ok = row_valid & (prev_image == row_image)
    down_ok = row_valid & (next_image == row_image)
    onehot = (row_image[:, None] == image_ids[None, :]).astype(jnp.float32)
    valid_rows = row_valid.astype(jnp.float32)[:, None, None]

    lat_float = latents.reshape(row_total, local_ch, col_count).astype(jnp.float32)
    part_first = jnp.dot(onehot.T, group_sums(lat_float, groups_here), precision=HIGH)
    part_second = jnp.dot(onehot.T, group_sums(lat_float * lat_float, groups_here), precision=HIGH)
    mean_img, rstd_img = norm_stats(part_first, part_second, counts)
    mean_rows = jnp.repeat(jnp.dot(onehot, mean_img, precision=HIGH), group_size, axis=1)[
        :, :, None
    ]
    rstd_rows = jnp.repeat(jnp.dot(onehot, rstd_img, precision=HIGH), group_size, axis=1)[
        :, :, None
    ]
    normed = (lat_float - mean_rows) * rstd_rows
    pre_act = normed * gain_col + bias_col
    act = (jax.nn.silu(pre_act) * valid_rows).astype(jnp.bfloat16)
    act_full = lax.all_gather(act, ("xl", "core"), axis=1, tiled=True)
    act_views = shifted_views(act_full, up_ok, down_ok)
    prediction = conv_views(act_views, conv_weight)
    loss_rows = jnp.dot(onehot, weights_img, precision=HIGH)[:, None, None]
    target_float = targets.reshape(row_total, local_ch, col_count).astype(jnp.float32)
    out_grad = (loss_rows * (prediction - target_float) * valid_rows).astype(jnp.bfloat16)
    parts = lax.axis_size(("xl", "core"))
    act_partial = grad_conv(shifted_views(out_grad, up_ok, down_ok), flipped, parts)
    act_grad = sum_chan(act_partial.astype(jnp.bfloat16))
    norm_grad = act_grad * silu_slope(pre_act) * gain_col
    grad_first = jnp.dot(onehot.T, group_sums(norm_grad, groups_here), precision=HIGH)
    grad_second = jnp.dot(onehot.T, group_sums(norm_grad * normed, groups_here), precision=HIGH)
    mean_g = jnp.repeat(
        jnp.dot(onehot, grad_first / counts[:, None], precision=HIGH), group_size, axis=1
    )[:, :, None]
    mean_gn = jnp.repeat(
        jnp.dot(onehot, grad_second / counts[:, None], precision=HIGH), group_size, axis=1
    )[:, :, None]
    x_rows = (rstd_rows * (norm_grad - mean_g - normed * mean_gn) * valid_rows).astype(
        jnp.bfloat16
    )

    tile_len = tile_rows * local_ch
    x_tiles = x_rows.reshape(slots_dev, tile_len, col_count)
    x_tiles = jnp.concatenate([x_tiles, jnp.zeros_like(x_tiles[:1])], axis=0)
    dest_ids = jnp.arange(devices, dtype=jnp.int32)
    send_match = my_owner[None, :] == dest_ids[:, None]
    send_slot = jnp.where(
        jnp.any(send_match, axis=1), jnp.argmax(send_match, axis=1), slots_dev
    ).astype(jnp.int32)
    outgoing = jnp.take(x_tiles, send_slot, axis=0)
    incoming = lax.all_to_all(outgoing, ("xh", "z", "y"), split_axis=0, concat_axis=0, tiled=True)
    slot_ids = jnp.arange(tiles_dev, dtype=jnp.int32)
    hit_mask = (tile_owner[None] == my_index) & (tile_slot[None] == slot_ids[:, None, None])
    recv_src = jnp.argmax(jnp.any(hit_mask, axis=2), axis=1).astype(jnp.int32)
    x_grad = jnp.take(incoming, recv_src, axis=0)
    x_grad = x_grad.reshape(tiles_dev, tile_rows, local_ch, col_count)

    weight_sum = weight_terms(act_views, out_grad)
    weight_grad = sum_space((weight_sum * grad_scale).astype(jnp.bfloat16)).astype(jnp.float32)
    return (x_grad, weight_grad)


WEIGHT_PLAN = "joint"


def scatter_sum(flat, axes):
    parts = lax.axis_size(axes)
    split = flat.reshape((parts, flat.shape[0] // parts) + flat.shape[1:])
    gathered = lax.all_to_all(split, axes, split_axis=0, concat_axis=0, tiled=True)
    return jnp.sum(gathered.astype(jnp.float32), axis=0).astype(flat.dtype)


def add_partner(part, axis):
    swapped = lax.ppermute(part, axis, perm=[(0, 1), (1, 0)])
    return (part.astype(jnp.float32) + swapped.astype(jnp.float32)).astype(part.dtype)


def sum_chan(partial):
    gathered = lax.all_to_all(partial, ("xl", "core"), split_axis=0, concat_axis=0, tiled=True)
    return jnp.sum(gathered.astype(jnp.float32), axis=0)


def sum_space(partial):
    shape = partial.shape
    flat = partial.reshape(-1, shape[-1])
    rows = flat.shape[0]
    padded_rows = -(-rows // 256) * 256
    flat = jnp.pad(flat, ((0, padded_rows - rows), (0, 0)))
    if WEIGHT_PLAN == "yz":
        part = lax.psum_scatter(flat, "y", scatter_dimension=0, tiled=True)
        part = lax.psum_scatter(part, "z", scatter_dimension=0, tiled=True)
        part = lax.psum(part, "xh")
        part = lax.all_gather(part, "z", axis=0, tiled=True)
        flat = lax.all_gather(part, "y", axis=0, tiled=True)
    else:
        part = scatter_sum(flat, ("z", "y"))
        part = add_partner(part, "xh")
        flat = lax.all_gather(part, ("z", "y"), axis=0, tiled=True)
    return flat[:rows].reshape(shape)


def solution(mesh):
    space_axes = ("xh", "z", "y")
    chan_axes = ("xl", "core")
    fine = Mesh(mesh.devices.reshape(2, 4, 4, 2, 2), space_axes + chan_axes)
    tiles = P(space_axes, None, chan_axes, None)
    in_specs = (
        tiles,
        tiles,
        P(chan_axes),
        P(chan_axes),
        P(None, None, chan_axes, None),
        P(),
        P(),
        P(),
        P(),
    )
    out_specs = (tiles, P(None, None, chan_axes, None))
    inner = jax.shard_map(
        fine_local, mesh=fine, in_specs=in_specs, out_specs=out_specs, check_vma=False
    )
    out_shardings = (
        NamedSharding(mesh, P("space", None, "chan", None)),
        NamedSharding(mesh, P(None, None, "chan", None)),
    )

    def run(*args):
        outs = inner(*args)
        return tuple(lax.with_sharding_constraint(o, sh) for o, sh in zip(outs, out_shardings))

    return run


def fine_local(*args):
    return local(*args)
```

```python
import math

import jax
import jax.numpy as jnp
from jax import lax
from jax.sharding import Mesh, NamedSharding
from jax.sharding import PartitionSpec as P

GROUPS = 32


EPS = 1e-05
HIGH = lax.Precision.HIGHEST


def loss_weights(timesteps):
    phase = (timesteps.astype(jnp.float32) / 1000.0 + 0.008) / 1.008 * (math.pi / 2.0)
    alpha_bar = jnp.cos(phase) ** 2
    return jnp.minimum(1.0, 5.0 * (1.0 - alpha_bar) / alpha_bar)


def silu_slope(pre_act):
    sigma_val = jax.nn.sigmoid(pre_act)
    return sigma_val * (1.0 + pre_act * (1.0 - sigma_val))


def group_sums(values, groups):
    grouped = values.reshape(
        values.shape[:-2] + (groups, values.shape[-2] // groups, values.shape[-1])
    )
    return jnp.sum(grouped, axis=(-2, -1))


def norm_stats(sum_first, sum_second, counts):
    mean_img = sum_first / counts[:, None]
    var_img = sum_second / counts[:, None] - mean_img * mean_img
    return (mean_img, lax.rsqrt(var_img + EPS))


def shifted_views(source_field, up_ok, down_ok):
    zero_rows = jnp.zeros_like(source_field[:1])
    up_mask = up_ok.astype(source_field.dtype)[:, None, None]
    down_mask = down_ok.astype(source_field.dtype)[:, None, None]
    rows_above = jnp.concatenate([zero_rows, source_field[:-1]], axis=0) * up_mask
    rows_below = jnp.concatenate([source_field[1:], zero_rows], axis=0) * down_mask
    return [rows_above, source_field, rows_below]


def conv_views(row_views, weight):
    running = None
    for row_tap in range(3):
        source = row_views[row_tap]
        col_count = source.shape[-1]
        padded = jnp.pad(source, ((0, 0), (0, 0), (1, 1)))
        for col_tap in range(3):
            window = padded[:, :, col_tap : col_tap + col_count]
            tap_term = jnp.einsum(
                "rcw,oc->row",
                window,
                weight[row_tap, col_tap],
                preferred_element_type=jnp.float32,
            )
            running = tap_term if running is None else running + tap_term
    return running


def weight_terms(row_views, grad_field):
    col_count = grad_field.shape[-1]
    padded = jnp.pad(grad_field, ((0, 0), (0, 0), (1, 1)))
    shifted = jnp.stack(
        [padded[:, :, 2 - col_tap : 2 - col_tap + col_count] for col_tap in range(3)]
    )
    tap_rows = [
        jnp.einsum("drow,rcw->doc", shifted, source, preferred_element_type=jnp.float32)
        for source in row_views
    ]
    return jnp.stack(tap_rows)


def grad_conv(row_views, matrix):
    col_count = row_views[0].shape[-1]
    cols = []
    for source in row_views:
        padded = jnp.pad(source, ((0, 0), (0, 0), (1, 1)))
        for col_tap in range(3):
            cols.append(padded[:, :, col_tap : col_tap + col_count])
    stacked = jnp.concatenate(cols, axis=1)
    return jnp.einsum("rkw,pck->prcw", stacked, matrix, preferred_element_type=jnp.float32)


def tap_matrix(weight, parts):
    c_total, o_total = weight.shape[2], weight.shape[3]
    return jnp.transpose(weight, (2, 0, 1, 3)).reshape(parts, c_total // parts, 9 * o_total)


def local(
    latents,
    targets,
    norm_gain,
    norm_bias,
    conv_weight,
    tile_image,
    tile_owner,
    tile_slot,
    timesteps,
):
    my_index = lax.axis_index(("xh", "z", "y"))
    devices = lax.axis_size(("xh", "z", "y"))
    slots_dev, tile_rows, local_ch, col_count = latents.shape
    channels = conv_weight.shape[3]
    group_size = channels // GROUPS
    groups_here = local_ch // group_size
    image_total = timesteps.shape[0]
    tiles_dev = slots_dev // 2
    row_total = slots_dev * tile_rows
    image_ids = jnp.arange(image_total, dtype=jnp.int32)
    counts = jnp.sum(
        (tile_image.reshape(-1)[None, :] == image_ids[:, None]).astype(jnp.float32), axis=1
    ) * float(tile_rows * col_count * group_size)
    weights_img = loss_weights(timesteps)
    flipped = jnp.transpose(conv_weight[::-1, ::-1], (0, 1, 3, 2))
    gain_col = norm_gain[:, None]
    bias_col = norm_bias[:, None]
    grad_scale = 1.0 / math.sqrt(devices * tiles_dev * tile_rows * col_count)

    my_image = lax.dynamic_index_in_dim(tile_image, my_index, 0, keepdims=False)
    my_owner = lax.dynamic_index_in_dim(tile_owner, my_index, 0, keepdims=False)
    row_image = jnp.repeat(my_image, tile_rows)
    row_valid = row_image >= 0
    prev_image = jnp.concatenate([jnp.full((1,), -2, jnp.int32), row_image[:-1]])
    next_image = jnp.concatenate([row_image[1:], jnp.full((1,), -2, jnp.int32)])
    up_ok = row_valid & (prev_image == row_image)
    down_ok = row_valid & (next_image == row_image)
    onehot = (row_image[:, None] == image_ids[None, :]).astype(jnp.float32)
    valid_rows = row_valid.astype(jnp.float32)[:, None, None]

    lat_float = latents.reshape(row_total, local_ch, col_count).astype(jnp.float32)
    part_first = jnp.dot(onehot.T, group_sums(lat_float, groups_here), precision=HIGH)
    part_second = jnp.dot(onehot.T, group_sums(lat_float * lat_float, groups_here), precision=HIGH)
    mean_img, rstd_img = norm_stats(part_first, part_second, counts)
    mean_rows = jnp.repeat(jnp.dot(onehot, mean_img, precision=HIGH), group_size, axis=1)[
        :, :, None
    ]
    rstd_rows = jnp.repeat(jnp.dot(onehot, rstd_img, precision=HIGH), group_size, axis=1)[
        :, :, None
    ]
    normed = (lat_float - mean_rows) * rstd_rows
    pre_act = normed * gain_col + bias_col
    act = (jax.nn.silu(pre_act) * valid_rows).astype(jnp.bfloat16)
    act_full = lax.all_gather(act, ("xl", "core"), axis=1, tiled=True)
    parts = lax.axis_size(("xl", "core"))
    act_full, matrix = lax.optimization_barrier((act_full, tap_matrix(flipped, parts)))
    act_views = shifted_views(act_full, up_ok, down_ok)
    prediction = conv_views(act_views, conv_weight)
    loss_rows = jnp.dot(onehot, weights_img, precision=HIGH)[:, None, None]
    target_float = targets.reshape(row_total, local_ch, col_count).astype(jnp.float32)
    out_grad = (loss_rows * (prediction - target_float) * valid_rows).astype(jnp.bfloat16)
    act_partial = grad_conv(shifted_views(out_grad, up_ok, down_ok), matrix)
    act_grad = sum_chan(act_partial.astype(jnp.bfloat16))
    norm_grad = act_grad * silu_slope(pre_act) * gain_col
    grad_first = jnp.dot(onehot.T, group_sums(norm_grad, groups_here), precision=HIGH)
    grad_second = jnp.dot(onehot.T, group_sums(norm_grad * normed, groups_here), precision=HIGH)
    mean_g = jnp.repeat(
        jnp.dot(onehot, grad_first / counts[:, None], precision=HIGH), group_size, axis=1
    )[:, :, None]
    mean_gn = jnp.repeat(
        jnp.dot(onehot, grad_second / counts[:, None], precision=HIGH), group_size, axis=1
    )[:, :, None]
    x_rows = (rstd_rows * (norm_grad - mean_g - normed * mean_gn) * valid_rows).astype(
        jnp.bfloat16
    )

    tile_len = tile_rows * local_ch
    x_tiles = x_rows.reshape(slots_dev, tile_len, col_count)
    x_tiles = jnp.concatenate([x_tiles, jnp.zeros_like(x_tiles[:1])], axis=0)
    dest_ids = jnp.arange(devices, dtype=jnp.int32)
    send_match = my_owner[None, :] == dest_ids[:, None]
    send_slot = jnp.where(
        jnp.any(send_match, axis=1), jnp.argmax(send_match, axis=1), slots_dev
    ).astype(jnp.int32)
    outgoing = jnp.take(x_tiles, send_slot, axis=0)
    incoming = lax.all_to_all(outgoing, ("xh", "z", "y"), split_axis=0, concat_axis=0, tiled=True)
    slot_ids = jnp.arange(tiles_dev, dtype=jnp.int32)
    hit_mask = (tile_owner[None] == my_index) & (tile_slot[None] == slot_ids[:, None, None])
    recv_src = jnp.argmax(jnp.any(hit_mask, axis=2), axis=1).astype(jnp.int32)
    x_grad = jnp.take(incoming, recv_src, axis=0)
    x_grad = x_grad.reshape(tiles_dev, tile_rows, local_ch, col_count)

    weight_sum = weight_terms(act_views, out_grad)
    weight_grad = sum_space((weight_sum * grad_scale).astype(jnp.bfloat16)).astype(jnp.float32)
    return (x_grad, weight_grad)


WEIGHT_PLAN = "joint"


def scatter_sum(flat, axes):
    parts = lax.axis_size(axes)
    split = flat.reshape((parts, flat.shape[0] // parts) + flat.shape[1:])
    gathered = lax.all_to_all(split, axes, split_axis=0, concat_axis=0, tiled=True)
    return jnp.sum(gathered.astype(jnp.float32), axis=0).astype(flat.dtype)


def add_partner(part, axis):
    swapped = lax.ppermute(part, axis, perm=[(0, 1), (1, 0)])
    return (part.astype(jnp.float32) + swapped.astype(jnp.float32)).astype(part.dtype)


def sum_chan(partial):
    summed = lax.psum_scatter(partial, ("xl", "core"), scatter_dimension=0, tiled=True)
    return summed[0].astype(jnp.float32)


def sum_space(partial):
    shape = partial.shape
    flat = partial.reshape(-1, shape[-1])
    rows = flat.shape[0]
    padded_rows = -(-rows // 256) * 256
    flat = jnp.pad(flat, ((0, padded_rows - rows), (0, 0)))
    if WEIGHT_PLAN == "yz":
        part = lax.psum_scatter(flat, "y", scatter_dimension=0, tiled=True)
        part = lax.psum_scatter(part, "z", scatter_dimension=0, tiled=True)
        part = lax.psum(part, "xh")
        part = lax.all_gather(part, "z", axis=0, tiled=True)
        flat = lax.all_gather(part, "y", axis=0, tiled=True)
    else:
        part = scatter_sum(flat, ("z", "y"))
        part = add_partner(part, "xh")
        flat = lax.all_gather(part, ("z", "y"), axis=0, tiled=True)
    return flat[:rows].reshape(shape)


def solution(mesh):
    space_axes = ("xh", "z", "y")
    chan_axes = ("xl", "core")
    fine = Mesh(mesh.devices.reshape(2, 4, 4, 2, 2), space_axes + chan_axes)
    tiles = P(space_axes, None, chan_axes, None)
    in_specs = (
        tiles,
        tiles,
        P(chan_axes),
        P(chan_axes),
        P(None, None, chan_axes, None),
        P(),
        P(),
        P(),
        P(),
    )
    out_specs = (tiles, P(None, None, chan_axes, None))
    inner = jax.shard_map(
        fine_local, mesh=fine, in_specs=in_specs, out_specs=out_specs, check_vma=False
    )
    out_shardings = (
        NamedSharding(mesh, P("space", None, "chan", None)),
        NamedSharding(mesh, P(None, None, "chan", None)),
    )

    def run(*args):
        outs = inner(*args)
        return tuple(lax.with_sharding_constraint(o, sh) for o, sh in zip(outs, out_shardings))

    return run


def fine_local(*args):
    return local(*args)
```

```python
import math

import jax
import jax.numpy as jnp
from jax import lax
from jax.sharding import Mesh, NamedSharding
from jax.sharding import PartitionSpec as P

GROUPS = 32


EPS = 1e-05
HIGH = lax.Precision.HIGHEST


def loss_weights(timesteps):
    phase = (timesteps.astype(jnp.float32) / 1000.0 + 0.008) / 1.008 * (math.pi / 2.0)
    alpha_bar = jnp.cos(phase) ** 2
    return jnp.minimum(1.0, 5.0 * (1.0 - alpha_bar) / alpha_bar)


def silu_slope(pre_act):
    sigma_val = jax.nn.sigmoid(pre_act)
    return sigma_val * (1.0 + pre_act * (1.0 - sigma_val))


def group_sums(values, groups):
    grouped = values.reshape(
        values.shape[:-2] + (groups, values.shape[-2] // groups, values.shape[-1])
    )
    return jnp.sum(grouped, axis=(-2, -1))


def norm_stats(sum_first, sum_second, counts):
    mean_img = sum_first / counts[:, None]
    var_img = sum_second / counts[:, None] - mean_img * mean_img
    return (mean_img, lax.rsqrt(var_img + EPS))


def shifted_views(source_field, up_ok, down_ok):
    zero_rows = jnp.zeros_like(source_field[:1])
    up_mask = up_ok.astype(source_field.dtype)[:, None, None]
    down_mask = down_ok.astype(source_field.dtype)[:, None, None]
    rows_above = jnp.concatenate([zero_rows, source_field[:-1]], axis=0) * up_mask
    rows_below = jnp.concatenate([source_field[1:], zero_rows], axis=0) * down_mask
    return [rows_above, source_field, rows_below]


def conv_views(row_views, weight):
    running = None
    for row_tap in range(3):
        source = row_views[row_tap]
        col_count = source.shape[-1]
        padded = jnp.pad(source, ((0, 0), (0, 0), (1, 1)))
        for col_tap in range(3):
            window = padded[:, :, col_tap : col_tap + col_count]
            tap_term = jnp.einsum(
                "rcw,oc->row",
                window,
                weight[row_tap, col_tap],
                preferred_element_type=jnp.float32,
            )
            running = tap_term if running is None else running + tap_term
    return running


def weight_terms(row_views, grad_field):
    col_count = grad_field.shape[-1]
    padded = jnp.pad(grad_field, ((0, 0), (0, 0), (1, 1)))
    shifted = jnp.stack(
        [padded[:, :, 2 - col_tap : 2 - col_tap + col_count] for col_tap in range(3)]
    )
    tap_rows = [
        jnp.einsum("drow,rcw->doc", shifted, source, preferred_element_type=jnp.float32)
        for source in row_views
    ]
    return jnp.stack(tap_rows)


def grad_conv(row_views, matrix):
    col_count = row_views[0].shape[-1]
    cols = []
    for source in row_views:
        padded = jnp.pad(source, ((0, 0), (0, 0), (1, 1)))
        for col_tap in range(3):
            cols.append(padded[:, :, col_tap : col_tap + col_count])
    stacked = jnp.concatenate(cols, axis=1)
    return jnp.einsum("rkw,pck->prcw", stacked, matrix, preferred_element_type=jnp.float32)


def tap_matrix(weight, parts):
    c_total, o_total = weight.shape[2], weight.shape[3]
    return jnp.transpose(weight, (2, 0, 1, 3)).reshape(parts, c_total // parts, 9 * o_total)


def local(
    latents,
    targets,
    norm_gain,
    norm_bias,
    conv_weight,
    tile_image,
    tile_owner,
    tile_slot,
    timesteps,
):
    my_index = lax.axis_index(("xh", "z", "y"))
    devices = lax.axis_size(("xh", "z", "y"))
    slots_dev, tile_rows, local_ch, col_count = latents.shape
    channels = conv_weight.shape[3]
    group_size = channels // GROUPS
    groups_here = local_ch // group_size
    image_total = timesteps.shape[0]
    tiles_dev = slots_dev // 2
    row_total = slots_dev * tile_rows
    image_ids = jnp.arange(image_total, dtype=jnp.int32)
    counts = jnp.sum(
        (tile_image.reshape(-1)[None, :] == image_ids[:, None]).astype(jnp.float32), axis=1
    ) * float(tile_rows * col_count * group_size)
    weights_img = loss_weights(timesteps)
    flipped = jnp.transpose(conv_weight[::-1, ::-1], (0, 1, 3, 2))
    gain_col = norm_gain[:, None]
    bias_col = norm_bias[:, None]
    grad_scale = 1.0 / math.sqrt(devices * tiles_dev * tile_rows * col_count)

    my_image = lax.dynamic_index_in_dim(tile_image, my_index, 0, keepdims=False)
    my_owner = lax.dynamic_index_in_dim(tile_owner, my_index, 0, keepdims=False)
    row_image = jnp.repeat(my_image, tile_rows)
    row_valid = row_image >= 0
    prev_image = jnp.concatenate([jnp.full((1,), -2, jnp.int32), row_image[:-1]])
    next_image = jnp.concatenate([row_image[1:], jnp.full((1,), -2, jnp.int32)])
    up_ok = row_valid & (prev_image == row_image)
    down_ok = row_valid & (next_image == row_image)
    onehot = (row_image[:, None] == image_ids[None, :]).astype(jnp.float32)
    valid_rows = row_valid.astype(jnp.float32)[:, None, None]

    lat_float = latents.reshape(row_total, local_ch, col_count).astype(jnp.float32)
    part_first = jnp.dot(onehot.T, group_sums(lat_float, groups_here), precision=HIGH)
    part_second = jnp.dot(onehot.T, group_sums(lat_float * lat_float, groups_here), precision=HIGH)
    mean_img, rstd_img = norm_stats(part_first, part_second, counts)
    mean_rows = jnp.repeat(jnp.dot(onehot, mean_img, precision=HIGH), group_size, axis=1)[
        :, :, None
    ]
    rstd_rows = jnp.repeat(jnp.dot(onehot, rstd_img, precision=HIGH), group_size, axis=1)[
        :, :, None
    ]
    normed = (lat_float - mean_rows) * rstd_rows
    pre_act = normed * gain_col + bias_col
    act = (jax.nn.silu(pre_act) * valid_rows).astype(jnp.bfloat16)
    act_full = gather_channels(act, ("xl", "core"))
    parts = lax.axis_size(("xl", "core"))
    act_full, matrix = lax.optimization_barrier((act_full, tap_matrix(flipped, parts)))
    act_views = shifted_views(act_full, up_ok, down_ok)
    prediction = conv_views(act_views, conv_weight)
    loss_rows = jnp.dot(onehot, weights_img, precision=HIGH)[:, None, None]
    target_float = targets.reshape(row_total, local_ch, col_count).astype(jnp.float32)
    out_grad = (loss_rows * (prediction - target_float) * valid_rows).astype(jnp.bfloat16)
    act_partial = grad_conv(shifted_views(out_grad, up_ok, down_ok), matrix)
    act_grad = sum_chan(act_partial.astype(jnp.bfloat16))
    norm_grad = act_grad * silu_slope(pre_act) * gain_col
    grad_first = jnp.dot(onehot.T, group_sums(norm_grad, groups_here), precision=HIGH)
    grad_second = jnp.dot(onehot.T, group_sums(norm_grad * normed, groups_here), precision=HIGH)
    mean_g = jnp.repeat(
        jnp.dot(onehot, grad_first / counts[:, None], precision=HIGH), group_size, axis=1
    )[:, :, None]
    mean_gn = jnp.repeat(
        jnp.dot(onehot, grad_second / counts[:, None], precision=HIGH), group_size, axis=1
    )[:, :, None]
    x_rows = (rstd_rows * (norm_grad - mean_g - normed * mean_gn) * valid_rows).astype(
        jnp.bfloat16
    )

    tile_len = tile_rows * local_ch
    x_tiles = x_rows.reshape(slots_dev, tile_len, col_count)
    x_tiles = jnp.concatenate([x_tiles, jnp.zeros_like(x_tiles[:1])], axis=0)
    dest_ids = jnp.arange(devices, dtype=jnp.int32)
    send_match = my_owner[None, :] == dest_ids[:, None]
    send_slot = jnp.where(
        jnp.any(send_match, axis=1), jnp.argmax(send_match, axis=1), slots_dev
    ).astype(jnp.int32)
    outgoing = jnp.take(x_tiles, send_slot, axis=0)
    incoming = lax.all_to_all(outgoing, ("xh", "z", "y"), split_axis=0, concat_axis=0, tiled=True)
    slot_ids = jnp.arange(tiles_dev, dtype=jnp.int32)
    hit_mask = (tile_owner[None] == my_index) & (tile_slot[None] == slot_ids[:, None, None])
    recv_src = jnp.argmax(jnp.any(hit_mask, axis=2), axis=1).astype(jnp.int32)
    x_grad = jnp.take(incoming, recv_src, axis=0)
    x_grad = x_grad.reshape(tiles_dev, tile_rows, local_ch, col_count)

    weight_sum = weight_terms(act_views, out_grad)
    weight_grad = sum_space((weight_sum * grad_scale).astype(jnp.bfloat16)).astype(jnp.float32)
    return (x_grad, weight_grad)


WEIGHT_PLAN = "joint"


def scatter_sum(flat, axes):
    parts = lax.axis_size(axes)
    split = flat.reshape((parts, flat.shape[0] // parts) + flat.shape[1:])
    gathered = lax.all_to_all(split, axes, split_axis=0, concat_axis=0, tiled=True)
    return jnp.sum(gathered.astype(jnp.float32), axis=0).astype(flat.dtype)


def gather_channels(act, axes):
    parts = lax.axis_size(axes)
    copies = jnp.broadcast_to(act[None], (parts,) + act.shape)
    gathered = lax.all_to_all(copies, axes, split_axis=0, concat_axis=0, tiled=True)
    rows, channels, cols = act.shape
    return jnp.transpose(gathered, (1, 0, 2, 3)).reshape(rows, parts * channels, cols)


def add_partner(part, axis):
    swapped = lax.ppermute(part, axis, perm=[(0, 1), (1, 0)])
    return (part.astype(jnp.float32) + swapped.astype(jnp.float32)).astype(part.dtype)


def sum_chan(partial):
    summed = lax.psum_scatter(partial, ("xl", "core"), scatter_dimension=0, tiled=True)
    return summed[0].astype(jnp.float32)


def sum_space(partial):
    shape = partial.shape
    flat = partial.reshape(-1, shape[-1])
    rows = flat.shape[0]
    padded_rows = -(-rows // 256) * 256
    flat = jnp.pad(flat, ((0, padded_rows - rows), (0, 0)))
    if WEIGHT_PLAN == "yz":
        part = lax.psum_scatter(flat, "y", scatter_dimension=0, tiled=True)
        part = lax.psum_scatter(part, "z", scatter_dimension=0, tiled=True)
        part = lax.psum(part, "xh")
        part = lax.all_gather(part, "z", axis=0, tiled=True)
        flat = lax.all_gather(part, "y", axis=0, tiled=True)
    else:
        part = scatter_sum(flat, ("z", "y"))
        part = add_partner(part, "xh")
        flat = lax.all_gather(part, ("z", "y"), axis=0, tiled=True)
    return flat[:rows].reshape(shape)


def solution(mesh):
    space_axes = ("xh", "z", "y")
    chan_axes = ("xl", "core")
    fine = Mesh(mesh.devices.reshape(2, 4, 4, 2, 2), space_axes + chan_axes)
    tiles = P(space_axes, None, chan_axes, None)
    in_specs = (
        tiles,
        tiles,
        P(chan_axes),
        P(chan_axes),
        P(None, None, chan_axes, None),
        P(),
        P(),
        P(),
        P(),
    )
    out_specs = (tiles, P(None, None, chan_axes, None))
    inner = jax.shard_map(
        fine_local, mesh=fine, in_specs=in_specs, out_specs=out_specs, check_vma=False
    )
    out_shardings = (
        NamedSharding(mesh, P("space", None, "chan", None)),
        NamedSharding(mesh, P(None, None, "chan", None)),
    )

    def run(*args):
        outs = inner(*args)
        return tuple(lax.with_sharding_constraint(o, sh) for o, sh in zip(outs, out_shardings))

    return run


def fine_local(*args):
    return local(*args)
```

```python
import math

import jax
import jax.numpy as jnp
from jax import lax
from jax.sharding import Mesh, NamedSharding
from jax.sharding import PartitionSpec as P

GROUPS = 32


EPS = 1e-05
HIGH = lax.Precision.HIGHEST


def loss_weights(timesteps):
    phase = (timesteps.astype(jnp.float32) / 1000.0 + 0.008) / 1.008 * (math.pi / 2.0)
    alpha_bar = jnp.cos(phase) ** 2
    return jnp.minimum(1.0, 5.0 * (1.0 - alpha_bar) / alpha_bar)


def silu_slope(pre_act):
    sigma_val = jax.nn.sigmoid(pre_act)
    return sigma_val * (1.0 + pre_act * (1.0 - sigma_val))


def group_sums(values, groups):
    grouped = values.reshape(
        values.shape[:-2] + (groups, values.shape[-2] // groups, values.shape[-1])
    )
    return jnp.sum(grouped, axis=(-2, -1))


def norm_stats(sum_first, sum_second, counts):
    mean_img = sum_first / counts[:, None]
    var_img = sum_second / counts[:, None] - mean_img * mean_img
    return (mean_img, lax.rsqrt(var_img + EPS))


def shifted_views(source_field, up_ok, down_ok):
    zero_rows = jnp.zeros_like(source_field[:1])
    up_mask = up_ok.astype(source_field.dtype)[:, None, None]
    down_mask = down_ok.astype(source_field.dtype)[:, None, None]
    rows_above = jnp.concatenate([zero_rows, source_field[:-1]], axis=0) * up_mask
    rows_below = jnp.concatenate([source_field[1:], zero_rows], axis=0) * down_mask
    return [rows_above, source_field, rows_below]


def conv_views(row_views, weight):
    running = None
    for row_tap in range(3):
        source = row_views[row_tap]
        col_count = source.shape[-1]
        padded = jnp.pad(source, ((0, 0), (0, 0), (1, 1)))
        for col_tap in range(3):
            window = padded[:, :, col_tap : col_tap + col_count]
            tap_term = jnp.einsum(
                "rcw,oc->row",
                window,
                weight[row_tap, col_tap],
                preferred_element_type=jnp.float32,
            )
            running = tap_term if running is None else running + tap_term
    return running


def weight_terms(row_views, grad_field):
    col_count = grad_field.shape[-1]
    padded = jnp.pad(grad_field, ((0, 0), (0, 0), (1, 1)))
    shifted = jnp.stack(
        [padded[:, :, 2 - col_tap : 2 - col_tap + col_count] for col_tap in range(3)]
    )
    tap_rows = [
        jnp.einsum("drow,rcw->doc", shifted, source, preferred_element_type=jnp.float32)
        for source in row_views
    ]
    return jnp.stack(tap_rows)


def grad_conv(row_views, matrix):
    col_count = row_views[0].shape[-1]
    cols = []
    for source in row_views:
        padded = jnp.pad(source, ((0, 0), (0, 0), (1, 1)))
        for col_tap in range(3):
            cols.append(padded[:, :, col_tap : col_tap + col_count])
    stacked = jnp.concatenate(cols, axis=1)
    return jnp.einsum("rkw,pck->prcw", stacked, matrix, preferred_element_type=jnp.float32)


def tap_matrix(weight, parts):
    c_total, o_total = weight.shape[2], weight.shape[3]
    return jnp.transpose(weight, (2, 0, 1, 3)).reshape(parts, c_total // parts, 9 * o_total)


def local(
    latents,
    targets,
    norm_gain,
    norm_bias,
    conv_weight,
    tile_image,
    tile_owner,
    tile_slot,
    timesteps,
):
    my_index = lax.axis_index(("xh", "z", "y"))
    devices = lax.axis_size(("xh", "z", "y"))
    slots_dev, tile_rows, local_ch, col_count = latents.shape
    channels = conv_weight.shape[3]
    group_size = channels // GROUPS
    groups_here = local_ch // group_size
    image_total = timesteps.shape[0]
    tiles_dev = slots_dev // 2
    row_total = slots_dev * tile_rows
    image_ids = jnp.arange(image_total, dtype=jnp.int32)
    counts = jnp.sum(
        (tile_image.reshape(-1)[None, :] == image_ids[:, None]).astype(jnp.float32), axis=1
    ) * float(tile_rows * col_count * group_size)
    weights_img = loss_weights(timesteps)
    flipped = jnp.transpose(conv_weight[::-1, ::-1], (0, 1, 3, 2))
    gain_col = norm_gain[:, None]
    bias_col = norm_bias[:, None]
    grad_scale = 1.0 / math.sqrt(devices * tiles_dev * tile_rows * col_count)

    my_image = lax.dynamic_index_in_dim(tile_image, my_index, 0, keepdims=False)
    my_owner = lax.dynamic_index_in_dim(tile_owner, my_index, 0, keepdims=False)
    row_image = jnp.repeat(my_image, tile_rows)
    row_valid = row_image >= 0
    prev_image = jnp.concatenate([jnp.full((1,), -2, jnp.int32), row_image[:-1]])
    next_image = jnp.concatenate([row_image[1:], jnp.full((1,), -2, jnp.int32)])
    up_ok = row_valid & (prev_image == row_image)
    down_ok = row_valid & (next_image == row_image)
    onehot = (row_image[:, None] == image_ids[None, :]).astype(jnp.float32)
    valid_rows = row_valid.astype(jnp.float32)[:, None, None]

    lat_float = latents.reshape(row_total, local_ch, col_count).astype(jnp.float32)
    part_first = jnp.dot(onehot.T, group_sums(lat_float, groups_here), precision=HIGH)
    part_second = jnp.dot(onehot.T, group_sums(lat_float * lat_float, groups_here), precision=HIGH)
    mean_img, rstd_img = norm_stats(part_first, part_second, counts)
    mean_rows = jnp.repeat(jnp.dot(onehot, mean_img, precision=HIGH), group_size, axis=1)[
        :, :, None
    ]
    rstd_rows = jnp.repeat(jnp.dot(onehot, rstd_img, precision=HIGH), group_size, axis=1)[
        :, :, None
    ]
    normed = (lat_float - mean_rows) * rstd_rows
    pre_act = normed * gain_col + bias_col
    act = (jax.nn.silu(pre_act) * valid_rows).astype(jnp.bfloat16)
    act_full = lax.all_gather(act, ("xl", "core"), axis=1, tiled=True)
    parts = lax.axis_size(("xl", "core"))
    act_full, matrix = lax.optimization_barrier((act_full, tap_matrix(flipped, parts)))
    act_views = shifted_views(act_full, up_ok, down_ok)
    prediction = conv_views(act_views, conv_weight)
    loss_rows = jnp.dot(onehot, weights_img, precision=HIGH)[:, None, None]
    target_float = targets.reshape(row_total, local_ch, col_count).astype(jnp.float32)
    out_grad = (loss_rows * (prediction - target_float) * valid_rows).astype(jnp.bfloat16)
    act_partial = grad_conv(shifted_views(out_grad, up_ok, down_ok), matrix)
    act_grad = sum_chan(act_partial.astype(jnp.bfloat16))
    norm_grad = act_grad * silu_slope(pre_act) * gain_col
    grad_first = jnp.dot(onehot.T, group_sums(norm_grad, groups_here), precision=HIGH)
    grad_second = jnp.dot(onehot.T, group_sums(norm_grad * normed, groups_here), precision=HIGH)
    mean_g = jnp.repeat(
        jnp.dot(onehot, grad_first / counts[:, None], precision=HIGH), group_size, axis=1
    )[:, :, None]
    mean_gn = jnp.repeat(
        jnp.dot(onehot, grad_second / counts[:, None], precision=HIGH), group_size, axis=1
    )[:, :, None]
    x_rows = (rstd_rows * (norm_grad - mean_g - normed * mean_gn) * valid_rows).astype(
        jnp.bfloat16
    )

    tile_len = tile_rows * local_ch
    x_tiles = x_rows.reshape(slots_dev, tile_len, col_count)
    x_tiles = jnp.concatenate([x_tiles, jnp.zeros_like(x_tiles[:1])], axis=0)
    dest_ids = jnp.arange(devices, dtype=jnp.int32)
    send_match = my_owner[None, :] == dest_ids[:, None]
    send_slot = jnp.where(
        jnp.any(send_match, axis=1), jnp.argmax(send_match, axis=1), slots_dev
    ).astype(jnp.int32)
    outgoing = jnp.take(x_tiles, send_slot, axis=0)
    incoming = lax.all_to_all(outgoing, ("xh", "z", "y"), split_axis=0, concat_axis=0, tiled=True)
    slot_ids = jnp.arange(tiles_dev, dtype=jnp.int32)
    hit_mask = (tile_owner[None] == my_index) & (tile_slot[None] == slot_ids[:, None, None])
    recv_src = jnp.argmax(jnp.any(hit_mask, axis=2), axis=1).astype(jnp.int32)
    x_grad = jnp.take(incoming, recv_src, axis=0)
    x_grad = x_grad.reshape(tiles_dev, tile_rows, local_ch, col_count)

    weight_sum = weight_terms(act_views, out_grad)
    weight_grad = sum_space((weight_sum * grad_scale).astype(jnp.bfloat16)).astype(jnp.float32)
    return (x_grad, weight_grad)


WEIGHT_PLAN = "joint"


def scatter_sum(flat, axes):
    parts = lax.axis_size(axes)
    split = flat.reshape((parts, flat.shape[0] // parts) + flat.shape[1:])
    gathered = lax.all_to_all(split, axes, split_axis=0, concat_axis=0, tiled=True)
    return jnp.sum(gathered.astype(jnp.float32), axis=0).astype(flat.dtype)


def add_partner(part, axis):
    swapped = lax.ppermute(part, axis, perm=[(0, 1), (1, 0)])
    return (part.astype(jnp.float32) + swapped.astype(jnp.float32)).astype(part.dtype)


def sum_chan(partial):
    summed = lax.psum_scatter(partial, ("xl", "core"), scatter_dimension=0, tiled=True)
    return summed[0].astype(jnp.float32)


def sum_space(partial):
    shape = partial.shape
    flat = partial.reshape(-1, shape[-1])
    rows = flat.shape[0]
    padded_rows = -(-rows // 256) * 256
    flat = jnp.pad(flat, ((0, padded_rows - rows), (0, 0)))
    if WEIGHT_PLAN == "yz":
        part = lax.psum_scatter(flat, "y", scatter_dimension=0, tiled=True)
        part = lax.psum_scatter(part, "z", scatter_dimension=0, tiled=True)
        part = lax.psum(part, "xh")
        part = lax.all_gather(part, "z", axis=0, tiled=True)
        flat = lax.all_gather(part, "y", axis=0, tiled=True)
    else:
        part = scatter_sum(flat, ("z", "y"))
        part = add_partner(part, "xh")
        part = lax.all_gather(part, "y", axis=0, tiled=True)
        flat = lax.all_gather(part, "z", axis=0, tiled=True)
    return flat[:rows].reshape(shape)


def solution(mesh):
    space_axes = ("xh", "z", "y")
    chan_axes = ("xl", "core")
    fine = Mesh(mesh.devices.reshape(2, 4, 4, 2, 2), space_axes + chan_axes)
    tiles = P(space_axes, None, chan_axes, None)
    in_specs = (
        tiles,
        tiles,
        P(chan_axes),
        P(chan_axes),
        P(None, None, chan_axes, None),
        P(),
        P(),
        P(),
        P(),
    )
    out_specs = (tiles, P(None, None, chan_axes, None))
    inner = jax.shard_map(
        fine_local, mesh=fine, in_specs=in_specs, out_specs=out_specs, check_vma=False
    )
    out_shardings = (
        NamedSharding(mesh, P("space", None, "chan", None)),
        NamedSharding(mesh, P(None, None, "chan", None)),
    )

    def run(*args):
        outs = inner(*args)
        return tuple(lax.with_sharding_constraint(o, sh) for o, sh in zip(outs, out_shardings))

    return run


def fine_local(*args):
    return local(*args)
```

```python
import math

import jax
import jax.numpy as jnp
from jax import lax
from jax.sharding import Mesh, NamedSharding
from jax.sharding import PartitionSpec as P

GROUPS = 32


EPS = 1e-05
HIGH = lax.Precision.HIGHEST


def loss_weights(timesteps):
    phase = (timesteps.astype(jnp.float32) / 1000.0 + 0.008) / 1.008 * (math.pi / 2.0)
    alpha_bar = jnp.cos(phase) ** 2
    return jnp.minimum(1.0, 5.0 * (1.0 - alpha_bar) / alpha_bar)


def silu_slope(pre_act):
    sigma_val = jax.nn.sigmoid(pre_act)
    return sigma_val * (1.0 + pre_act * (1.0 - sigma_val))


def group_sums(values, groups):
    grouped = values.reshape(
        values.shape[:-2] + (groups, values.shape[-2] // groups, values.shape[-1])
    )
    return jnp.sum(grouped, axis=(-2, -1))


def norm_stats(sum_first, sum_second, counts):
    mean_img = sum_first / counts[:, None]
    var_img = sum_second / counts[:, None] - mean_img * mean_img
    return (mean_img, lax.rsqrt(var_img + EPS))


def shifted_views(source_field, up_ok, down_ok):
    zero_rows = jnp.zeros_like(source_field[:1])
    up_mask = up_ok.astype(source_field.dtype)[:, None, None]
    down_mask = down_ok.astype(source_field.dtype)[:, None, None]
    rows_above = jnp.concatenate([zero_rows, source_field[:-1]], axis=0) * up_mask
    rows_below = jnp.concatenate([source_field[1:], zero_rows], axis=0) * down_mask
    return [rows_above, source_field, rows_below]


def conv_views(row_views, weight):
    running = None
    for row_tap in range(3):
        source = row_views[row_tap]
        col_count = source.shape[-1]
        padded = jnp.pad(source, ((0, 0), (0, 0), (1, 1)))
        for col_tap in range(3):
            window = padded[:, :, col_tap : col_tap + col_count]
            tap_term = jnp.einsum(
                "rcw,oc->row",
                window,
                weight[row_tap, col_tap],
                preferred_element_type=jnp.float32,
            )
            running = tap_term if running is None else running + tap_term
    return running


def weight_terms(row_views, grad_field):
    col_count = grad_field.shape[-1]
    padded = jnp.pad(grad_field, ((0, 0), (0, 0), (1, 1)))
    shifted = jnp.stack(
        [padded[:, :, 2 - col_tap : 2 - col_tap + col_count] for col_tap in range(3)]
    )
    tap_rows = [
        jnp.einsum("drow,rcw->doc", shifted, source, preferred_element_type=jnp.float32)
        for source in row_views
    ]
    return jnp.stack(tap_rows)


def grad_conv(row_views, matrix):
    col_count = row_views[0].shape[-1]
    cols = []
    for source in row_views:
        padded = jnp.pad(source, ((0, 0), (0, 0), (1, 1)))
        for col_tap in range(3):
            cols.append(padded[:, :, col_tap : col_tap + col_count])
    stacked = jnp.concatenate(cols, axis=1)
    return jnp.einsum("rkw,pck->prcw", stacked, matrix, preferred_element_type=jnp.float32)


def tap_matrix(weight, parts):
    c_total, o_total = weight.shape[2], weight.shape[3]
    return jnp.transpose(weight, (2, 0, 1, 3)).reshape(parts, c_total // parts, 9 * o_total)


def local(
    latents,
    targets,
    norm_gain,
    norm_bias,
    conv_weight,
    tile_image,
    tile_owner,
    tile_slot,
    timesteps,
):
    my_index = lax.axis_index(("xh", "z", "y"))
    devices = lax.axis_size(("xh", "z", "y"))
    slots_dev, tile_rows, local_ch, col_count = latents.shape
    channels = conv_weight.shape[3]
    group_size = channels // GROUPS
    groups_here = local_ch // group_size
    image_total = timesteps.shape[0]
    tiles_dev = slots_dev // 2
    row_total = slots_dev * tile_rows
    image_ids = jnp.arange(image_total, dtype=jnp.int32)
    counts = jnp.sum(
        (tile_image.reshape(-1)[None, :] == image_ids[:, None]).astype(jnp.float32), axis=1
    ) * float(tile_rows * col_count * group_size)
    weights_img = loss_weights(timesteps)
    flipped = jnp.transpose(conv_weight[::-1, ::-1], (0, 1, 3, 2))
    gain_col = norm_gain[:, None]
    bias_col = norm_bias[:, None]
    grad_scale = 1.0 / math.sqrt(devices * tiles_dev * tile_rows * col_count)

    my_image = lax.dynamic_index_in_dim(tile_image, my_index, 0, keepdims=False)
    my_owner = lax.dynamic_index_in_dim(tile_owner, my_index, 0, keepdims=False)
    row_image = jnp.repeat(my_image, tile_rows)
    row_valid = row_image >= 0
    prev_image = jnp.concatenate([jnp.full((1,), -2, jnp.int32), row_image[:-1]])
    next_image = jnp.concatenate([row_image[1:], jnp.full((1,), -2, jnp.int32)])
    up_ok = row_valid & (prev_image == row_image)
    down_ok = row_valid & (next_image == row_image)
    onehot = (row_image[:, None] == image_ids[None, :]).astype(jnp.float32)
    valid_rows = row_valid.astype(jnp.float32)[:, None, None]

    lat_float = latents.reshape(row_total, local_ch, col_count).astype(jnp.float32)
    part_first = jnp.dot(onehot.T, group_sums(lat_float, groups_here), precision=HIGH)
    part_second = jnp.dot(onehot.T, group_sums(lat_float * lat_float, groups_here), precision=HIGH)
    mean_img, rstd_img = norm_stats(part_first, part_second, counts)
    mean_rows = jnp.repeat(jnp.dot(onehot, mean_img, precision=HIGH), group_size, axis=1)[
        :, :, None
    ]
    rstd_rows = jnp.repeat(jnp.dot(onehot, rstd_img, precision=HIGH), group_size, axis=1)[
        :, :, None
    ]
    normed = (lat_float - mean_rows) * rstd_rows
    pre_act = normed * gain_col + bias_col
    act = (jax.nn.silu(pre_act) * valid_rows).astype(jnp.bfloat16)
    act_full = lax.all_gather(act, ("xl", "core"), axis=1, tiled=True)
    parts = lax.axis_size(("xl", "core"))
    act_full, matrix = lax.optimization_barrier((act_full, tap_matrix(flipped, parts)))
    act_views = shifted_views(act_full, up_ok, down_ok)
    prediction = conv_views(act_views, conv_weight)
    loss_rows = jnp.dot(onehot, weights_img, precision=HIGH)[:, None, None]
    target_float = targets.reshape(row_total, local_ch, col_count).astype(jnp.float32)
    out_grad = (loss_rows * (prediction - target_float) * valid_rows).astype(jnp.bfloat16)
    act_partial = grad_conv(shifted_views(out_grad, up_ok, down_ok), matrix)
    act_grad = sum_chan(act_partial.astype(jnp.bfloat16))
    norm_grad = act_grad * silu_slope(pre_act) * gain_col
    grad_first = jnp.dot(onehot.T, group_sums(norm_grad, groups_here), precision=HIGH)
    grad_second = jnp.dot(onehot.T, group_sums(norm_grad * normed, groups_here), precision=HIGH)
    mean_g = jnp.repeat(
        jnp.dot(onehot, grad_first / counts[:, None], precision=HIGH), group_size, axis=1
    )[:, :, None]
    mean_gn = jnp.repeat(
        jnp.dot(onehot, grad_second / counts[:, None], precision=HIGH), group_size, axis=1
    )[:, :, None]
    x_rows = (rstd_rows * (norm_grad - mean_g - normed * mean_gn) * valid_rows).astype(
        jnp.bfloat16
    )

    tile_len = tile_rows * local_ch
    x_tiles = x_rows.reshape(slots_dev, tile_len, col_count)
    x_tiles = jnp.concatenate([x_tiles, jnp.zeros_like(x_tiles[:1])], axis=0)
    dest_ids = jnp.arange(devices, dtype=jnp.int32)
    send_match = my_owner[None, :] == dest_ids[:, None]
    send_slot = jnp.where(
        jnp.any(send_match, axis=1), jnp.argmax(send_match, axis=1), slots_dev
    ).astype(jnp.int32)
    outgoing = jnp.take(x_tiles, send_slot, axis=0)
    incoming = lax.all_to_all(outgoing, ("xh", "z", "y"), split_axis=0, concat_axis=0, tiled=True)
    slot_ids = jnp.arange(tiles_dev, dtype=jnp.int32)
    hit_mask = (tile_owner[None] == my_index) & (tile_slot[None] == slot_ids[:, None, None])
    recv_src = jnp.argmax(jnp.any(hit_mask, axis=2), axis=1).astype(jnp.int32)
    x_grad = jnp.take(incoming, recv_src, axis=0)
    x_grad = x_grad.reshape(tiles_dev, tile_rows, local_ch, col_count)

    weight_sum = weight_terms(act_views, out_grad)
    weight_grad = sum_space((weight_sum * grad_scale).astype(jnp.bfloat16)).astype(jnp.float32)
    return (x_grad, weight_grad)


WEIGHT_PLAN = "joint"


def scatter_sum(flat, axes):
    parts = lax.axis_size(axes)
    split = flat.reshape((parts, flat.shape[0] // parts) + flat.shape[1:])
    gathered = lax.all_to_all(split, axes, split_axis=0, concat_axis=0, tiled=True)
    return jnp.sum(gathered.astype(jnp.float32), axis=0).astype(flat.dtype)


def add_partner(part, axis):
    swapped = lax.ppermute(part, axis, perm=[(0, 1), (1, 0)])
    return (part.astype(jnp.float32) + swapped.astype(jnp.float32)).astype(part.dtype)


def sum_chan(partial):
    summed = lax.psum_scatter(partial, ("xl", "core"), scatter_dimension=0, tiled=True)
    return summed[0].astype(jnp.float32)


def sum_space(partial):
    shape = partial.shape
    flat = partial.reshape(-1, shape[-1])
    rows = flat.shape[0]
    padded_rows = -(-rows // 16) * 16
    flat = jnp.pad(flat, ((0, padded_rows - rows), (0, 0)))
    if WEIGHT_PLAN == "yz":
        part = lax.psum_scatter(flat, "y", scatter_dimension=0, tiled=True)
        part = lax.psum_scatter(part, "z", scatter_dimension=0, tiled=True)
        part = lax.psum(part, "xh")
        part = lax.all_gather(part, "z", axis=0, tiled=True)
        flat = lax.all_gather(part, "y", axis=0, tiled=True)
    else:
        part = scatter_sum(flat, ("z", "y"))
        part = add_partner(part, "xh")
        flat = lax.all_gather(part, ("z", "y"), axis=0, tiled=True)
    return flat[:rows].reshape(shape)


def solution(mesh):
    space_axes = ("xh", "z", "y")
    chan_axes = ("xl", "core")
    fine = Mesh(mesh.devices.reshape(2, 4, 4, 2, 2), space_axes + chan_axes)
    tiles = P(space_axes, None, chan_axes, None)
    in_specs = (
        tiles,
        tiles,
        P(chan_axes),
        P(chan_axes),
        P(None, None, chan_axes, None),
        P(),
        P(),
        P(),
        P(),
    )
    out_specs = (tiles, P(None, None, chan_axes, None))
    inner = jax.shard_map(
        fine_local, mesh=fine, in_specs=in_specs, out_specs=out_specs, check_vma=False
    )
    out_shardings = (
        NamedSharding(mesh, P("space", None, "chan", None)),
        NamedSharding(mesh, P(None, None, "chan", None)),
    )

    def run(*args):
        outs = inner(*args)
        return tuple(lax.with_sharding_constraint(o, sh) for o, sh in zip(outs, out_shardings))

    return run


def fine_local(*args):
    return local(*args)
```

```python
import math

import jax
import jax.numpy as jnp
from jax import lax
from jax.sharding import Mesh, NamedSharding
from jax.sharding import PartitionSpec as P

GROUPS = 32


EPS = 1e-05
HIGH = lax.Precision.HIGHEST


def loss_weights(timesteps):
    phase = (timesteps.astype(jnp.float32) / 1000.0 + 0.008) / 1.008 * (math.pi / 2.0)
    alpha_bar = jnp.cos(phase) ** 2
    return jnp.minimum(1.0, 5.0 * (1.0 - alpha_bar) / alpha_bar)


def silu_slope(pre_act):
    sigma_val = jax.nn.sigmoid(pre_act)
    return sigma_val * (1.0 + pre_act * (1.0 - sigma_val))


def group_sums(values, groups):
    grouped = values.reshape(
        values.shape[:-2] + (groups, values.shape[-2] // groups, values.shape[-1])
    )
    return jnp.sum(grouped, axis=(-2, -1))


def norm_stats(sum_first, sum_second, counts):
    mean_img = sum_first / counts[:, None]
    var_img = sum_second / counts[:, None] - mean_img * mean_img
    return (mean_img, lax.rsqrt(var_img + EPS))


def shifted_views(source_field, up_ok, down_ok):
    zero_rows = jnp.zeros_like(source_field[:1])
    up_mask = up_ok.astype(source_field.dtype)[:, None, None]
    down_mask = down_ok.astype(source_field.dtype)[:, None, None]
    rows_above = jnp.concatenate([zero_rows, source_field[:-1]], axis=0) * up_mask
    rows_below = jnp.concatenate([source_field[1:], zero_rows], axis=0) * down_mask
    return [rows_above, source_field, rows_below]


def conv_views(row_views, weight):
    running = None
    for row_tap in range(3):
        source = row_views[row_tap]
        col_count = source.shape[-1]
        padded = jnp.pad(source, ((0, 0), (0, 0), (1, 1)))
        for col_tap in range(3):
            window = padded[:, :, col_tap : col_tap + col_count]
            tap_term = jnp.einsum(
                "rcw,oc->row",
                window,
                weight[row_tap, col_tap],
                preferred_element_type=jnp.float32,
            )
            running = tap_term if running is None else running + tap_term
    return running


def weight_terms(row_views, grad_field):
    col_count = grad_field.shape[-1]
    padded = jnp.pad(grad_field, ((0, 0), (0, 0), (1, 1)))
    shifted = jnp.stack(
        [padded[:, :, 2 - col_tap : 2 - col_tap + col_count] for col_tap in range(3)]
    )
    tap_rows = [
        jnp.einsum("drow,rcw->doc", shifted, source, preferred_element_type=jnp.float32)
        for source in row_views
    ]
    return jnp.stack(tap_rows)


def grad_conv(row_views, matrix):
    col_count = row_views[0].shape[-1]
    cols = []
    for source in row_views:
        padded = jnp.pad(source, ((0, 0), (0, 0), (1, 1)))
        for col_tap in range(3):
            cols.append(padded[:, :, col_tap : col_tap + col_count])
    stacked = jnp.concatenate(cols, axis=1)
    return jnp.einsum("rkw,pck->prcw", stacked, matrix, preferred_element_type=jnp.float32)


def tap_matrix(weight, parts):
    c_total, o_total = weight.shape[2], weight.shape[3]
    return jnp.transpose(weight, (2, 0, 1, 3)).reshape(parts, c_total // parts, 9 * o_total)


def local(
    latents,
    targets,
    norm_gain,
    norm_bias,
    conv_weight,
    tile_image,
    tile_owner,
    tile_slot,
    timesteps,
):
    my_index = lax.axis_index(("xh", "z", "y"))
    devices = lax.axis_size(("xh", "z", "y"))
    slots_dev, tile_rows, local_ch, col_count = latents.shape
    channels = conv_weight.shape[3]
    group_size = channels // GROUPS
    groups_here = local_ch // group_size
    image_total = timesteps.shape[0]
    tiles_dev = slots_dev // 2
    row_total = slots_dev * tile_rows
    image_ids = jnp.arange(image_total, dtype=jnp.int32)
    counts = jnp.sum(
        (tile_image.reshape(-1)[None, :] == image_ids[:, None]).astype(jnp.float32), axis=1
    ) * float(tile_rows * col_count * group_size)
    weights_img = loss_weights(timesteps)
    flipped = jnp.transpose(conv_weight[::-1, ::-1], (0, 1, 3, 2))
    gain_col = norm_gain[:, None]
    bias_col = norm_bias[:, None]
    grad_scale = 1.0 / math.sqrt(devices * tiles_dev * tile_rows * col_count)

    my_image = lax.dynamic_index_in_dim(tile_image, my_index, 0, keepdims=False)
    my_owner = lax.dynamic_index_in_dim(tile_owner, my_index, 0, keepdims=False)
    row_image = jnp.repeat(my_image, tile_rows)
    row_valid = row_image >= 0
    prev_image = jnp.concatenate([jnp.full((1,), -2, jnp.int32), row_image[:-1]])
    next_image = jnp.concatenate([row_image[1:], jnp.full((1,), -2, jnp.int32)])
    up_ok = row_valid & (prev_image == row_image)
    down_ok = row_valid & (next_image == row_image)
    onehot = (row_image[:, None] == image_ids[None, :]).astype(jnp.float32)
    valid_rows = row_valid.astype(jnp.float32)[:, None, None]

    lat_float = latents.reshape(row_total, local_ch, col_count).astype(jnp.float32)
    part_first = jnp.dot(onehot.T, group_sums(lat_float, groups_here), precision=HIGH)
    part_second = jnp.dot(onehot.T, group_sums(lat_float * lat_float, groups_here), precision=HIGH)
    mean_img, rstd_img = norm_stats(part_first, part_second, counts)
    mean_rows = jnp.repeat(jnp.dot(onehot, mean_img, precision=HIGH), group_size, axis=1)[
        :, :, None
    ]
    rstd_rows = jnp.repeat(jnp.dot(onehot, rstd_img, precision=HIGH), group_size, axis=1)[
        :, :, None
    ]
    normed = (lat_float - mean_rows) * rstd_rows
    pre_act = normed * gain_col + bias_col
    act = (jax.nn.silu(pre_act) * valid_rows).astype(jnp.bfloat16)
    act_full = lax.all_gather(act, ("xl", "core"), axis=1, tiled=True)
    parts = lax.axis_size(("xl", "core"))
    act_full, matrix = lax.optimization_barrier((act_full, tap_matrix(flipped, parts)))
    act_views = shifted_views(act_full, up_ok, down_ok)
    prediction = conv_views(act_views, conv_weight)
    loss_rows = jnp.dot(onehot, weights_img, precision=HIGH)[:, None, None]
    target_float = targets.reshape(row_total, local_ch, col_count).astype(jnp.float32)
    out_grad = (loss_rows * (prediction - target_float) * valid_rows).astype(jnp.bfloat16)
    act_partial = grad_conv(shifted_views(out_grad, up_ok, down_ok), matrix)
    act_grad = sum_chan(act_partial.astype(jnp.bfloat16))
    norm_grad = act_grad * silu_slope(pre_act) * gain_col
    grad_first = jnp.dot(onehot.T, group_sums(norm_grad, groups_here), precision=HIGH)
    grad_second = jnp.dot(onehot.T, group_sums(norm_grad * normed, groups_here), precision=HIGH)
    mean_g = jnp.repeat(
        jnp.dot(onehot, grad_first / counts[:, None], precision=HIGH), group_size, axis=1
    )[:, :, None]
    mean_gn = jnp.repeat(
        jnp.dot(onehot, grad_second / counts[:, None], precision=HIGH), group_size, axis=1
    )[:, :, None]
    x_rows = (rstd_rows * (norm_grad - mean_g - normed * mean_gn) * valid_rows).astype(
        jnp.bfloat16
    )

    tile_len = tile_rows * local_ch
    x_tiles = x_rows.reshape(slots_dev, tile_len, col_count)
    x_tiles = jnp.concatenate([x_tiles, jnp.zeros_like(x_tiles[:1])], axis=0)
    dest_ids = jnp.arange(devices, dtype=jnp.int32)
    send_match = my_owner[None, :] == dest_ids[:, None]
    send_slot = jnp.where(
        jnp.any(send_match, axis=1), jnp.argmax(send_match, axis=1), slots_dev
    ).astype(jnp.int32)
    outgoing = jnp.take(x_tiles, send_slot, axis=0)
    incoming = lax.all_to_all(outgoing, ("xh", "z", "y"), split_axis=0, concat_axis=0, tiled=True)
    slot_ids = jnp.arange(tiles_dev, dtype=jnp.int32)
    hit_mask = (tile_owner[None] == my_index) & (tile_slot[None] == slot_ids[:, None, None])
    recv_src = jnp.argmax(jnp.any(hit_mask, axis=2), axis=1).astype(jnp.int32)
    x_grad = jnp.take(incoming, recv_src, axis=0)
    x_grad = x_grad.reshape(tiles_dev, tile_rows, local_ch, col_count)

    weight_sum = weight_terms(act_views, out_grad)
    weight_grad = sum_space((weight_sum * grad_scale).astype(jnp.bfloat16)).astype(jnp.float32)
    return (x_grad, weight_grad)


WEIGHT_PLAN = "joint"


def scatter_sum(flat, axes):
    parts = lax.axis_size(axes)
    split = flat.reshape((parts, flat.shape[0] // parts) + flat.shape[1:])
    gathered = lax.all_to_all(split, axes, split_axis=0, concat_axis=0, tiled=True)
    return jnp.sum(gathered.astype(jnp.float32), axis=0).astype(flat.dtype)


def add_partner(part, axis):
    swapped = lax.ppermute(part, axis, perm=[(0, 1), (1, 0)])
    return (part.astype(jnp.float32) + swapped.astype(jnp.float32)).astype(part.dtype)


def sum_chan(partial):
    summed = lax.psum_scatter(partial, ("xl", "core"), scatter_dimension=0, tiled=True)
    return summed[0].astype(jnp.float32)


def sum_space(partial):
    shape = partial.shape
    flat = partial.reshape(-1, shape[-1])
    rows = flat.shape[0]
    padded_rows = -(-rows // 32) * 32
    flat = jnp.pad(flat, ((0, padded_rows - rows), (0, 0)))
    if WEIGHT_PLAN == "yz":
        part = lax.psum_scatter(flat, "y", scatter_dimension=0, tiled=True)
        part = lax.psum_scatter(part, "z", scatter_dimension=0, tiled=True)
        part = lax.psum(part, "xh")
        part = lax.all_gather(part, "z", axis=0, tiled=True)
        flat = lax.all_gather(part, "y", axis=0, tiled=True)
    else:
        part = scatter_sum(flat, ("z", "y"))
        part = add_partner(part, "xh")
        side = lax.axis_index("xh")
        halves = part.reshape((2, part.shape[0] // 2) + part.shape[1:])
        mine = lax.dynamic_index_in_dim(halves, side, 0, keepdims=False)
        gathered = lax.all_gather(mine, ("z", "y"), axis=0, tiled=False)
        theirs = lax.ppermute(gathered, "xh", perm=[(0, 1), (1, 0)])
        first = jnp.where(side == 0, gathered, theirs)
        second = jnp.where(side == 0, theirs, gathered)
        flat = jnp.stack([first, second], axis=1).reshape(flat.shape)
    return flat[:rows].reshape(shape)


def solution(mesh):
    space_axes = ("xh", "z", "y")
    chan_axes = ("xl", "core")
    fine = Mesh(mesh.devices.reshape(2, 4, 4, 2, 2), space_axes + chan_axes)
    tiles = P(space_axes, None, chan_axes, None)
    in_specs = (
        tiles,
        tiles,
        P(chan_axes),
        P(chan_axes),
        P(None, None, chan_axes, None),
        P(),
        P(),
        P(),
        P(),
    )
    out_specs = (tiles, P(None, None, chan_axes, None))
    inner = jax.shard_map(
        fine_local, mesh=fine, in_specs=in_specs, out_specs=out_specs, check_vma=False
    )
    out_shardings = (
        NamedSharding(mesh, P("space", None, "chan", None)),
        NamedSharding(mesh, P(None, None, "chan", None)),
    )

    def run(*args):
        outs = inner(*args)
        return tuple(lax.with_sharding_constraint(o, sh) for o, sh in zip(outs, out_shardings))

    return run


def fine_local(*args):
    return local(*args)
```

```python
import math

import jax
import jax.numpy as jnp
from jax import lax
from jax.sharding import Mesh, NamedSharding
from jax.sharding import PartitionSpec as P

GROUPS = 32


EPS = 1e-05
HIGH = lax.Precision.HIGHEST


def loss_weights(timesteps):
    phase = (timesteps.astype(jnp.float32) / 1000.0 + 0.008) / 1.008 * (math.pi / 2.0)
    alpha_bar = jnp.cos(phase) ** 2
    return jnp.minimum(1.0, 5.0 * (1.0 - alpha_bar) / alpha_bar)


def silu_slope(pre_act):
    sigma_val = jax.nn.sigmoid(pre_act)
    return sigma_val * (1.0 + pre_act * (1.0 - sigma_val))


def group_sums(values, groups):
    grouped = values.reshape(
        values.shape[:-2] + (groups, values.shape[-2] // groups, values.shape[-1])
    )
    return jnp.sum(grouped, axis=(-2, -1))


def norm_stats(sum_first, sum_second, counts):
    mean_img = sum_first / counts[:, None]
    var_img = sum_second / counts[:, None] - mean_img * mean_img
    return (mean_img, lax.rsqrt(var_img + EPS))


def shifted_views(source_field, up_ok, down_ok):
    zero_rows = jnp.zeros_like(source_field[:1])
    up_mask = up_ok.astype(source_field.dtype)[:, None, None]
    down_mask = down_ok.astype(source_field.dtype)[:, None, None]
    rows_above = jnp.concatenate([zero_rows, source_field[:-1]], axis=0) * up_mask
    rows_below = jnp.concatenate([source_field[1:], zero_rows], axis=0) * down_mask
    return [rows_above, source_field, rows_below]


def conv_views(row_views, weight):
    running = None
    for row_tap in range(3):
        source = row_views[row_tap]
        col_count = source.shape[-1]
        padded = jnp.pad(source, ((0, 0), (0, 0), (1, 1)))
        for col_tap in range(3):
            window = padded[:, :, col_tap : col_tap + col_count]
            tap_term = jnp.einsum(
                "rcw,oc->row",
                window,
                weight[row_tap, col_tap],
                preferred_element_type=jnp.float32,
            )
            running = tap_term if running is None else running + tap_term
    return running


def weight_terms(row_views, grad_field):
    col_count = grad_field.shape[-1]
    padded = jnp.pad(grad_field, ((0, 0), (0, 0), (1, 1)))
    shifted = jnp.stack(
        [padded[:, :, 2 - col_tap : 2 - col_tap + col_count] for col_tap in range(3)]
    )
    tap_rows = [
        jnp.einsum("drow,rcw->doc", shifted, source, preferred_element_type=jnp.float32)
        for source in row_views
    ]
    return jnp.stack(tap_rows)


def grad_conv(row_views, matrix):
    col_count = row_views[0].shape[-1]
    cols = []
    for source in row_views:
        padded = jnp.pad(source, ((0, 0), (0, 0), (1, 1)))
        for col_tap in range(3):
            cols.append(padded[:, :, col_tap : col_tap + col_count])
    stacked = jnp.concatenate(cols, axis=1)
    return jnp.einsum("rkw,pck->prcw", stacked, matrix, preferred_element_type=jnp.float32)


def tap_matrix(weight, parts):
    c_total, o_total = weight.shape[2], weight.shape[3]
    return jnp.transpose(weight, (2, 0, 1, 3)).reshape(parts, c_total // parts, 9 * o_total)


def local(
    latents,
    targets,
    norm_gain,
    norm_bias,
    conv_weight,
    tile_image,
    tile_owner,
    tile_slot,
    timesteps,
):
    my_index = lax.axis_index(("xh", "z", "y"))
    devices = lax.axis_size(("xh", "z", "y"))
    slots_dev, tile_rows, local_ch, col_count = latents.shape
    channels = conv_weight.shape[3]
    group_size = channels // GROUPS
    groups_here = local_ch // group_size
    image_total = timesteps.shape[0]
    tiles_dev = slots_dev // 2
    row_total = slots_dev * tile_rows
    image_ids = jnp.arange(image_total, dtype=jnp.int32)
    counts = jnp.sum(
        (tile_image.reshape(-1)[None, :] == image_ids[:, None]).astype(jnp.float32), axis=1
    ) * float(tile_rows * col_count * group_size)
    weights_img = loss_weights(timesteps)
    flipped = jnp.transpose(conv_weight[::-1, ::-1], (0, 1, 3, 2))
    gain_col = norm_gain[:, None]
    bias_col = norm_bias[:, None]
    grad_scale = 1.0 / math.sqrt(devices * tiles_dev * tile_rows * col_count)

    my_image = lax.dynamic_index_in_dim(tile_image, my_index, 0, keepdims=False)
    my_owner = lax.dynamic_index_in_dim(tile_owner, my_index, 0, keepdims=False)
    row_image = jnp.repeat(my_image, tile_rows)
    row_valid = row_image >= 0
    prev_image = jnp.concatenate([jnp.full((1,), -2, jnp.int32), row_image[:-1]])
    next_image = jnp.concatenate([row_image[1:], jnp.full((1,), -2, jnp.int32)])
    up_ok = row_valid & (prev_image == row_image)
    down_ok = row_valid & (next_image == row_image)
    onehot = (row_image[:, None] == image_ids[None, :]).astype(jnp.float32)
    valid_rows = row_valid.astype(jnp.float32)[:, None, None]

    lat_float = latents.reshape(row_total, local_ch, col_count).astype(jnp.float32)
    part_first = jnp.dot(onehot.T, group_sums(lat_float, groups_here), precision=HIGH)
    part_second = jnp.dot(onehot.T, group_sums(lat_float * lat_float, groups_here), precision=HIGH)
    mean_img, rstd_img = norm_stats(part_first, part_second, counts)
    mean_rows = jnp.repeat(jnp.dot(onehot, mean_img, precision=HIGH), group_size, axis=1)[
        :, :, None
    ]
    rstd_rows = jnp.repeat(jnp.dot(onehot, rstd_img, precision=HIGH), group_size, axis=1)[
        :, :, None
    ]
    normed = (lat_float - mean_rows) * rstd_rows
    pre_act = normed * gain_col + bias_col
    act = (jax.nn.silu(pre_act) * valid_rows).astype(jnp.bfloat16)
    act_full = lax.all_gather(act, ("xl", "core"), axis=1, tiled=True)
    parts = lax.axis_size(("xl", "core"))
    act_full, matrix = lax.optimization_barrier((act_full, tap_matrix(flipped, parts)))
    act_views = shifted_views(act_full, up_ok, down_ok)
    prediction = conv_views(act_views, conv_weight)
    loss_rows = jnp.dot(onehot, weights_img, precision=HIGH)[:, None, None]
    target_float = targets.reshape(row_total, local_ch, col_count).astype(jnp.float32)
    out_grad = (loss_rows * (prediction - target_float) * valid_rows).astype(jnp.bfloat16)
    act_partial = grad_conv(shifted_views(out_grad, up_ok, down_ok), matrix)
    act_grad = sum_chan(act_partial.astype(jnp.bfloat16))
    norm_grad = act_grad * silu_slope(pre_act) * gain_col
    grad_first = jnp.dot(onehot.T, group_sums(norm_grad, groups_here), precision=HIGH)
    grad_second = jnp.dot(onehot.T, group_sums(norm_grad * normed, groups_here), precision=HIGH)
    mean_g = jnp.repeat(
        jnp.dot(onehot, grad_first / counts[:, None], precision=HIGH), group_size, axis=1
    )[:, :, None]
    mean_gn = jnp.repeat(
        jnp.dot(onehot, grad_second / counts[:, None], precision=HIGH), group_size, axis=1
    )[:, :, None]
    x_rows = (rstd_rows * (norm_grad - mean_g - normed * mean_gn) * valid_rows).astype(
        jnp.bfloat16
    )

    tile_len = tile_rows * local_ch
    x_tiles = x_rows.reshape(slots_dev, tile_len, col_count)
    x_tiles = jnp.concatenate([x_tiles, jnp.zeros_like(x_tiles[:1])], axis=0)
    dest_ids = jnp.arange(devices, dtype=jnp.int32)
    send_match = my_owner[None, :] == dest_ids[:, None]
    send_slot = jnp.where(
        jnp.any(send_match, axis=1), jnp.argmax(send_match, axis=1), slots_dev
    ).astype(jnp.int32)
    outgoing = jnp.take(x_tiles, send_slot, axis=0)
    weight_sum = weight_terms(act_views, out_grad)
    weight_part = (weight_sum * grad_scale).astype(jnp.bfloat16)
    weight_grad, outgoing = sum_space(weight_part, outgoing)
    weight_grad = weight_grad.astype(jnp.float32)
    incoming = lax.all_to_all(outgoing, ("xh", "z", "y"), split_axis=0, concat_axis=0, tiled=True)
    slot_ids = jnp.arange(tiles_dev, dtype=jnp.int32)
    hit_mask = (tile_owner[None] == my_index) & (tile_slot[None] == slot_ids[:, None, None])
    recv_src = jnp.argmax(jnp.any(hit_mask, axis=2), axis=1).astype(jnp.int32)
    x_grad = jnp.take(incoming, recv_src, axis=0)
    x_grad = x_grad.reshape(tiles_dev, tile_rows, local_ch, col_count)

    return (x_grad, weight_grad)


WEIGHT_PLAN = "joint"


def scatter_sum(flat, axes):
    parts = lax.axis_size(axes)
    split = flat.reshape((parts, flat.shape[0] // parts) + flat.shape[1:])
    gathered = lax.all_to_all(split, axes, split_axis=0, concat_axis=0, tiled=True)
    return jnp.sum(gathered.astype(jnp.float32), axis=0).astype(flat.dtype)


def add_partner(part, axis):
    swapped = lax.ppermute(part, axis, perm=[(0, 1), (1, 0)])
    return (part.astype(jnp.float32) + swapped.astype(jnp.float32)).astype(part.dtype)


def sum_chan(partial):
    summed = lax.psum_scatter(partial, ("xl", "core"), scatter_dimension=0, tiled=True)
    return summed[0].astype(jnp.float32)


def sum_space(partial, rider):
    shape = partial.shape
    flat = partial.reshape(-1, shape[-1])
    rows = flat.shape[0]
    padded_rows = -(-rows // 16) * 16
    flat = jnp.pad(flat, ((0, padded_rows - rows), (0, 0)))
    if WEIGHT_PLAN == "yz":
        part = lax.psum_scatter(flat, "y", scatter_dimension=0, tiled=True)
        part = lax.psum_scatter(part, "z", scatter_dimension=0, tiled=True)
        part = lax.psum(part, "xh")
        part = lax.all_gather(part, "z", axis=0, tiled=True)
        flat = lax.all_gather(part, "y", axis=0, tiled=True)
    else:
        axes = ("z", "y")
        parts = lax.axis_size(axes)
        split = flat.reshape((parts, flat.shape[0] // parts) + flat.shape[1:])
        gathered = lax.all_to_all(split, axes, split_axis=0, concat_axis=0, tiled=True)
        gathered, rider = lax.optimization_barrier((gathered, rider))
        part = jnp.sum(gathered.astype(jnp.float32), axis=0).astype(flat.dtype)
        swapped = lax.ppermute(part, "xh", perm=[(0, 1), (1, 0)])
        swapped, rider = lax.optimization_barrier((swapped, rider))
        part = (part.astype(jnp.float32) + swapped.astype(jnp.float32)).astype(part.dtype)
        flat = lax.all_gather(part, axes, axis=0, tiled=True)
    return flat[:rows].reshape(shape), rider


def solution(mesh):
    space_axes = ("xh", "z", "y")
    chan_axes = ("xl", "core")
    fine = Mesh(mesh.devices.reshape(2, 4, 4, 2, 2), space_axes + chan_axes)
    tiles = P(space_axes, None, chan_axes, None)
    in_specs = (
        tiles,
        tiles,
        P(chan_axes),
        P(chan_axes),
        P(None, None, chan_axes, None),
        P(),
        P(),
        P(),
        P(),
    )
    out_specs = (tiles, P(None, None, chan_axes, None))
    inner = jax.shard_map(
        fine_local, mesh=fine, in_specs=in_specs, out_specs=out_specs, check_vma=False
    )
    out_shardings = (
        NamedSharding(mesh, P("space", None, "chan", None)),
        NamedSharding(mesh, P(None, None, "chan", None)),
    )

    def run(*args):
        outs = inner(*args)
        return tuple(lax.with_sharding_constraint(o, sh) for o, sh in zip(outs, out_shardings))

    return run


def fine_local(*args):
    return local(*args)
```

```python
import math

import jax
import jax.numpy as jnp
from jax import lax
from jax.sharding import Mesh, NamedSharding
from jax.sharding import PartitionSpec as P

GROUPS = 32


EPS = 1e-05
HIGH = lax.Precision.HIGHEST


def loss_weights(timesteps):
    phase = (timesteps.astype(jnp.float32) / 1000.0 + 0.008) / 1.008 * (math.pi / 2.0)
    alpha_bar = jnp.cos(phase) ** 2
    return jnp.minimum(1.0, 5.0 * (1.0 - alpha_bar) / alpha_bar)


def silu_slope(pre_act):
    sigma_val = jax.nn.sigmoid(pre_act)
    return sigma_val * (1.0 + pre_act * (1.0 - sigma_val))


def group_sums(values, groups):
    grouped = values.reshape(
        values.shape[:-2] + (groups, values.shape[-2] // groups, values.shape[-1])
    )
    return jnp.sum(grouped, axis=(-2, -1))


def norm_stats(sum_first, sum_second, counts):
    mean_img = sum_first / counts[:, None]
    var_img = sum_second / counts[:, None] - mean_img * mean_img
    return (mean_img, lax.rsqrt(var_img + EPS))


def shifted_views(source_field, up_ok, down_ok):
    zero_rows = jnp.zeros_like(source_field[:1])
    up_mask = up_ok.astype(source_field.dtype)[:, None, None]
    down_mask = down_ok.astype(source_field.dtype)[:, None, None]
    rows_above = jnp.concatenate([zero_rows, source_field[:-1]], axis=0) * up_mask
    rows_below = jnp.concatenate([source_field[1:], zero_rows], axis=0) * down_mask
    return [rows_above, source_field, rows_below]


def conv_views(row_views, weight):
    running = None
    for row_tap in range(3):
        source = row_views[row_tap]
        col_count = source.shape[-1]
        padded = jnp.pad(source, ((0, 0), (0, 0), (1, 1)))
        for col_tap in range(3):
            window = padded[:, :, col_tap : col_tap + col_count]
            tap_term = jnp.einsum(
                "rcw,oc->row",
                window,
                weight[row_tap, col_tap],
                preferred_element_type=jnp.float32,
            )
            running = tap_term if running is None else running + tap_term
    return running


def weight_terms(row_views, grad_field):
    col_count = grad_field.shape[-1]
    padded = jnp.pad(grad_field, ((0, 0), (0, 0), (1, 1)))
    shifted = jnp.stack(
        [padded[:, :, 2 - col_tap : 2 - col_tap + col_count] for col_tap in range(3)]
    )
    tap_rows = [
        jnp.einsum("drow,rcw->doc", shifted, source, preferred_element_type=jnp.float32)
        for source in row_views
    ]
    return jnp.stack(tap_rows)


def grad_conv(row_views, matrix):
    col_count = row_views[0].shape[-1]
    cols = []
    for source in row_views:
        padded = jnp.pad(source, ((0, 0), (0, 0), (1, 1)))
        for col_tap in range(3):
            cols.append(padded[:, :, col_tap : col_tap + col_count])
    stacked = jnp.concatenate(cols, axis=1)
    return jnp.einsum("rkw,pck->prcw", stacked, matrix, preferred_element_type=jnp.float32)


def tap_matrix(weight, parts):
    c_total, o_total = weight.shape[2], weight.shape[3]
    return jnp.transpose(weight, (2, 0, 1, 3)).reshape(parts, c_total // parts, 9 * o_total)


def local(
    latents,
    targets,
    norm_gain,
    norm_bias,
    conv_weight,
    tile_image,
    tile_owner,
    tile_slot,
    timesteps,
):
    my_index = lax.axis_index(("xh", "z", "y"))
    devices = lax.axis_size(("xh", "z", "y"))
    slots_dev, tile_rows, local_ch, col_count = latents.shape
    channels = conv_weight.shape[3]
    group_size = channels // GROUPS
    groups_here = local_ch // group_size
    image_total = timesteps.shape[0]
    tiles_dev = slots_dev // 2
    row_total = slots_dev * tile_rows
    image_ids = jnp.arange(image_total, dtype=jnp.int32)
    counts = jnp.sum(
        (tile_image.reshape(-1)[None, :] == image_ids[:, None]).astype(jnp.float32), axis=1
    ) * float(tile_rows * col_count * group_size)
    weights_img = loss_weights(timesteps)
    flipped = jnp.transpose(conv_weight[::-1, ::-1], (0, 1, 3, 2))
    gain_col = norm_gain[:, None]
    bias_col = norm_bias[:, None]
    grad_scale = 1.0 / math.sqrt(devices * tiles_dev * tile_rows * col_count)

    my_image = lax.dynamic_index_in_dim(tile_image, my_index, 0, keepdims=False)
    my_owner = lax.dynamic_index_in_dim(tile_owner, my_index, 0, keepdims=False)
    row_image = jnp.repeat(my_image, tile_rows)
    row_valid = row_image >= 0
    prev_image = jnp.concatenate([jnp.full((1,), -2, jnp.int32), row_image[:-1]])
    next_image = jnp.concatenate([row_image[1:], jnp.full((1,), -2, jnp.int32)])
    up_ok = row_valid & (prev_image == row_image)
    down_ok = row_valid & (next_image == row_image)
    onehot = (row_image[:, None] == image_ids[None, :]).astype(jnp.float32)
    valid_rows = row_valid.astype(jnp.float32)[:, None, None]

    lat_float = latents.reshape(row_total, local_ch, col_count).astype(jnp.float32)
    part_first = jnp.dot(onehot.T, group_sums(lat_float, groups_here), precision=HIGH)
    part_second = jnp.dot(onehot.T, group_sums(lat_float * lat_float, groups_here), precision=HIGH)
    mean_img, rstd_img = norm_stats(part_first, part_second, counts)
    mean_rows = jnp.repeat(jnp.dot(onehot, mean_img, precision=HIGH), group_size, axis=1)[
        :, :, None
    ]
    rstd_rows = jnp.repeat(jnp.dot(onehot, rstd_img, precision=HIGH), group_size, axis=1)[
        :, :, None
    ]
    normed = (lat_float - mean_rows) * rstd_rows
    pre_act = normed * gain_col + bias_col
    act = (jax.nn.silu(pre_act) * valid_rows).astype(jnp.bfloat16)
    act_full = lax.all_gather(act, ("xl", "core"), axis=1, tiled=True)
    parts = lax.axis_size(("xl", "core"))
    act_full, matrix = lax.optimization_barrier((act_full, tap_matrix(flipped, parts)))
    act_views = shifted_views(act_full, up_ok, down_ok)
    prediction = conv_views(act_views, conv_weight)
    loss_rows = jnp.dot(onehot, weights_img, precision=HIGH)[:, None, None]
    target_float = targets.reshape(row_total, local_ch, col_count).astype(jnp.float32)
    out_grad = (loss_rows * (prediction - target_float) * valid_rows).astype(jnp.bfloat16)
    act_partial = grad_conv(shifted_views(out_grad, up_ok, down_ok), matrix)
    act_grad = sum_chan(act_partial.astype(jnp.bfloat16))
    norm_grad = act_grad * silu_slope(pre_act) * gain_col
    grad_first = jnp.dot(onehot.T, group_sums(norm_grad, groups_here), precision=HIGH)
    grad_second = jnp.dot(onehot.T, group_sums(norm_grad * normed, groups_here), precision=HIGH)
    mean_g = jnp.repeat(
        jnp.dot(onehot, grad_first / counts[:, None], precision=HIGH), group_size, axis=1
    )[:, :, None]
    mean_gn = jnp.repeat(
        jnp.dot(onehot, grad_second / counts[:, None], precision=HIGH), group_size, axis=1
    )[:, :, None]
    x_rows = (rstd_rows * (norm_grad - mean_g - normed * mean_gn) * valid_rows).astype(
        jnp.bfloat16
    )

    tile_len = tile_rows * local_ch
    x_tiles = x_rows.reshape(slots_dev, tile_len, col_count)
    x_tiles = jnp.concatenate([x_tiles, jnp.zeros_like(x_tiles[:1])], axis=0)
    dest_ids = jnp.arange(devices, dtype=jnp.int32)
    send_match = my_owner[None, :] == dest_ids[:, None]
    send_slot = jnp.where(
        jnp.any(send_match, axis=1), jnp.argmax(send_match, axis=1), slots_dev
    ).astype(jnp.int32)
    outgoing = jnp.take(x_tiles, send_slot, axis=0)
    weight_sum = weight_terms(act_views, out_grad)
    weight_part = (weight_sum * grad_scale).astype(jnp.bfloat16)
    weight_grad, outgoing = sum_space(weight_part, outgoing)
    weight_grad = weight_grad.astype(jnp.float32)
    incoming = lax.all_to_all(outgoing, ("xh", "z", "y"), split_axis=0, concat_axis=0, tiled=True)
    slot_ids = jnp.arange(tiles_dev, dtype=jnp.int32)
    hit_mask = (tile_owner[None] == my_index) & (tile_slot[None] == slot_ids[:, None, None])
    recv_src = jnp.argmax(jnp.any(hit_mask, axis=2), axis=1).astype(jnp.int32)
    x_grad = jnp.take(incoming, recv_src, axis=0)
    x_grad = x_grad.reshape(tiles_dev, tile_rows, local_ch, col_count)

    return (x_grad, weight_grad)


WEIGHT_PLAN = "joint"


def scatter_sum(flat, axes):
    parts = lax.axis_size(axes)
    split = flat.reshape((parts, flat.shape[0] // parts) + flat.shape[1:])
    gathered = lax.all_to_all(split, axes, split_axis=0, concat_axis=0, tiled=True)
    return jnp.sum(gathered.astype(jnp.float32), axis=0).astype(flat.dtype)


def add_partner(part, axis):
    swapped = lax.ppermute(part, axis, perm=[(0, 1), (1, 0)])
    return (part.astype(jnp.float32) + swapped.astype(jnp.float32)).astype(part.dtype)


def sum_chan(partial):
    summed = lax.psum_scatter(partial, ("xl", "core"), scatter_dimension=0, tiled=True)
    return summed[0].astype(jnp.float32)


def sum_space(partial, rider):
    shape = partial.shape
    flat = partial.reshape(-1, shape[-1])
    rows = flat.shape[0]
    padded_rows = -(-rows // 16) * 16
    flat = jnp.pad(flat, ((0, padded_rows - rows), (0, 0)))
    if WEIGHT_PLAN == "yz":
        part = lax.psum_scatter(flat, "y", scatter_dimension=0, tiled=True)
        part = lax.psum_scatter(part, "z", scatter_dimension=0, tiled=True)
        part = lax.psum(part, "xh")
        part = lax.all_gather(part, "z", axis=0, tiled=True)
        flat = lax.all_gather(part, "y", axis=0, tiled=True)
    else:
        axes = ("z", "y")
        parts = lax.axis_size(axes)
        split = flat.reshape((parts, flat.shape[0] // parts) + flat.shape[1:])
        gathered = lax.all_to_all(split, axes, split_axis=0, concat_axis=0, tiled=True)
        gathered, rider = lax.optimization_barrier((gathered, rider))
        part = jnp.sum(gathered.astype(jnp.float32), axis=0).astype(flat.dtype)
        swapped = lax.ppermute(part, "xh", perm=[(0, 1), (1, 0)])
        swapped, rider = lax.optimization_barrier((swapped, rider))
        part = (part.astype(jnp.float32) + swapped.astype(jnp.float32)).astype(part.dtype)
        keep = (part.shape[0] * 2 // 3) // 8 * 8
        offload = lax.all_gather(part[:keep], axes, axis=0, tiled=False)
        rest = part[keep:]
        copies = jnp.broadcast_to(rest[None], (parts,) + rest.shape)
        local_copy = lax.all_to_all(copies, axes, split_axis=0, concat_axis=0, tiled=True)
        flat = jnp.concatenate([offload, local_copy], axis=1).reshape(flat.shape)
    return flat[:rows].reshape(shape), rider


def solution(mesh):
    space_axes = ("xh", "z", "y")
    chan_axes = ("xl", "core")
    fine = Mesh(mesh.devices.reshape(2, 4, 4, 2, 2), space_axes + chan_axes)
    tiles = P(space_axes, None, chan_axes, None)
    in_specs = (
        tiles,
        tiles,
        P(chan_axes),
        P(chan_axes),
        P(None, None, chan_axes, None),
        P(),
        P(),
        P(),
        P(),
    )
    out_specs = (tiles, P(None, None, chan_axes, None))
    inner = jax.shard_map(
        fine_local, mesh=fine, in_specs=in_specs, out_specs=out_specs, check_vma=False
    )
    out_shardings = (
        NamedSharding(mesh, P("space", None, "chan", None)),
        NamedSharding(mesh, P(None, None, "chan", None)),
    )

    def run(*args):
        outs = inner(*args)
        return tuple(lax.with_sharding_constraint(o, sh) for o, sh in zip(outs, out_shardings))

    return run


def fine_local(*args):
    return local(*args)
```

```python
import math

import jax
import jax.numpy as jnp
from jax import lax
from jax.sharding import Mesh, NamedSharding
from jax.sharding import PartitionSpec as P

GROUPS = 32


EPS = 1e-05
HIGH = lax.Precision.HIGHEST


def loss_weights(timesteps):
    phase = (timesteps.astype(jnp.float32) / 1000.0 + 0.008) / 1.008 * (math.pi / 2.0)
    alpha_bar = jnp.cos(phase) ** 2
    return jnp.minimum(1.0, 5.0 * (1.0 - alpha_bar) / alpha_bar)


def silu_slope(pre_act):
    sigma_val = jax.nn.sigmoid(pre_act)
    return sigma_val * (1.0 + pre_act * (1.0 - sigma_val))


def group_sums(values, groups):
    grouped = values.reshape(
        values.shape[:-2] + (groups, values.shape[-2] // groups, values.shape[-1])
    )
    return jnp.sum(grouped, axis=(-2, -1))


def norm_stats(sum_first, sum_second, counts):
    mean_img = sum_first / counts[:, None]
    var_img = sum_second / counts[:, None] - mean_img * mean_img
    return (mean_img, lax.rsqrt(var_img + EPS))


def shifted_views(source_field, up_ok, down_ok):
    zero_rows = jnp.zeros_like(source_field[:1])
    up_mask = up_ok.astype(source_field.dtype)[:, None, None]
    down_mask = down_ok.astype(source_field.dtype)[:, None, None]
    rows_above = jnp.concatenate([zero_rows, source_field[:-1]], axis=0) * up_mask
    rows_below = jnp.concatenate([source_field[1:], zero_rows], axis=0) * down_mask
    return [rows_above, source_field, rows_below]


def conv_views(row_views, weight):
    running = None
    for row_tap in range(3):
        source = row_views[row_tap]
        col_count = source.shape[-1]
        padded = jnp.pad(source, ((0, 0), (0, 0), (1, 1)))
        for col_tap in range(3):
            window = padded[:, :, col_tap : col_tap + col_count]
            tap_term = jnp.einsum(
                "rcw,oc->row",
                window,
                weight[row_tap, col_tap],
                preferred_element_type=jnp.float32,
            )
            running = tap_term if running is None else running + tap_term
    return running


def weight_terms(source, grad_views):
    col_count = source.shape[-1]
    tap_rows = []
    for grad_field in grad_views:
        padded = jnp.pad(grad_field, ((0, 0), (0, 0), (1, 1)))
        shifted = jnp.stack(
            [padded[:, :, 2 - col_tap : 2 - col_tap + col_count] for col_tap in range(3)]
        )
        tap_rows.append(
            jnp.einsum("drow,rcw->doc", shifted, source, preferred_element_type=jnp.float32)
        )
    return jnp.stack(tap_rows)


def conv_rows(source, up_ok, down_ok, weight):
    col_count = source.shape[-1]
    padded = jnp.pad(source, ((0, 0), (0, 0), (1, 1)))
    outs = []
    for row_tap in range(3):
        running = None
        for col_tap in range(3):
            tap_term = jnp.einsum(
                "rcw,oc->row",
                padded[:, :, col_tap : col_tap + col_count],
                weight[row_tap, col_tap],
                preferred_element_type=jnp.float32,
            )
            running = tap_term if running is None else running + tap_term
        outs.append(running)
    above, _, below = shifted_views(outs[0], up_ok, down_ok)
    _, _, below = shifted_views(outs[2], up_ok, down_ok)
    return above + outs[1] + below


def grad_conv(row_views, matrix):
    col_count = row_views[0].shape[-1]
    cols = []
    for source in row_views:
        padded = jnp.pad(source, ((0, 0), (0, 0), (1, 1)))
        for col_tap in range(3):
            cols.append(padded[:, :, col_tap : col_tap + col_count])
    stacked = jnp.concatenate(cols, axis=1)
    return jnp.einsum("rkw,pck->prcw", stacked, matrix, preferred_element_type=jnp.float32)


def tap_matrix(weight, parts):
    c_total, o_total = weight.shape[2], weight.shape[3]
    return jnp.transpose(weight, (2, 0, 1, 3)).reshape(parts, c_total // parts, 9 * o_total)


def local(
    latents,
    targets,
    norm_gain,
    norm_bias,
    conv_weight,
    tile_image,
    tile_owner,
    tile_slot,
    timesteps,
):
    my_index = lax.axis_index(("xh", "z", "y"))
    devices = lax.axis_size(("xh", "z", "y"))
    slots_dev, tile_rows, local_ch, col_count = latents.shape
    channels = conv_weight.shape[3]
    group_size = channels // GROUPS
    groups_here = local_ch // group_size
    image_total = timesteps.shape[0]
    tiles_dev = slots_dev // 2
    row_total = slots_dev * tile_rows
    image_ids = jnp.arange(image_total, dtype=jnp.int32)
    counts = jnp.sum(
        (tile_image.reshape(-1)[None, :] == image_ids[:, None]).astype(jnp.float32), axis=1
    ) * float(tile_rows * col_count * group_size)
    weights_img = loss_weights(timesteps)
    flipped = jnp.transpose(conv_weight[::-1, ::-1], (0, 1, 3, 2))
    gain_col = norm_gain[:, None]
    bias_col = norm_bias[:, None]
    grad_scale = 1.0 / math.sqrt(devices * tiles_dev * tile_rows * col_count)

    my_image = lax.dynamic_index_in_dim(tile_image, my_index, 0, keepdims=False)
    my_owner = lax.dynamic_index_in_dim(tile_owner, my_index, 0, keepdims=False)
    row_image = jnp.repeat(my_image, tile_rows)
    row_valid = row_image >= 0
    prev_image = jnp.concatenate([jnp.full((1,), -2, jnp.int32), row_image[:-1]])
    next_image = jnp.concatenate([row_image[1:], jnp.full((1,), -2, jnp.int32)])
    up_ok = row_valid & (prev_image == row_image)
    down_ok = row_valid & (next_image == row_image)
    onehot = (row_image[:, None] == image_ids[None, :]).astype(jnp.float32)
    valid_rows = row_valid.astype(jnp.float32)[:, None, None]

    lat_float = latents.reshape(row_total, local_ch, col_count).astype(jnp.float32)
    part_first = jnp.dot(onehot.T, group_sums(lat_float, groups_here), precision=HIGH)
    part_second = jnp.dot(onehot.T, group_sums(lat_float * lat_float, groups_here), precision=HIGH)
    mean_img, rstd_img = norm_stats(part_first, part_second, counts)
    mean_rows = jnp.repeat(jnp.dot(onehot, mean_img, precision=HIGH), group_size, axis=1)[
        :, :, None
    ]
    rstd_rows = jnp.repeat(jnp.dot(onehot, rstd_img, precision=HIGH), group_size, axis=1)[
        :, :, None
    ]
    normed = (lat_float - mean_rows) * rstd_rows
    pre_act = normed * gain_col + bias_col
    act = (jax.nn.silu(pre_act) * valid_rows).astype(jnp.bfloat16)
    act_full = lax.all_gather(act, ("xl", "core"), axis=1, tiled=True)
    parts = lax.axis_size(("xl", "core"))
    act_full, matrix = lax.optimization_barrier((act_full, tap_matrix(flipped, parts)))
    prediction = conv_rows(act_full, up_ok, down_ok, conv_weight)
    loss_rows = jnp.dot(onehot, weights_img, precision=HIGH)[:, None, None]
    target_float = targets.reshape(row_total, local_ch, col_count).astype(jnp.float32)
    out_grad = (loss_rows * (prediction - target_float) * valid_rows).astype(jnp.bfloat16)
    grad_views = shifted_views(out_grad, up_ok, down_ok)
    act_partial = grad_conv(grad_views, matrix)
    act_grad = sum_chan(act_partial.astype(jnp.bfloat16))
    norm_grad = act_grad * silu_slope(pre_act) * gain_col
    grad_first = jnp.dot(onehot.T, group_sums(norm_grad, groups_here), precision=HIGH)
    grad_second = jnp.dot(onehot.T, group_sums(norm_grad * normed, groups_here), precision=HIGH)
    mean_g = jnp.repeat(
        jnp.dot(onehot, grad_first / counts[:, None], precision=HIGH), group_size, axis=1
    )[:, :, None]
    mean_gn = jnp.repeat(
        jnp.dot(onehot, grad_second / counts[:, None], precision=HIGH), group_size, axis=1
    )[:, :, None]
    x_rows = (rstd_rows * (norm_grad - mean_g - normed * mean_gn) * valid_rows).astype(
        jnp.bfloat16
    )

    tile_len = tile_rows * local_ch
    x_tiles = x_rows.reshape(slots_dev, tile_len, col_count)
    x_tiles = jnp.concatenate([x_tiles, jnp.zeros_like(x_tiles[:1])], axis=0)
    dest_ids = jnp.arange(devices, dtype=jnp.int32)
    send_match = my_owner[None, :] == dest_ids[:, None]
    send_slot = jnp.where(
        jnp.any(send_match, axis=1), jnp.argmax(send_match, axis=1), slots_dev
    ).astype(jnp.int32)
    outgoing = jnp.take(x_tiles, send_slot, axis=0)
    incoming = lax.all_to_all(outgoing, ("xh", "z", "y"), split_axis=0, concat_axis=0, tiled=True)
    slot_ids = jnp.arange(tiles_dev, dtype=jnp.int32)
    hit_mask = (tile_owner[None] == my_index) & (tile_slot[None] == slot_ids[:, None, None])
    recv_src = jnp.argmax(jnp.any(hit_mask, axis=2), axis=1).astype(jnp.int32)
    x_grad = jnp.take(incoming, recv_src, axis=0)
    x_grad = x_grad.reshape(tiles_dev, tile_rows, local_ch, col_count)

    weight_sum = weight_terms(act_full, [grad_views[2], out_grad, grad_views[0]])
    weight_grad = sum_space((weight_sum * grad_scale).astype(jnp.bfloat16)).astype(jnp.float32)
    return (x_grad, weight_grad)


WEIGHT_PLAN = "joint"


def scatter_sum(flat, axes):
    parts = lax.axis_size(axes)
    split = flat.reshape((parts, flat.shape[0] // parts) + flat.shape[1:])
    gathered = lax.all_to_all(split, axes, split_axis=0, concat_axis=0, tiled=True)
    return jnp.sum(gathered.astype(jnp.float32), axis=0).astype(flat.dtype)


def add_partner(part, axis):
    swapped = lax.ppermute(part, axis, perm=[(0, 1), (1, 0)])
    return (part.astype(jnp.float32) + swapped.astype(jnp.float32)).astype(part.dtype)


def sum_chan(partial):
    summed = lax.psum_scatter(partial, ("xl", "core"), scatter_dimension=0, tiled=True)
    return summed[0].astype(jnp.float32)


def sum_space(partial):
    shape = partial.shape
    flat = partial.reshape(-1, shape[-1])
    rows = flat.shape[0]
    padded_rows = -(-rows // 16) * 16
    flat = jnp.pad(flat, ((0, padded_rows - rows), (0, 0)))
    if WEIGHT_PLAN == "yz":
        part = lax.psum_scatter(flat, "y", scatter_dimension=0, tiled=True)
        part = lax.psum_scatter(part, "z", scatter_dimension=0, tiled=True)
        part = lax.psum(part, "xh")
        part = lax.all_gather(part, "z", axis=0, tiled=True)
        flat = lax.all_gather(part, "y", axis=0, tiled=True)
    else:
        part = scatter_sum(flat, ("z", "y"))
        part = add_partner(part, "xh")
        flat = lax.all_gather(part, ("z", "y"), axis=0, tiled=True)
    return flat[:rows].reshape(shape)


def solution(mesh):
    space_axes = ("xh", "z", "y")
    chan_axes = ("xl", "core")
    fine = Mesh(mesh.devices.reshape(2, 4, 4, 2, 2), space_axes + chan_axes)
    tiles = P(space_axes, None, chan_axes, None)
    in_specs = (
        tiles,
        tiles,
        P(chan_axes),
        P(chan_axes),
        P(None, None, chan_axes, None),
        P(),
        P(),
        P(),
        P(),
    )
    out_specs = (tiles, P(None, None, chan_axes, None))
    inner = jax.shard_map(
        fine_local, mesh=fine, in_specs=in_specs, out_specs=out_specs, check_vma=False
    )
    out_shardings = (
        NamedSharding(mesh, P("space", None, "chan", None)),
        NamedSharding(mesh, P(None, None, "chan", None)),
    )

    def run(*args):
        outs = inner(*args)
        return tuple(lax.with_sharding_constraint(o, sh) for o, sh in zip(outs, out_shardings))

    return run


def fine_local(*args):
    return local(*args)
```

```python
import math

import jax
import jax.numpy as jnp
from jax import lax
from jax.sharding import Mesh, NamedSharding
from jax.sharding import PartitionSpec as P

GROUPS = 32


EPS = 1e-05
HIGH = lax.Precision.HIGHEST


def loss_weights(timesteps):
    phase = (timesteps.astype(jnp.float32) / 1000.0 + 0.008) / 1.008 * (math.pi / 2.0)
    alpha_bar = jnp.cos(phase) ** 2
    return jnp.minimum(1.0, 5.0 * (1.0 - alpha_bar) / alpha_bar)


def silu_slope(pre_act):
    sigma_val = jax.nn.sigmoid(pre_act)
    return sigma_val * (1.0 + pre_act * (1.0 - sigma_val))


def group_sums(values, groups):
    grouped = values.reshape(
        values.shape[:-2] + (groups, values.shape[-2] // groups, values.shape[-1])
    )
    return jnp.sum(grouped, axis=(-2, -1))


def norm_stats(sum_first, sum_second, counts):
    mean_img = sum_first / counts[:, None]
    var_img = sum_second / counts[:, None] - mean_img * mean_img
    return (mean_img, lax.rsqrt(var_img + EPS))


def shifted_views(source_field, up_ok, down_ok):
    zero_rows = jnp.zeros_like(source_field[:1])
    up_mask = up_ok.astype(source_field.dtype)[:, None, None]
    down_mask = down_ok.astype(source_field.dtype)[:, None, None]
    rows_above = jnp.concatenate([zero_rows, source_field[:-1]], axis=0) * up_mask
    rows_below = jnp.concatenate([source_field[1:], zero_rows], axis=0) * down_mask
    return [rows_above, source_field, rows_below]


def conv_views(row_views, weight):
    running = None
    for row_tap in range(3):
        source = row_views[row_tap]
        col_count = source.shape[-1]
        padded = jnp.pad(source, ((0, 0), (0, 0), (1, 1)))
        for col_tap in range(3):
            window = padded[:, :, col_tap : col_tap + col_count]
            tap_term = jnp.einsum(
                "rcw,oc->row",
                window,
                weight[row_tap, col_tap],
                preferred_element_type=jnp.float32,
            )
            running = tap_term if running is None else running + tap_term
    return running


def weight_terms(row_views, grad_field):
    col_count = grad_field.shape[-1]
    padded = jnp.pad(grad_field, ((0, 0), (0, 0), (1, 1)))
    shifted = jnp.stack(
        [padded[:, :, 2 - col_tap : 2 - col_tap + col_count] for col_tap in range(3)]
    )
    tap_rows = [
        jnp.einsum("drow,rcw->doc", shifted, source, preferred_element_type=jnp.float32)
        for source in row_views
    ]
    return jnp.stack(tap_rows)


def grad_conv(row_views, matrix):
    col_count = row_views[0].shape[-1]
    cols = []
    for source in row_views:
        padded = jnp.pad(source, ((0, 0), (0, 0), (1, 1)))
        for col_tap in range(3):
            cols.append(padded[:, :, col_tap : col_tap + col_count])
    stacked = jnp.concatenate(cols, axis=1)
    return jnp.einsum("rkw,pck->prcw", stacked, matrix, preferred_element_type=jnp.float32)


def tap_matrix(weight, parts):
    c_total, o_total = weight.shape[2], weight.shape[3]
    return jnp.transpose(weight, (2, 0, 1, 3)).reshape(parts, c_total // parts, 9 * o_total)


def local(
    latents,
    targets,
    norm_gain,
    norm_bias,
    conv_weight,
    tile_image,
    tile_owner,
    tile_slot,
    timesteps,
):
    my_index = lax.axis_index(("xh", "z", "y"))
    devices = lax.axis_size(("xh", "z", "y"))
    slots_dev, tile_rows, local_ch, col_count = latents.shape
    channels = conv_weight.shape[3]
    group_size = channels // GROUPS
    groups_here = local_ch // group_size
    image_total = timesteps.shape[0]
    tiles_dev = slots_dev // 2
    row_total = slots_dev * tile_rows
    image_ids = jnp.arange(image_total, dtype=jnp.int32)
    counts = jnp.sum(
        (tile_image.reshape(-1)[None, :] == image_ids[:, None]).astype(jnp.float32), axis=1
    ) * float(tile_rows * col_count * group_size)
    weights_img = loss_weights(timesteps)
    flipped = jnp.transpose(conv_weight[::-1, ::-1], (0, 1, 3, 2))
    gain_col = norm_gain[:, None]
    bias_col = norm_bias[:, None]
    grad_scale = 1.0 / math.sqrt(devices * tiles_dev * tile_rows * col_count)

    my_image = lax.dynamic_index_in_dim(tile_image, my_index, 0, keepdims=False)
    my_owner = lax.dynamic_index_in_dim(tile_owner, my_index, 0, keepdims=False)
    row_image = jnp.repeat(my_image, tile_rows)
    row_valid = row_image >= 0
    prev_image = jnp.concatenate([jnp.full((1,), -2, jnp.int32), row_image[:-1]])
    next_image = jnp.concatenate([row_image[1:], jnp.full((1,), -2, jnp.int32)])
    up_ok = row_valid & (prev_image == row_image)
    down_ok = row_valid & (next_image == row_image)
    onehot = (row_image[:, None] == image_ids[None, :]).astype(jnp.float32)
    valid_rows = row_valid.astype(jnp.float32)[:, None, None]

    lat_float = latents.reshape(row_total, local_ch, col_count).astype(jnp.float32)
    part_first = jnp.dot(onehot.T, group_sums(lat_float, groups_here), precision=HIGH)
    part_second = jnp.dot(onehot.T, group_sums(lat_float * lat_float, groups_here), precision=HIGH)
    mean_img, rstd_img = norm_stats(part_first, part_second, counts)
    mean_rows = jnp.repeat(jnp.dot(onehot, mean_img, precision=HIGH), group_size, axis=1)[
        :, :, None
    ]
    rstd_rows = jnp.repeat(jnp.dot(onehot, rstd_img, precision=HIGH), group_size, axis=1)[
        :, :, None
    ]
    normed = (lat_float - mean_rows) * rstd_rows
    pre_act = normed * gain_col + bias_col
    act = (jax.nn.silu(pre_act) * valid_rows).astype(jnp.bfloat16)
    act_full = lax.all_gather(act, ("xl", "core"), axis=1, tiled=True)
    parts = lax.axis_size(("xl", "core"))
    act_full, matrix = lax.optimization_barrier((act_full, tap_matrix(flipped, parts)))
    act_views = shifted_views(act_full, up_ok, down_ok)
    prediction = conv_views(act_views, conv_weight)
    loss_rows = jnp.dot(onehot, weights_img, precision=HIGH)[:, None, None]
    target_float = targets.reshape(row_total, local_ch, col_count).astype(jnp.float32)
    out_grad = (loss_rows * (prediction - target_float) * valid_rows).astype(jnp.bfloat16)
    act_partial = grad_conv(shifted_views(out_grad, up_ok, down_ok), matrix)
    act_grad = sum_chan(act_partial.astype(jnp.bfloat16))
    norm_grad = act_grad * silu_slope(pre_act) * gain_col
    grad_first = jnp.dot(onehot.T, group_sums(norm_grad, groups_here), precision=HIGH)
    grad_second = jnp.dot(onehot.T, group_sums(norm_grad * normed, groups_here), precision=HIGH)
    mean_g = jnp.repeat(
        jnp.dot(onehot, grad_first / counts[:, None], precision=HIGH), group_size, axis=1
    )[:, :, None]
    mean_gn = jnp.repeat(
        jnp.dot(onehot, grad_second / counts[:, None], precision=HIGH), group_size, axis=1
    )[:, :, None]
    x_rows = (rstd_rows * (norm_grad - mean_g - normed * mean_gn) * valid_rows).astype(
        jnp.bfloat16
    )

    tile_len = tile_rows * local_ch
    x_tiles = x_rows.reshape(slots_dev, tile_len, col_count)
    x_tiles = jnp.concatenate([x_tiles, jnp.zeros_like(x_tiles[:1])], axis=0)
    dest_ids = jnp.arange(devices, dtype=jnp.int32)
    send_match = my_owner[None, :] == dest_ids[:, None]
    send_slot = jnp.where(
        jnp.any(send_match, axis=1), jnp.argmax(send_match, axis=1), slots_dev
    ).astype(jnp.int32)
    outgoing = jnp.take(x_tiles, send_slot, axis=0)
    incoming = lax.all_to_all(outgoing, ("xh", "z", "y"), split_axis=0, concat_axis=0, tiled=True)
    slot_ids = jnp.arange(tiles_dev, dtype=jnp.int32)
    hit_mask = (tile_owner[None] == my_index) & (tile_slot[None] == slot_ids[:, None, None])
    recv_src = jnp.argmax(jnp.any(hit_mask, axis=2), axis=1).astype(jnp.int32)
    x_grad = jnp.take(incoming, recv_src, axis=0)
    x_grad = x_grad.reshape(tiles_dev, tile_rows, local_ch, col_count)

    weight_sum = weight_terms(act_views, out_grad)
    weight_grad = sum_space((weight_sum * grad_scale).astype(jnp.bfloat16)).astype(jnp.float32)
    return (x_grad, weight_grad)


WEIGHT_PLAN = "joint"


def scatter_sum(flat, axes):
    parts = lax.axis_size(axes)
    split = flat.reshape((parts, flat.shape[0] // parts) + flat.shape[1:])
    gathered = lax.all_to_all(split, axes, split_axis=0, concat_axis=0, tiled=True)
    return jnp.sum(gathered.astype(jnp.float32), axis=0).astype(flat.dtype)


def add_partner(part, axis):
    swapped = lax.ppermute(part, axis, perm=[(0, 1), (1, 0)])
    return (part.astype(jnp.float32) + swapped.astype(jnp.float32)).astype(part.dtype)


def sum_chan(partial):
    summed = lax.psum_scatter(partial, ("xl", "core"), scatter_dimension=0, tiled=True)
    return summed[0].astype(jnp.float32)


def sum_space(partial):
    shape = partial.shape
    flat = partial.reshape(-1, shape[-1])
    rows = flat.shape[0]
    padded_rows = -(-rows // 32) * 32
    flat = jnp.pad(flat, ((0, padded_rows - rows), (0, 0)))
    if WEIGHT_PLAN == "yz":
        part = lax.psum_scatter(flat, "y", scatter_dimension=0, tiled=True)
        part = lax.psum_scatter(part, "z", scatter_dimension=0, tiled=True)
        part = lax.psum(part, "xh")
        part = lax.all_gather(part, "z", axis=0, tiled=True)
        flat = lax.all_gather(part, "y", axis=0, tiled=True)
    else:
        part = scatter_sum(flat, ("z", "y", "xh"))
        side = lax.axis_index("xh")
        other = lax.ppermute(part, "xh", perm=[(0, 1), (1, 0)])
        first = jnp.where(side == 0, part, other)
        second = jnp.where(side == 0, other, part)
        part = jnp.concatenate([first, second], axis=0)
        flat = lax.all_gather(part, ("z", "y"), axis=0, tiled=True)
    return flat[:rows].reshape(shape)


def solution(mesh):
    space_axes = ("xh", "z", "y")
    chan_axes = ("xl", "core")
    fine = Mesh(mesh.devices.reshape(2, 4, 4, 2, 2), space_axes + chan_axes)
    tiles = P(space_axes, None, chan_axes, None)
    in_specs = (
        tiles,
        tiles,
        P(chan_axes),
        P(chan_axes),
        P(None, None, chan_axes, None),
        P(),
        P(),
        P(),
        P(),
    )
    out_specs = (tiles, P(None, None, chan_axes, None))
    inner = jax.shard_map(
        fine_local, mesh=fine, in_specs=in_specs, out_specs=out_specs, check_vma=False
    )
    out_shardings = (
        NamedSharding(mesh, P("space", None, "chan", None)),
        NamedSharding(mesh, P(None, None, "chan", None)),
    )

    def run(*args):
        outs = inner(*args)
        return tuple(lax.with_sharding_constraint(o, sh) for o, sh in zip(outs, out_shardings))

    return run


def fine_local(*args):
    return local(*args)
```
